32 devices in a mesh: groups: 2 (over y), gx: 4 (over z), gy: 2 (over x), gz: 2 (over core).
Axes of the slice: x: 2, y: 2, z: 4, core: 2. Of those that a mesh axis runs over, the one named last changes fastest.
Arguments:
- parent: bfloat16 [160, 32, 1024], P('groups', 'gx', ('gy', 'gz')), parts along dimension 0, may hold values from -6 to 6
- nest: bfloat16 [160, 24, 1536], P('groups', 'gx', ('gy', 'gz')), parts along dimension 0, may hold values from -6 to 6
- nu_parent: float32 [80], replicated, may hold values from 0.03 to 0.24
- nu_nest: float32 [80], replicated, may hold values from 0.03 to 0.24
- relax: float32 [80], replicated, may hold values from 0.1 to 0.5
- feedback: float32 [80], replicated, may hold values from 0.3 to 1
- vert_mix: float32 [80, 80], replicated, may hold values from -1 to 1
- fp_owner: int32 [4, 4, 256, 1], P('gx', ('gy', 'gz')), may hold values from 0 to 3; in each aligned block of 256 rows (0 to 255, 256 to 511, ..., all dimensions but the last counted through in order) at most 256 rows name the same one
- fp_cell: int32 [4, 4, 256], P('gx', ('gy', 'gz')), may hold values from 0 to 2047
- nest_of: int32 [24], replicated, may hold values from 0 to 2, as said below
Outputs:
- parent_out: bfloat16 [160, 32, 1024], P('groups', 'gx', ('gy', 'gz')), parts along dimension 0
- nest_out: bfloat16 [160, 24, 1536], P('groups', 'gx', ('gy', 'gz')), parts along dimension 0
The draws below stay inside these ranges and needn't reach their ends.
There are 2 independent parts, one for each index of `groups`. The reference program is written for one: setup_inputs(seed, part) draws one part's arguments, and reference() takes and returns one part's arrays. A program takes and returns all parts, laid end to end along the dimension named above; an argument that names none is the same for every part. Nothing has to cross between parts.
Inputs may be any that keep to these rules, and one draw needn't show every extreme that they name: `fp_owner`: within the 256 blocks of one nest tile no parent tile is named more than 256 times; in some nest tiles one is named exactly 256 times. `nest_of`: never falls along the rows; every nest holds one or more rows; nest 1 holds rows 11 and 12.
All inputs are finite; a program needn't handle non-finite values.
Results may differ from the reference program's by a relative error of at most 0.0033.
Values may be sent and summed in bfloat16 or wider, within the bound.
No kernel may reach another device: no remote copies, remote signals or barrier semaphores. Data moves between devices by JAX's collectives and lax.ppermute only.
A program may use at most 64 MiB of HBM per device.

```python
import math
import jax
import jax.numpy as jnp
import numpy as np
from jax import lax

LEV = 80
PCX = 8
PCY = 256
BCX = 2
BCY = 128
NYT = 4
REQ = 256
CAP = 256
PX = 32
PY = 1024
NX = 24
NY = 1536
N_GX = 4
N_GY = 2
N_GZ = 2


def draw_vert_mix(key, part):
    first_key, second_key = jax.random.split(jax.random.fold_in(key, 7))
    spread = jax.random.normal(first_key, (LEV, LEV), jnp.float32) * (0.25 / LEV ** 0.5)
    spread = jnp.clip(spread, -0.2, 0.2)
    diagonal = jax.random.uniform(second_key, (LEV,), jnp.float32, 0.5, 0.7)
    identity = jnp.eye(LEV, dtype=jnp.float32)
    return (spread * (1.0 - identity) + identity * diagonal[:, None]).astype(jnp.float32)


def draw_nest_of(key, part):
    first_key, second_key = jax.random.split(jax.random.fold_in(key, 11))
    start_one = jax.random.randint(first_key, (), 1, NX // 2, jnp.int32)
    start_two = jax.random.randint(second_key, (), NX // 2 + 1, NX, jnp.int32)
    rows_all = jnp.arange(NX, dtype=jnp.int32)
    return ((rows_all >= start_one).astype(jnp.int32) + (rows_all >= start_two).astype(jnp.int32)).astype(jnp.int32)


def place_ends(result, own_key, least, largest):
    index_at = [jax.random.randint(jax.random.fold_in(own_key, axis), (), 0, length) for axis, length in enumerate(result.shape)]
    longest = result.shape.index(max(result.shape))
    beside = index_at[:longest] + [(index_at[longest] + 1) % result.shape[longest]] + index_at[longest + 1:]
    return result.at[tuple(index_at)].set(least).at[tuple(beside)].set(largest)


def shard_levels(rng, dims, shards, smallest, top_value):
    level, own = 1.0, jax.random.fold_in(rng, 6)
    for position, shards_of in shards:
        draws = jnp.exp(jax.random.uniform(jax.random.fold_in(own, position), (shards_of,), jnp.float32, smallest / len(shards), top_value / len(shards)))
        level = level * jnp.repeat(draws, dims[position] // shards_of).reshape([-1 if axis == position else 1 for axis in range(len(dims))])
    return level


def shared_out(own_key, own, number, rows, number_of, top, reach, slope):
    ranking = jax.random.permutation(own_key, number_of)
    heavy_load, common = shares(number_of, rows * top, reach, slope, True), shares(number_of, rows * top, reach, slope, False)
    places = jnp.arange(number_of)

    def named(lengths, offset_by):
        used = int((lengths > 0).sum())
        fixed = max(1, used // 4)
        shifted = fixed + (places - fixed + offset_by * (used - fixed)) % max(1, number_of - fixed)
        return jnp.zeros((number_of,), jnp.int32).at[ranking[jnp.where(places < fixed, places, shifted)]].set(jnp.asarray(lengths, jnp.int32))

    lengths = jnp.where(number % 4 == 0, named(heavy_load, number // 4), named(common, number - number // 4 - 1))
    mixed = jax.random.permutation(jax.random.fold_in(own, 3), number_of)
    donor, receiver = mixed[0:number_of // 2 * 2:2], mixed[1:number_of // 2 * 2:2]
    slack = jnp.minimum(lengths[donor] - 1, reach - lengths[receiver]) // 2
    slack = jnp.where((donor == ranking[0]) | (receiver == ranking[0]) | (lengths[receiver] == 0), 0, jnp.maximum(slack, 0))
    shifted = jax.random.randint(jax.random.fold_in(own, 4), (number_of // 2,), 0, 1 << 20) % (slack + 1)
    lengths = lengths.at[donor].add(-shifted).at[receiver].add(shifted)
    items = jnp.searchsorted(jnp.cumsum(lengths), jnp.arange(rows * top), side="right").astype(jnp.int32)
    table = items.reshape(top, rows).T
    table = table[jax.random.permutation(jax.random.fold_in(own, 1), rows)]
    offset_by = jax.random.randint(jax.random.fold_in(own, 2), (rows, 1), 0, top)
    return jnp.take_along_axis(table, (jnp.arange(top)[None, :] + offset_by) % top, axis=1)


def shares(number_of, total, bound, skew, full):
    weights = [(1 << 20) // math.isqrt(rank ** skew) + 1 for rank in range(1, number_of + 1)]
    largest = bound if full else min(bound, max(-(-total // number_of), total * weights[0] // sum(weights)))
    least = 1 if total - largest >= number_of - 1 else 0
    counts, surplus = [largest] + [least] * (number_of - 1), total - largest - least * (number_of - 1)
    while surplus > 0:
        free = [i for i in range(1, number_of) if counts[i] < largest] or [i for i in range(1, number_of) if counts[i] < bound]
        mass, budget = sum([weights[i] for i in free]), surplus
        for i in free:
            extra = min(bound - counts[i], max(1, budget * weights[i] // mass), surplus)
            counts[i] = counts[i] + extra
            surplus = surplus - extra
    return np.array(counts)


def noise(key, dims, scale, reach, pieces=(), kind=jnp.bfloat16):
    drawn = jax.random.normal(key, dims, jnp.float32) * scale
    if len(pieces) > 0:
        drawn = shard_levels(key, dims, pieces, -0.22, 0.18) * drawn
    return jnp.clip(drawn, min=-reach, max=reach).astype(kind)


def setup_inputs(seed: int = 0, part: int = 0) -> dict:
    arg_keys = jax.random.split(jax.random.key(seed), 11)
    part_splits = jax.random.split(jax.random.fold_in(arg_keys[10], part), 11)
    parent = noise(part_splits[0], (LEV, PX, PY), 1.0, 6.0, ((1, 4), (2, 4)))
    nest = noise(part_splits[1], (LEV, NX, NY), 1.0, 6.0, ((1, 4), (2, 4)))
    nu_parent = jnp.clip(jnp.exp(jax.random.uniform(arg_keys[2], (LEV,), jnp.float32, math.log(0.03), math.log(0.24))), 0.03, 0.24)
    nu_nest = jnp.clip(jnp.exp(jax.random.uniform(arg_keys[3], (LEV,), jnp.float32, math.log(0.03), math.log(0.24))), 0.03, 0.24)
    relax = jnp.clip(jnp.exp(jax.random.uniform(arg_keys[4], (LEV,), jnp.float32, math.log(0.1), math.log(0.5))), 0.1, 0.5)
    feedback = jnp.clip(jnp.exp(jax.random.uniform(arg_keys[5], (LEV,), jnp.float32, math.log(0.3), math.log(1.0))), 0.3, 1.0)
    vert_mix = draw_vert_mix(jax.random.fold_in(arg_keys[10], 71), part)
    fp_owner_keys = jax.random.split(jax.random.fold_in(arg_keys[7], 1), N_GX * NYT * REQ // REQ)
    fp_owner_turns = jax.random.permutation(jax.random.fold_in(arg_keys[7], 3), N_GX * NYT * REQ // REQ)
    fp_owner = jax.vmap(lambda own, number: shared_out(jax.random.fold_in(arg_keys[7], 2), own, number, REQ, N_GX, 1, CAP, 2))(fp_owner_keys, fp_owner_turns).reshape((N_GX, NYT, REQ, 1))
    fp_cell = place_ends(jax.random.randint(arg_keys[8], (N_GX, NYT, REQ), 0, PCX * PCY), jax.random.fold_in(arg_keys[8], 1), 0, (PCX * PCY) - 1).astype(jnp.int32)
    nest_of = draw_nest_of(jax.random.fold_in(arg_keys[10], 71), part)
    return dict(parent=parent, nest=nest, nu_parent=nu_parent, nu_nest=nu_nest, relax=relax, feedback=feedback, vert_mix=vert_mix, fp_owner=fp_owner, fp_cell=fp_cell, nest_of=nest_of)


def mix_levels(matrix, values):
    flat_values = values.reshape(values.shape[0], -1)
    mixed = jnp.dot(matrix, flat_values, precision=lax.Precision.HIGHEST, preferred_element_type=jnp.float32)
    return mixed.reshape(values.shape)


def laplace(padded, centre):
    return ((padded[:, 2:, 1:-1] + padded[:, :-2, 1:-1]) + padded[:, 1:-1, 2:]) + padded[:, 1:-1, :-2] - 4.0 * centre


def to_grid(values, tiles_y):
    shaped = values.reshape(N_GX, tiles_y, BCX, BCY).transpose(0, 2, 1, 3)
    return shaped.reshape(N_GX * BCX, tiles_y * BCY)


def reference(parent, nest, nu_parent, nu_nest, relax, feedback, vert_mix, fp_owner, fp_cell, nest_of):
    coarse = parent.astype(jnp.float32)
    padded = jnp.pad(coarse, ((0, 0), (1, 1), (1, 1)))
    stepped = mix_levels(vert_mix, coarse + nu_parent[:, None, None] * laplace(padded, coarse))
    tiles_y = N_GY * N_GZ
    owners = fp_owner[..., 0].astype(jnp.int32)
    tile_index = jnp.arange(tiles_y, dtype=jnp.int32)[None, :, None]
    source_rows = to_grid(owners * PCX + fp_cell // PCY, tiles_y)
    source_cols = to_grid(tile_index * PCY + fp_cell % PCY, tiles_y)
    forcing_block = stepped[:, source_rows, source_cols]
    forcing_full = jnp.repeat(jnp.repeat(forcing_block, 3, axis=1), 3, axis=2)
    segment = nest_of.astype(jnp.int32)
    same_nest = (segment[1:] == segment[:-1]).astype(jnp.float32)
    zero_edge = jnp.zeros((1,), jnp.float32)
    left_ok = jnp.concatenate([zero_edge, same_nest])
    right_ok = jnp.concatenate([same_nest, zero_edge])
    nest_state = nest.astype(jnp.float32)
    for turn_no in range(3):
        padded = jnp.pad(nest_state, ((0, 0), (1, 1), (1, 1)))
        stencil_sum = ((padded[:, 2:, 1:-1] * right_ok[None, :, None] + padded[:, :-2, 1:-1] * left_ok[None, :, None]) + padded[:, 1:-1, 2:]) + padded[:, 1:-1, :-2] - 4.0 * nest_state
        moved = nest_state + nu_nest[:, None, None] * stencil_sum
        moved = moved + relax[:, None, None] * (forcing_full - moved)
        nest_state = mix_levels(vert_mix, moved)
    blocks = nest_state.reshape(LEV, N_GX * BCX, 3, tiles_y * BCY, 3).mean(axis=(2, 4))
    nudge_gap = blocks - forcing_block
    returned = jnp.zeros_like(stepped).at[:, source_rows, source_cols].add(nudge_gap)
    parent_out = (stepped + feedback[:, None, None] * returned).astype(jnp.bfloat16)
    return parent_out, nest_state.astype(jnp.bfloat16)
```

```python
import jax
import jax.numpy as jnp
from jax import lax
from jax.sharding import PartitionSpec as P

Y_AXES = ("gy", "gz")


def shift_pairs(count):
    forward = [(i, i + 1) for i in range(count - 1)]
    backward = [(i + 1, i) for i in range(count - 1)]
    return forward, backward


def exchange(blocks):
    fwd_x, bwd_x = shift_pairs(lax.axis_size("gx"))
    fwd_y, bwd_y = shift_pairs(lax.axis_size(Y_AXES))
    widths = [b.shape[2] for b in blocks]
    heights = [b.shape[1] for b in blocks]
    last_rows = jnp.concatenate([b[:, -1, :] for b in blocks], axis=1)
    first_rows = jnp.concatenate([b[:, 0, :] for b in blocks], axis=1)
    last_cols = jnp.concatenate([b[:, :, -1] for b in blocks], axis=1)
    first_cols = jnp.concatenate([b[:, :, 0] for b in blocks], axis=1)
    above = lax.ppermute(last_rows, "gx", fwd_x)
    below = lax.ppermute(first_rows, "gx", bwd_x)
    left = lax.ppermute(last_cols, Y_AXES, fwd_y)
    right = lax.ppermute(first_cols, Y_AXES, bwd_y)
    out = []
    xo = 0
    yo = 0
    for w, h in zip(widths, heights):
        out.append(
            (
                above[:, xo : xo + w],
                below[:, xo : xo + w],
                left[:, yo : yo + h],
                right[:, yo : yo + h],
            )
        )
        xo += w
        yo += h
    return out


def neighbours(centre, halo):
    above, below, left, right = (h.astype(centre.dtype) for h in halo)
    up = jnp.concatenate([above[:, None, :], centre[:, :-1, :]], axis=1)
    down = jnp.concatenate([centre[:, 1:, :], below[:, None, :]], axis=1)
    west = jnp.concatenate([left[:, :, None], centre[:, :, :-1]], axis=2)
    east = jnp.concatenate([centre[:, :, 1:], right[:, :, None]], axis=2)
    return up, down, west, east


def mix_levels(matrix, values):
    return jnp.einsum(
        "kl,lrc->krc",
        matrix,
        values,
        precision=lax.Precision.HIGHEST,
        preferred_element_type=jnp.float32,
    )


def nest_segments(nest_of, first, count):
    index_rows = first + jnp.arange(count, dtype=jnp.int32)
    inside = (index_rows >= 0) & (index_rows < nest_of.shape[0])
    return jnp.where(inside, nest_of[jnp.clip(index_rows, 0, nest_of.shape[0] - 1)], -1)


def row_weights(segments):
    left_w = (segments[:-2] == segments[1:-1]).astype(jnp.float32)
    right_w = (segments[2:] == segments[1:-1]).astype(jnp.float32)
    return (left_w, right_w)


def nest_advance(state, halo, target, nu_nest, relax, vert_mix, left_w, right_w):
    up, down, west, east = neighbours(state, halo)
    stencil_sum = (
        down * right_w[None, :, None] + up * left_w[None, :, None] + east + west - 4.0 * state
    )
    moved = state + nu_nest[:, None, None] * stencil_sum
    moved = moved + relax[:, None, None] * (target - moved)
    return mix_levels(vert_mix, moved)


def body(parent, nest, nu_parent, nu_nest, relax, feedback, vert_mix, fp_owner, fp_cell, nest_of):
    levels = parent.shape[0]
    tiles_x = lax.axis_size("gx")
    here_x = lax.axis_index("gx")

    parent_halo, nest_halo = exchange([parent, nest])
    centre = parent.astype(jnp.float32)
    up, down, west, east = neighbours(centre, parent_halo)
    stencil = down + up + east + west - 4.0 * centre
    stepped = mix_levels(vert_mix, centre + nu_parent[:, None, None] * stencil)
    flat_parent = stepped.reshape(levels, -1)

    owners = fp_owner.reshape(-1)
    cells = fp_cell.reshape(-1)
    requests = owners.shape[0]
    slots = 4 * requests // tiles_x
    onehot = (owners[:, None] == jnp.arange(tiles_x, dtype=jnp.int32)[None, :]).astype(jnp.int32)
    before = jnp.cumsum(onehot, axis=0) - onehot
    order_in = jnp.sum(before * onehot, axis=1)
    places = owners * slots + order_in
    wanted = jnp.zeros((tiles_x * slots,), jnp.int32).at[places].set(cells)
    served_ids = lax.all_to_all(wanted, "gx", split_axis=0, concat_axis=0, tiled=True)
    answers = lax.all_to_all(
        jnp.take(flat_parent, served_ids, axis=1), "gx", split_axis=1, concat_axis=1, tiled=True
    )
    forcing_flat = jnp.take(answers, places, axis=1)

    nest_rows = nest.shape[1]
    nest_cols = nest.shape[2]
    block_rows = nest_rows // 3
    block_cols = nest_cols // 3
    forcing_block = forcing_flat.reshape(levels, block_rows, block_cols)
    row_start = here_x * nest_rows
    forcing_full = jnp.repeat(jnp.repeat(forcing_block, 3, axis=1), 3, axis=2)
    left_w, right_w = row_weights(nest_segments(nest_of, row_start - 1, nest_rows + 2))

    nest_state = nest.astype(jnp.float32)
    halo = nest_halo
    for turn_no in range(3):
        if turn_no > 0:
            (halo,) = exchange([nest_state.astype(jnp.bfloat16)])
        nest_state = nest_advance(
            nest_state, halo, forcing_full, nu_nest, relax, vert_mix, left_w, right_w
        )

    blocks = nest_state.reshape(levels, block_rows, 3, block_cols, 3).mean(axis=(2, 4))
    nudge_gap = (blocks - forcing_block).reshape(levels, -1)
    outgoing = jnp.zeros((levels, tiles_x * slots), jnp.float32).at[:, places].set(nudge_gap)
    incoming = lax.all_to_all(outgoing, "gx", split_axis=1, concat_axis=1, tiled=True)
    summed = jnp.zeros_like(flat_parent).at[:, served_ids].add(incoming)
    parent_out = (stepped + feedback[:, None, None] * summed.reshape(stepped.shape)).astype(
        jnp.bfloat16
    )
    return (parent_out, nest_state.astype(jnp.bfloat16))


def solution(mesh):
    placed = (
        P("groups", "gx", Y_AXES),
        P("groups", "gx", Y_AXES),
        P(),
        P(),
        P(),
        P(),
        P(),
        P("gx", Y_AXES, None, None),
        P("gx", Y_AXES, None),
        P(),
    )
    return jax.shard_map(
        body,
        mesh=mesh,
        in_specs=placed,
        out_specs=(P("groups", "gx", Y_AXES), P("groups", "gx", Y_AXES)),
        check_vma=False,
    )
```

```python
import jax
import jax.numpy as jnp
from jax import lax
from jax.sharding import PartitionSpec as P

Y_AXES = ("gy", "gz")
HI = lax.Precision.HIGHEST


def shift_pairs(count):
    forward = [(i, i + 1) for i in range(count - 1)]
    backward = [(i + 1, i) for i in range(count - 1)]
    return forward, backward


def exchange(blocks):
    fwd_x, bwd_x = shift_pairs(lax.axis_size("gx"))
    fwd_y, bwd_y = shift_pairs(lax.axis_size(Y_AXES))
    last_rows = jnp.concatenate([b[:, -1, :] for b in blocks], axis=1)
    first_rows = jnp.concatenate([b[:, 0, :] for b in blocks], axis=1)
    last_cols = jnp.concatenate([b[:, :, -1] for b in blocks], axis=1)
    first_cols = jnp.concatenate([b[:, :, 0] for b in blocks], axis=1)
    above = lax.ppermute(last_rows, "gx", fwd_x)
    below = lax.ppermute(first_rows, "gx", bwd_x)
    left = lax.ppermute(last_cols, Y_AXES, fwd_y)
    right = lax.ppermute(first_cols, Y_AXES, bwd_y)
    out = []
    xo = 0
    yo = 0
    for b in blocks:
        w, h = b.shape[2], b.shape[1]
        out.append(
            (above[:, xo : xo + w], below[:, xo : xo + w], left[:, yo : yo + h], right[:, yo : yo + h])
        )
        xo += w
        yo += h
    return out


def per_row(values, rows, cols):
    if values.ndim == 1:
        return jnp.broadcast_to(values[:, None], (rows, cols)).reshape(rows * cols)
    return jnp.broadcast_to(values[:, :, None], values.shape + (cols,)).reshape(
        values.shape[0], rows * cols
    )


def flat_stencil(flat, rows, cols, halo, up_w=None, down_w=None):
    above, below, left, right = (h.astype(flat.dtype) for h in halo)
    levels = flat.shape[0]
    up = jnp.concatenate([above, flat[:, :-cols]], axis=1)
    down = jnp.concatenate([flat[:, cols:], below], axis=1)
    col = lax.broadcasted_iota(jnp.int32, (1, rows * cols), 1) % cols
    zero = jnp.zeros((levels, 1), flat.dtype)
    west = jnp.where(col == 0, per_row(left, rows, cols), jnp.concatenate([zero, flat[:, :-1]], axis=1))
    east = jnp.where(
        col == cols - 1, per_row(right, rows, cols), jnp.concatenate([flat[:, 1:], zero], axis=1)
    )
    if down_w is not None:
        down = down * down_w[None, :]
        up = up * up_w[None, :]
    return down + up + east + west - 4.0 * flat


def mix_levels(matrix, flat):
    return jnp.dot(matrix, flat, precision=HI, preferred_element_type=jnp.float32)


def nest_segments(nest_of, first, count):
    index_rows = first + jnp.arange(count, dtype=jnp.int32)
    inside = (index_rows >= 0) & (index_rows < nest_of.shape[0])
    return jnp.where(inside, nest_of[jnp.clip(index_rows, 0, nest_of.shape[0] - 1)], -1)


def row_weights(segments):
    left_w = (segments[:-2] == segments[1:-1]).astype(jnp.float32)
    right_w = (segments[2:] == segments[1:-1]).astype(jnp.float32)
    return (left_w, right_w)


def block_expansion(block_rows, block_cols, rows, cols, zero):
    r = lax.broadcasted_iota(jnp.int32, (block_rows * block_cols, rows * cols), 0) + zero
    p = lax.broadcasted_iota(jnp.int32, (block_rows * block_cols, rows * cols), 1)
    hit = ((p // cols) // 3 == r // block_cols) & ((p % cols) // 3 == r % block_cols)
    return hit.astype(jnp.float32)


def body(parent, nest, nu_parent, nu_nest, relax, feedback, vert_mix, fp_owner, fp_cell, nest_of):
    levels, p_rows, p_cols = parent.shape
    _, n_rows, n_cols = nest.shape
    tiles_x = lax.axis_size("gx")
    here_x = lax.axis_index("gx")
    zero = jnp.minimum(here_x, 0)

    parent_halo, nest_halo = exchange([parent, nest])
    centre = parent.astype(jnp.float32).reshape(levels, p_rows * p_cols)
    stencil = flat_stencil(centre, p_rows, p_cols, parent_halo)
    flat_parent = mix_levels(vert_mix, centre + nu_parent[:, None] * stencil)

    owners = fp_owner.reshape(-1)
    cells = fp_cell.reshape(-1)
    requests = owners.shape[0]
    slots = 4 * requests // tiles_x
    owner_ids = jnp.arange(tiles_x, dtype=jnp.int32)
    if slots >= requests:
        chosen = owners[None, :] == owner_ids[:, None]
        wanted = jnp.where(chosen, cells[None, :], 0)
        wanted = jnp.pad(wanted, ((0, 0), (0, slots - requests))).reshape(-1)
    else:
        onehot = (owners[:, None] == owner_ids[None, :]).astype(jnp.int32)
        before = jnp.cumsum(onehot, axis=0) - onehot
        order_in = jnp.sum(before * onehot, axis=1)
        places = owners * slots + order_in
        wanted = jnp.zeros((tiles_x * slots,), jnp.int32).at[places].set(cells)
    served_ids = lax.all_to_all(wanted, "gx", split_axis=0, concat_axis=0, tiled=True)
    answers = lax.all_to_all(
        jnp.take(flat_parent, served_ids, axis=1), "gx", split_axis=1, concat_axis=1, tiled=True
    )
    if slots >= requests:
        answers = answers.reshape(levels, tiles_x, slots)[:, :, :requests]
        forcing_flat = answers[:, 0, :]
        for o in range(1, tiles_x):
            forcing_flat = jnp.where(chosen[o][None, :], answers[:, o, :], forcing_flat)
    else:
        forcing_flat = jnp.take(answers, places, axis=1)

    block_rows = n_rows // 3
    block_cols = n_cols // 3
    expand = block_expansion(block_rows, block_cols, n_rows, n_cols, zero)
    forcing_full = jnp.dot(forcing_flat, expand, precision=HI, preferred_element_type=jnp.float32)
    row_start = here_x * n_rows
    left_w, right_w = row_weights(nest_segments(nest_of, row_start - 1, n_rows + 2))
    up_w = per_row(left_w, n_rows, n_cols)
    down_w = per_row(right_w, n_rows, n_cols)

    nest_state = nest.astype(jnp.float32).reshape(levels, n_rows * n_cols)
    halo = nest_halo
    for turn_no in range(3):
        if turn_no > 0:
            shaped = nest_state.astype(jnp.bfloat16).reshape(levels, n_rows, n_cols)
            (halo,) = exchange([shaped])
        stencil_sum = flat_stencil(nest_state, n_rows, n_cols, halo, up_w, down_w)
        moved = nest_state + nu_nest[:, None] * stencil_sum
        moved = moved + relax[:, None] * (forcing_full - moved)
        nest_state = mix_levels(vert_mix, moved)

    block_sum = lax.dot_general(
        nest_state, expand, (((1,), (1,)), ((), ())), precision=HI, preferred_element_type=jnp.float32
    )
    nudge_gap = block_sum / 9.0 - forcing_flat
    if slots >= requests:
        outgoing = jnp.where(chosen[None, :, :], nudge_gap[:, None, :], 0.0)
        outgoing = jnp.pad(outgoing, ((0, 0), (0, 0), (0, slots - requests)))
        outgoing = outgoing.reshape(levels, tiles_x * slots)
    else:
        outgoing = jnp.zeros((levels, tiles_x * slots), jnp.float32).at[:, places].set(nudge_gap)
    incoming = lax.all_to_all(outgoing, "gx", split_axis=1, concat_axis=1, tiled=True)
    summed = jnp.zeros_like(flat_parent).at[:, served_ids].add(incoming)
    parent_out = (flat_parent + feedback[:, None] * summed).astype(jnp.bfloat16)
    return (
        parent_out.reshape(levels, p_rows, p_cols),
        nest_state.astype(jnp.bfloat16).reshape(levels, n_rows, n_cols),
    )


def solution(mesh):
    placed = (
        P("groups", "gx", Y_AXES),
        P("groups", "gx", Y_AXES),
        P(),
        P(),
        P(),
        P(),
        P(),
        P("gx", Y_AXES, None, None),
        P("gx", Y_AXES, None),
        P(),
    )
    return jax.shard_map(
        body,
        mesh=mesh,
        in_specs=placed,
        out_specs=(P("groups", "gx", Y_AXES), P("groups", "gx", Y_AXES)),
        check_vma=False,
    )
```

```python
import jax
import jax.numpy as jnp
from jax import lax
from jax.sharding import PartitionSpec as P

Y_AXES = ("gy", "gz")
HI = lax.Precision.HIGHEST


def shift_pairs(count):
    forward = [(i, i + 1) for i in range(count - 1)]
    backward = [(i + 1, i) for i in range(count - 1)]
    return forward, backward


def edges_3d(block):
    return (block[:, -1, :], block[:, 0, :], block[:, :, -1], block[:, :, 0])


def edges_flat(flat, rows, cols):
    return (flat[:, (rows - 1) * cols :], flat[:, :cols], flat[:, cols - 1 :: cols], flat[:, ::cols])


def exchange(edge_sets):
    fwd_x, bwd_x = shift_pairs(lax.axis_size("gx"))
    fwd_y, bwd_y = shift_pairs(lax.axis_size(Y_AXES))
    last_rows = jnp.concatenate([e[0] for e in edge_sets], axis=1)
    first_rows = jnp.concatenate([e[1] for e in edge_sets], axis=1)
    last_cols = jnp.concatenate([e[2] for e in edge_sets], axis=1)
    first_cols = jnp.concatenate([e[3] for e in edge_sets], axis=1)
    above = lax.ppermute(last_rows, "gx", fwd_x)
    below = lax.ppermute(first_rows, "gx", bwd_x)
    left = lax.ppermute(last_cols, Y_AXES, fwd_y)
    right = lax.ppermute(first_cols, Y_AXES, bwd_y)
    out = []
    xo = 0
    yo = 0
    for e in edge_sets:
        w, h = e[0].shape[1], e[2].shape[1]
        out.append(
            (above[:, xo : xo + w], below[:, xo : xo + w], left[:, yo : yo + h], right[:, yo : yo + h])
        )
        xo += w
        yo += h
    return out


def per_row(values, rows, cols):
    if values.ndim == 1:
        return jnp.broadcast_to(values[:, None], (rows, cols)).reshape(rows * cols)
    return jnp.broadcast_to(values[:, :, None], values.shape + (cols,)).reshape(
        values.shape[0], rows * cols
    )


def flat_stencil(flat, rows, cols, halo, up_w=None, down_w=None):
    above, below, left, right = (h.astype(flat.dtype) for h in halo)
    levels = flat.shape[0]
    up = jnp.concatenate([above, flat[:, :-cols]], axis=1)
    down = jnp.concatenate([flat[:, cols:], below], axis=1)
    col = lax.broadcasted_iota(jnp.int32, (1, rows * cols), 1) % cols
    zero = jnp.zeros((levels, 1), flat.dtype)
    west = jnp.where(col == 0, per_row(left, rows, cols), jnp.concatenate([zero, flat[:, :-1]], axis=1))
    east = jnp.where(
        col == cols - 1, per_row(right, rows, cols), jnp.concatenate([flat[:, 1:], zero], axis=1)
    )
    if down_w is not None:
        down = down * down_w[None, :]
        up = up * up_w[None, :]
    return down + up + east + west - 4.0 * flat


def mix_levels(matrix, flat):
    return jnp.dot(matrix, flat, precision=lax.Precision.HIGH, preferred_element_type=jnp.float32)


def nest_segments(nest_of, first, count):
    index_rows = first + jnp.arange(count, dtype=jnp.int32)
    inside = (index_rows >= 0) & (index_rows < nest_of.shape[0])
    return jnp.where(inside, nest_of[jnp.clip(index_rows, 0, nest_of.shape[0] - 1)], -1)


def row_weights(segments):
    left_w = (segments[:-2] == segments[1:-1]).astype(jnp.float32)
    right_w = (segments[2:] == segments[1:-1]).astype(jnp.float32)
    return (left_w, right_w)


def column_expansion(block_cols, cols, zero):
    b = lax.broadcasted_iota(jnp.int32, (block_cols, cols), 0) + zero
    c = lax.broadcasted_iota(jnp.int32, (block_cols, cols), 1)
    return (c // 3 == b).astype(jnp.float32)


def expand_blocks(block_flat, block_rows, block_cols, cols, expand):
    pieces = []
    for a in range(block_rows):
        wide = jnp.dot(
            block_flat[:, a * block_cols : (a + 1) * block_cols],
            expand,
            precision=HI,
            preferred_element_type=jnp.float32,
        )
        pieces += [wide, wide, wide]
    return jnp.concatenate(pieces, axis=1)


def block_sums(flat, block_rows, cols, expand):
    pieces = []
    for a in range(block_rows):
        rows3 = (
            flat[:, (3 * a) * cols : (3 * a + 1) * cols]
            + flat[:, (3 * a + 1) * cols : (3 * a + 2) * cols]
        ) + flat[:, (3 * a + 2) * cols : (3 * a + 3) * cols]
        pieces.append(
            lax.dot_general(
                rows3, expand, (((1,), (1,)), ((), ())), precision=HI,
                preferred_element_type=jnp.float32,
            )
        )
    return jnp.concatenate(pieces, axis=1)


def body(parent, nest, nu_parent, nu_nest, relax, feedback, vert_mix, fp_owner, fp_cell, nest_of):
    levels, p_rows, p_cols = parent.shape
    _, n_rows, n_cols = nest.shape
    tiles_x = lax.axis_size("gx")
    here_x = lax.axis_index("gx")
    zero = jnp.minimum(here_x, 0)

    parent_halo, nest_halo = exchange([edges_3d(parent), edges_3d(nest)])
    centre = parent.astype(jnp.float32).reshape(levels, p_rows * p_cols)
    stencil = flat_stencil(centre, p_rows, p_cols, parent_halo)
    flat_parent = mix_levels(vert_mix, centre + nu_parent[:, None] * stencil)

    owners = fp_owner.reshape(-1)
    cells = fp_cell.reshape(-1)
    requests = owners.shape[0]
    slots = 4 * requests // tiles_x
    owner_ids = jnp.arange(tiles_x, dtype=jnp.int32)
    if slots >= requests:
        chosen = owners[None, :] == owner_ids[:, None]
        wanted = jnp.where(chosen, cells[None, :], 0)
        wanted = jnp.pad(wanted, ((0, 0), (0, slots - requests))).reshape(-1)
    else:
        onehot = (owners[:, None] == owner_ids[None, :]).astype(jnp.int32)
        before = jnp.cumsum(onehot, axis=0) - onehot
        order_in = jnp.sum(before * onehot, axis=1)
        places = owners * slots + order_in
        wanted = jnp.zeros((tiles_x * slots,), jnp.int32).at[places].set(cells)
    served_ids = lax.all_to_all(wanted, "gx", split_axis=0, concat_axis=0, tiled=True)
    answers = lax.all_to_all(
        jnp.take(flat_parent, served_ids, axis=1), "gx", split_axis=1, concat_axis=1, tiled=True
    )
    if slots >= requests:
        answers = answers.reshape(levels, tiles_x, slots)[:, :, :requests]
        forcing_flat = answers[:, 0, :]
        for o in range(1, tiles_x):
            forcing_flat = jnp.where(chosen[o][None, :], answers[:, o, :], forcing_flat)
    else:
        forcing_flat = jnp.take(answers, places, axis=1)

    block_rows = n_rows // 3
    block_cols = n_cols // 3
    expand = column_expansion(block_cols, n_cols, zero)
    forcing_full = expand_blocks(forcing_flat, block_rows, block_cols, n_cols, expand)
    row_start = here_x * n_rows
    left_w, right_w = row_weights(nest_segments(nest_of, row_start - 1, n_rows + 2))
    up_w = per_row(left_w, n_rows, n_cols)
    down_w = per_row(right_w, n_rows, n_cols)

    nest_state = nest.astype(jnp.float32).reshape(levels, n_rows * n_cols)
    halo = nest_halo
    for turn_no in range(3):
        if turn_no > 0:
            (halo,) = exchange([edges_flat(nest_state.astype(jnp.bfloat16), n_rows, n_cols)])
        stencil_sum = flat_stencil(nest_state, n_rows, n_cols, halo, up_w, down_w)
        moved = nest_state + nu_nest[:, None] * stencil_sum
        moved = moved + relax[:, None] * (forcing_full - moved)
        nest_state = mix_levels(vert_mix, moved)

    block_sum = block_sums(nest_state, block_rows, n_cols, expand)
    nudge_gap = block_sum / 9.0 - forcing_flat
    if slots >= requests:
        outgoing = jnp.where(chosen[None, :, :], nudge_gap[:, None, :], 0.0)
        outgoing = jnp.pad(outgoing, ((0, 0), (0, 0), (0, slots - requests)))
        outgoing = outgoing.reshape(levels, tiles_x * slots)
    else:
        outgoing = jnp.zeros((levels, tiles_x * slots), jnp.float32).at[:, places].set(nudge_gap)
    incoming = lax.all_to_all(outgoing, "gx", split_axis=1, concat_axis=1, tiled=True)
    summed = jnp.zeros_like(flat_parent).at[:, served_ids].add(incoming)
    parent_out = (flat_parent + feedback[:, None] * summed).astype(jnp.bfloat16)
    return (
        parent_out.reshape(levels, p_rows, p_cols),
        nest_state.astype(jnp.bfloat16).reshape(levels, n_rows, n_cols),
    )


def solution(mesh):
    placed = (
        P("groups", "gx", Y_AXES),
        P("groups", "gx", Y_AXES),
        P(),
        P(),
        P(),
        P(),
        P(),
        P("gx", Y_AXES, None, None),
        P("gx", Y_AXES, None),
        P(),
    )
    return jax.shard_map(
        body,
        mesh=mesh,
        in_specs=placed,
        out_specs=(P("groups", "gx", Y_AXES), P("groups", "gx", Y_AXES)),
        check_vma=False,
    )
```

```python
import jax
import jax.numpy as jnp
from jax import lax
from jax.sharding import PartitionSpec as P

Y_AXES = ("gy", "gz")
HI = lax.Precision.HIGHEST


def shift_pairs(count):
    forward = [(i, i + 1) for i in range(count - 1)]
    backward = [(i + 1, i) for i in range(count - 1)]
    return forward, backward


def edges_3d(block):
    return (block[:, -1, :], block[:, 0, :], block[:, :, -1], block[:, :, 0])


def edges_flat(flat, rows, cols):
    return (flat[:, (rows - 1) * cols :], flat[:, :cols], flat[:, cols - 1 :: cols], flat[:, ::cols])


def exchange(edge_sets):
    fwd_x, bwd_x = shift_pairs(lax.axis_size("gx"))
    fwd_y, bwd_y = shift_pairs(lax.axis_size(Y_AXES))
    last_rows = jnp.concatenate([e[0] for e in edge_sets], axis=1)
    first_rows = jnp.concatenate([e[1] for e in edge_sets], axis=1)
    last_cols = jnp.concatenate([e[2] for e in edge_sets], axis=1)
    first_cols = jnp.concatenate([e[3] for e in edge_sets], axis=1)
    above = lax.ppermute(last_rows, "gx", fwd_x)
    below = lax.ppermute(first_rows, "gx", bwd_x)
    left = lax.ppermute(last_cols, Y_AXES, fwd_y)
    right = lax.ppermute(first_cols, Y_AXES, bwd_y)
    out = []
    xo = 0
    yo = 0
    for e in edge_sets:
        w, h = e[0].shape[1], e[2].shape[1]
        out.append(
            (above[:, xo : xo + w], below[:, xo : xo + w], left[:, yo : yo + h], right[:, yo : yo + h])
        )
        xo += w
        yo += h
    return out


def per_row(values, rows, cols):
    if values.ndim == 1:
        return jnp.broadcast_to(values[:, None], (rows, cols)).reshape(rows * cols)
    return jnp.broadcast_to(values[:, :, None], values.shape + (cols,)).reshape(
        values.shape[0], rows * cols
    )


def flat_stencil(flat, rows, cols, halo, up_w=None, down_w=None):
    above, below, left, right = (h.astype(flat.dtype) for h in halo)
    levels = flat.shape[0]
    up = jnp.concatenate([above, flat[:, :-cols]], axis=1)
    down = jnp.concatenate([flat[:, cols:], below], axis=1)
    col = lax.broadcasted_iota(jnp.int32, (1, rows * cols), 1) % cols
    zero = jnp.zeros((levels, 1), flat.dtype)
    west = jnp.where(col == 0, per_row(left, rows, cols), jnp.concatenate([zero, flat[:, :-1]], axis=1))
    east = jnp.where(
        col == cols - 1, per_row(right, rows, cols), jnp.concatenate([flat[:, 1:], zero], axis=1)
    )
    if down_w is not None:
        down = down * down_w[None, :]
        up = up * up_w[None, :]
    return down + up + east + west - 4.0 * flat


def mix_levels(matrix, flat):
    return jnp.dot(matrix, flat, precision=HI, preferred_element_type=jnp.float32)


def nest_segments(nest_of, first, count):
    index_rows = first + jnp.arange(count, dtype=jnp.int32)
    inside = (index_rows >= 0) & (index_rows < nest_of.shape[0])
    return jnp.where(inside, nest_of[jnp.clip(index_rows, 0, nest_of.shape[0] - 1)], -1)


def row_weights(segments):
    left_w = (segments[:-2] == segments[1:-1]).astype(jnp.float32)
    right_w = (segments[2:] == segments[1:-1]).astype(jnp.float32)
    return (left_w, right_w)


def column_expansion(block_cols, cols, zero):
    b = lax.broadcasted_iota(jnp.int32, (block_cols, cols), 0) + zero
    c = lax.broadcasted_iota(jnp.int32, (block_cols, cols), 1)
    return (c // 3 == b).astype(jnp.float32)


def expand_blocks(block_flat, block_rows, block_cols, cols, expand):
    pieces = []
    for a in range(block_rows):
        wide = jnp.dot(
            block_flat[:, a * block_cols : (a + 1) * block_cols],
            expand,
            precision=HI,
            preferred_element_type=jnp.float32,
        )
        pieces += [wide, wide, wide]
    return jnp.concatenate(pieces, axis=1)


def block_sums(flat, block_rows, cols, expand):
    pieces = []
    for a in range(block_rows):
        rows3 = (
            flat[:, (3 * a) * cols : (3 * a + 1) * cols]
            + flat[:, (3 * a + 1) * cols : (3 * a + 2) * cols]
        ) + flat[:, (3 * a + 2) * cols : (3 * a + 3) * cols]
        pieces.append(
            lax.dot_general(
                rows3, expand, (((1,), (1,)), ((), ())), precision=HI,
                preferred_element_type=jnp.float32,
            )
        )
    return jnp.concatenate(pieces, axis=1)


def split3(values):
    hi = values.astype(jnp.bfloat16)
    rest = values - hi.astype(jnp.float32)
    mid = rest.astype(jnp.bfloat16)
    lo = (rest - mid.astype(jnp.float32)).astype(jnp.bfloat16)
    return hi, mid, lo


def scatter_add_columns(values, ids, width):
    levels = values.shape[0]
    onehot = (ids[:, None] == lax.broadcasted_iota(jnp.int32, (1, width), 1)).astype(jnp.bfloat16)
    parts = jnp.concatenate(split3(values), axis=0)
    total = jnp.dot(parts, onehot, preferred_element_type=jnp.float32)
    return (total[:levels] + total[levels : 2 * levels]) + total[2 * levels :]


def body(parent, nest, nu_parent, nu_nest, relax, feedback, vert_mix, fp_owner, fp_cell, nest_of):
    levels, p_rows, p_cols = parent.shape
    _, n_rows, n_cols = nest.shape
    tiles_x = lax.axis_size("gx")
    here_x = lax.axis_index("gx")
    zero = jnp.minimum(here_x, 0)

    parent_halo, nest_halo = exchange([edges_3d(parent), edges_3d(nest)])
    centre = parent.astype(jnp.float32).reshape(levels, p_rows * p_cols)
    stencil = flat_stencil(centre, p_rows, p_cols, parent_halo)
    flat_parent = mix_levels(vert_mix, centre + nu_parent[:, None] * stencil)

    owners = fp_owner.reshape(-1)
    cells = fp_cell.reshape(-1)
    requests = owners.shape[0]
    slots = 4 * requests // tiles_x
    owner_ids = jnp.arange(tiles_x, dtype=jnp.int32)
    if slots >= requests:
        chosen = owners[None, :] == owner_ids[:, None]
        wanted = jnp.where(chosen, cells[None, :], 0)
        wanted = jnp.pad(wanted, ((0, 0), (0, slots - requests))).reshape(-1)
    else:
        onehot = (owners[:, None] == owner_ids[None, :]).astype(jnp.int32)
        before = jnp.cumsum(onehot, axis=0) - onehot
        order_in = jnp.sum(before * onehot, axis=1)
        places = owners * slots + order_in
        wanted = jnp.zeros((tiles_x * slots,), jnp.int32).at[places].set(cells)
    served_ids = lax.all_to_all(wanted, "gx", split_axis=0, concat_axis=0, tiled=True)
    answers = lax.all_to_all(
        jnp.take(flat_parent, served_ids, axis=1), "gx", split_axis=1, concat_axis=1, tiled=True
    )
    if slots >= requests:
        answers = answers.reshape(levels, tiles_x, slots)[:, :, :requests]
        forcing_flat = answers[:, 0, :]
        for o in range(1, tiles_x):
            forcing_flat = jnp.where(chosen[o][None, :], answers[:, o, :], forcing_flat)
    else:
        forcing_flat = jnp.take(answers, places, axis=1)

    block_rows = n_rows // 3
    block_cols = n_cols // 3
    expand = column_expansion(block_cols, n_cols, zero)
    forcing_full = expand_blocks(forcing_flat, block_rows, block_cols, n_cols, expand)
    row_start = here_x * n_rows
    left_w, right_w = row_weights(nest_segments(nest_of, row_start - 1, n_rows + 2))
    up_w = per_row(left_w, n_rows, n_cols)
    down_w = per_row(right_w, n_rows, n_cols)

    nest_state = nest.astype(jnp.float32).reshape(levels, n_rows * n_cols)
    halo = nest_halo
    for turn_no in range(3):
        if turn_no > 0:
            (halo,) = exchange([edges_flat(nest_state.astype(jnp.bfloat16), n_rows, n_cols)])
        stencil_sum = flat_stencil(nest_state, n_rows, n_cols, halo, up_w, down_w)
        moved = nest_state + nu_nest[:, None] * stencil_sum
        moved = moved + relax[:, None] * (forcing_full - moved)
        nest_state = mix_levels(vert_mix, moved)

    block_sum = block_sums(nest_state, block_rows, n_cols, expand)
    nudge_gap = block_sum / 9.0 - forcing_flat
    if slots >= requests:
        outgoing = jnp.where(chosen[None, :, :], nudge_gap[:, None, :], 0.0)
        outgoing = jnp.pad(outgoing, ((0, 0), (0, 0), (0, slots - requests)))
        outgoing = outgoing.reshape(levels, tiles_x * slots)
    else:
        outgoing = jnp.zeros((levels, tiles_x * slots), jnp.float32).at[:, places].set(nudge_gap)
    incoming = lax.all_to_all(outgoing, "gx", split_axis=1, concat_axis=1, tiled=True)
    summed = scatter_add_columns(incoming, served_ids, flat_parent.shape[1])
    parent_out = (flat_parent + feedback[:, None] * summed).astype(jnp.bfloat16)
    return (
        parent_out.reshape(levels, p_rows, p_cols),
        nest_state.astype(jnp.bfloat16).reshape(levels, n_rows, n_cols),
    )


def solution(mesh):
    placed = (
        P("groups", "gx", Y_AXES),
        P("groups", "gx", Y_AXES),
        P(),
        P(),
        P(),
        P(),
        P(),
        P("gx", Y_AXES, None, None),
        P("gx", Y_AXES, None),
        P(),
    )
    return jax.shard_map(
        body,
        mesh=mesh,
        in_specs=placed,
        out_specs=(P("groups", "gx", Y_AXES), P("groups", "gx", Y_AXES)),
        check_vma=False,
    )
```

```python
import functools

import jax
import jax.numpy as jnp
from jax import lax
from jax.experimental import pallas as pl
from jax.experimental.pallas import tpu as pltpu
from jax.sharding import PartitionSpec as P

Y_AXES = ("gy", "gz")
HI = lax.Precision.HIGHEST


def shift_pairs(count):
    forward = [(i, i + 1) for i in range(count - 1)]
    backward = [(i + 1, i) for i in range(count - 1)]
    return forward, backward


def edges_3d(block):
    return (block[:, -1, :], block[:, 0, :], block[:, :, -1], block[:, :, 0])


def edges_flat(flat, rows, cols):
    return (flat[:, (rows - 1) * cols :], flat[:, :cols], flat[:, cols - 1 :: cols], flat[:, ::cols])


def exchange(edge_sets):
    fwd_x, bwd_x = shift_pairs(lax.axis_size("gx"))
    fwd_y, bwd_y = shift_pairs(lax.axis_size(Y_AXES))
    last_rows = jnp.concatenate([e[0] for e in edge_sets], axis=1)
    first_rows = jnp.concatenate([e[1] for e in edge_sets], axis=1)
    last_cols = jnp.concatenate([e[2] for e in edge_sets], axis=1)
    first_cols = jnp.concatenate([e[3] for e in edge_sets], axis=1)
    above = lax.ppermute(last_rows, "gx", fwd_x)
    below = lax.ppermute(first_rows, "gx", bwd_x)
    left = lax.ppermute(last_cols, Y_AXES, fwd_y)
    right = lax.ppermute(first_cols, Y_AXES, bwd_y)
    out = []
    xo = 0
    yo = 0
    for e in edge_sets:
        w, h = e[0].shape[1], e[2].shape[1]
        out.append(
            (above[:, xo : xo + w], below[:, xo : xo + w], left[:, yo : yo + h], right[:, yo : yo + h])
        )
        xo += w
        yo += h
    return out


def per_row(values, rows, cols):
    if values.ndim == 1:
        return jnp.broadcast_to(values[:, None], (rows, cols)).reshape(rows * cols)
    return jnp.broadcast_to(values[:, :, None], values.shape + (cols,)).reshape(
        values.shape[0], rows * cols
    )


def flat_stencil(flat, rows, cols, halo, up_w=None, down_w=None):
    above, below, left, right = (h.astype(flat.dtype) for h in halo)
    levels = flat.shape[0]
    up = jnp.concatenate([above, flat[:, :-cols]], axis=1)
    down = jnp.concatenate([flat[:, cols:], below], axis=1)
    col = lax.broadcasted_iota(jnp.int32, (1, rows * cols), 1) % cols
    zero = jnp.zeros((levels, 1), flat.dtype)
    west = jnp.where(col == 0, per_row(left, rows, cols), jnp.concatenate([zero, flat[:, :-1]], axis=1))
    east = jnp.where(
        col == cols - 1, per_row(right, rows, cols), jnp.concatenate([flat[:, 1:], zero], axis=1)
    )
    if down_w is not None:
        down = down * down_w[None, :]
        up = up * up_w[None, :]
    return down + up + east + west - 4.0 * flat


def step_kernel(*refs, rows, cols, nest):
    if nest:
        (state_ref, above_ref, below_ref, left_ref, right_ref, forcing_ref, upw_ref, dnw_ref,
         nu_ref, relax_ref, vm_ref, new_ref, lrow_ref, frow_ref, lcol_ref, fcol_ref, up_sc, dn_sc) = refs
    else:
        (state_ref, above_ref, below_ref, left_ref, right_ref, nu_ref, vm_ref,
         new_ref, lrow_ref, frow_ref, lcol_ref, fcol_ref, up_sc, dn_sc) = refs
    n = rows * cols
    state = state_ref[...].astype(jnp.float32)
    levels = state.shape[0]
    up_sc[:, 0:cols] = above_ref[...].astype(jnp.float32)
    up_sc[:, cols:n] = state[:, 0 : n - cols]
    dn_sc[:, 0 : n - cols] = state[:, cols:n]
    dn_sc[:, n - cols : n] = below_ref[...].astype(jnp.float32)
    up = up_sc[...]
    down = dn_sc[...]
    lane = lax.broadcasted_iota(jnp.int32, (levels, n), 1)
    left = left_ref[...].astype(jnp.float32)
    right = right_ref[...].astype(jnp.float32)
    west = pltpu.roll(state, 1, 1)
    east = pltpu.roll(state, n - 1, 1)
    for r in range(rows):
        west = jnp.where(lane == r * cols, left[:, r : r + 1], west)
        east = jnp.where(lane == r * cols + cols - 1, right[:, r : r + 1], east)
    if nest:
        down = down * dnw_ref[...]
        up = up * upw_ref[...]
    stencil = down + up + east + west - 4.0 * state
    moved = state + nu_ref[...] * stencil
    if nest:
        moved = moved + relax_ref[...] * (forcing_ref[...] - moved)
    new = jnp.dot(vm_ref[...], moved, precision=HI, preferred_element_type=jnp.float32)
    new_ref[...] = new
    lrow_ref[...] = new[:, n - cols : n].astype(jnp.bfloat16)
    frow_ref[...] = new[:, 0:cols].astype(jnp.bfloat16)
    narrow = new.astype(jnp.bfloat16)
    p = lax.broadcasted_iota(jnp.int32, (n, rows), 0)
    j = lax.broadcasted_iota(jnp.int32, (n, rows), 1)
    last_sel = (p == j * cols + (cols - 1)).astype(jnp.bfloat16)
    first_sel = (p == j * cols).astype(jnp.bfloat16)
    lcol_ref[...] = jnp.dot(narrow, last_sel, preferred_element_type=jnp.float32).astype(jnp.bfloat16)
    fcol_ref[...] = jnp.dot(narrow, first_sel, preferred_element_type=jnp.float32).astype(jnp.bfloat16)


def stencil_step(state, halo, nu, vert_mix, rows, cols, forcing=None, up_w=None, down_w=None, relax=None):
    levels = state.shape[0]
    n = rows * cols
    nest = forcing is not None
    above, below, left, right = halo
    if nest:
        args = (state, above, below, left, right, forcing, up_w[None, :], down_w[None, :],
                nu[:, None], relax[:, None], vert_mix)
    else:
        args = (state, above, below, left, right, nu[:, None], vert_mix)
    out_shape = (
        jax.ShapeDtypeStruct((levels, n), jnp.float32),
        jax.ShapeDtypeStruct((levels, cols), jnp.bfloat16),
        jax.ShapeDtypeStruct((levels, cols), jnp.bfloat16),
        jax.ShapeDtypeStruct((levels, rows), jnp.bfloat16),
        jax.ShapeDtypeStruct((levels, rows), jnp.bfloat16),
    )
    flops = 2 * levels * levels * n * 6 + 4 * levels * n * rows + 20 * levels * n
    moved_bytes = sum(int(a.size) * a.dtype.itemsize for a in args) + levels * n * 4
    new, lrow, frow, lcol, fcol = pl.pallas_call(
        functools.partial(step_kernel, rows=rows, cols=cols, nest=nest),
        out_shape=out_shape,
        scratch_shapes=[pltpu.VMEM((levels, n), jnp.float32), pltpu.VMEM((levels, n), jnp.float32)],
        cost_estimate=pl.CostEstimate(flops=flops, bytes_accessed=moved_bytes, transcendentals=0),
    )(*args)
    return new, (lrow, frow, lcol, fcol)


def mix_levels(matrix, flat):
    return jnp.dot(matrix, flat, precision=HI, preferred_element_type=jnp.float32)


def nest_segments(nest_of, first, count):
    index_rows = first + jnp.arange(count, dtype=jnp.int32)
    inside = (index_rows >= 0) & (index_rows < nest_of.shape[0])
    return jnp.where(inside, nest_of[jnp.clip(index_rows, 0, nest_of.shape[0] - 1)], -1)


def row_weights(segments):
    left_w = (segments[:-2] == segments[1:-1]).astype(jnp.float32)
    right_w = (segments[2:] == segments[1:-1]).astype(jnp.float32)
    return (left_w, right_w)


def column_expansion(block_cols, cols, zero):
    b = lax.broadcasted_iota(jnp.int32, (block_cols, cols), 0) + zero
    c = lax.broadcasted_iota(jnp.int32, (block_cols, cols), 1)
    return (c // 3 == b).astype(jnp.float32)


def expand_blocks(block_flat, block_rows, block_cols, cols, expand):
    pieces = []
    for a in range(block_rows):
        wide = jnp.dot(
            block_flat[:, a * block_cols : (a + 1) * block_cols],
            expand,
            precision=HI,
            preferred_element_type=jnp.float32,
        )
        pieces += [wide, wide, wide]
    return jnp.concatenate(pieces, axis=1)


def block_sums(flat, block_rows, cols, expand):
    pieces = []
    for a in range(block_rows):
        rows3 = (
            flat[:, (3 * a) * cols : (3 * a + 1) * cols]
            + flat[:, (3 * a + 1) * cols : (3 * a + 2) * cols]
        ) + flat[:, (3 * a + 2) * cols : (3 * a + 3) * cols]
        pieces.append(
            lax.dot_general(
                rows3, expand, (((1,), (1,)), ((), ())), precision=HI,
                preferred_element_type=jnp.float32,
            )
        )
    return jnp.concatenate(pieces, axis=1)


def split3(values):
    hi = values.astype(jnp.bfloat16)
    rest = values - hi.astype(jnp.float32)
    mid = rest.astype(jnp.bfloat16)
    lo = (rest - mid.astype(jnp.float32)).astype(jnp.bfloat16)
    return hi, mid, lo


def scatter_add_columns(values, ids, width):
    levels = values.shape[0]
    onehot = (ids[:, None] == lax.broadcasted_iota(jnp.int32, (1, width), 1)).astype(jnp.bfloat16)
    parts = jnp.concatenate(split3(values), axis=0)
    total = jnp.dot(parts, onehot, preferred_element_type=jnp.float32)
    return (total[:levels] + total[levels : 2 * levels]) + total[2 * levels :]


def body(parent, nest, nu_parent, nu_nest, relax, feedback, vert_mix, fp_owner, fp_cell, nest_of):
    levels, p_rows, p_cols = parent.shape
    _, n_rows, n_cols = nest.shape
    tiles_x = lax.axis_size("gx")
    here_x = lax.axis_index("gx")
    zero = jnp.minimum(here_x, 0)

    parent_halo, nest_halo = exchange([edges_3d(parent), edges_3d(nest)])
    flat_parent, _ = stencil_step(
        parent.reshape(levels, p_rows * p_cols), parent_halo, nu_parent, vert_mix, p_rows, p_cols
    )

    owners = fp_owner.reshape(-1)
    cells = fp_cell.reshape(-1)
    requests = owners.shape[0]
    slots = 4 * requests // tiles_x
    owner_ids = jnp.arange(tiles_x, dtype=jnp.int32)
    if slots >= requests:
        chosen = owners[None, :] == owner_ids[:, None]
        wanted = jnp.where(chosen, cells[None, :], 0)
        wanted = jnp.pad(wanted, ((0, 0), (0, slots - requests))).reshape(-1)
    else:
        onehot = (owners[:, None] == owner_ids[None, :]).astype(jnp.int32)
        before = jnp.cumsum(onehot, axis=0) - onehot
        order_in = jnp.sum(before * onehot, axis=1)
        places = owners * slots + order_in
        wanted = jnp.zeros((tiles_x * slots,), jnp.int32).at[places].set(cells)
    served_ids = lax.all_to_all(wanted, "gx", split_axis=0, concat_axis=0, tiled=True)
    answers = lax.all_to_all(
        jnp.take(flat_parent, served_ids, axis=1), "gx", split_axis=1, concat_axis=1, tiled=True
    )
    if slots >= requests:
        answers = answers.reshape(levels, tiles_x, slots)[:, :, :requests]
        forcing_flat = answers[:, 0, :]
        for o in range(1, tiles_x):
            forcing_flat = jnp.where(chosen[o][None, :], answers[:, o, :], forcing_flat)
    else:
        forcing_flat = jnp.take(answers, places, axis=1)

    block_rows = n_rows // 3
    block_cols = n_cols // 3
    expand = column_expansion(block_cols, n_cols, zero)
    forcing_full = expand_blocks(forcing_flat, block_rows, block_cols, n_cols, expand)
    row_start = here_x * n_rows
    left_w, right_w = row_weights(nest_segments(nest_of, row_start - 1, n_rows + 2))
    up_w = per_row(left_w, n_rows, n_cols)
    down_w = per_row(right_w, n_rows, n_cols)

    nest_state = nest.reshape(levels, n_rows * n_cols)
    halo = nest_halo
    for turn_no in range(3):
        if turn_no > 0:
            (halo,) = exchange([edges])
        nest_state, edges = stencil_step(
            nest_state, halo, nu_nest, vert_mix, n_rows, n_cols, forcing_full, up_w, down_w, relax
        )

    block_sum = block_sums(nest_state, block_rows, n_cols, expand)
    nudge_gap = block_sum / 9.0 - forcing_flat
    if slots >= requests:
        outgoing = jnp.where(chosen[None, :, :], nudge_gap[:, None, :], 0.0)
        outgoing = jnp.pad(outgoing, ((0, 0), (0, 0), (0, slots - requests)))
        outgoing = outgoing.reshape(levels, tiles_x * slots)
    else:
        outgoing = jnp.zeros((levels, tiles_x * slots), jnp.float32).at[:, places].set(nudge_gap)
    incoming = lax.all_to_all(outgoing, "gx", split_axis=1, concat_axis=1, tiled=True)
    summed = scatter_add_columns(incoming, served_ids, flat_parent.shape[1])
    parent_out = (flat_parent + feedback[:, None] * summed).astype(jnp.bfloat16)
    return (
        parent_out.reshape(levels, p_rows, p_cols),
        nest_state.astype(jnp.bfloat16).reshape(levels, n_rows, n_cols),
    )


def solution(mesh):
    placed = (
        P("groups", "gx", Y_AXES),
        P("groups", "gx", Y_AXES),
        P(),
        P(),
        P(),
        P(),
        P(),
        P("gx", Y_AXES, None, None),
        P("gx", Y_AXES, None),
        P(),
    )
    return jax.shard_map(
        body,
        mesh=mesh,
        in_specs=placed,
        out_specs=(P("groups", "gx", Y_AXES), P("groups", "gx", Y_AXES)),
        check_vma=False,
    )
```

```python
import functools

import jax
import jax.numpy as jnp
from jax import lax
from jax.experimental import pallas as pl
from jax.experimental.pallas import tpu as pltpu
from jax.sharding import PartitionSpec as P

Y_AXES = ("gy", "gz")
HI = lax.Precision.HIGHEST


def shift_pairs(count):
    forward = [(i, i + 1) for i in range(count - 1)]
    backward = [(i + 1, i) for i in range(count - 1)]
    return forward, backward


def edges_3d(block):
    return (block[:, -1, :], block[:, 0, :], block[:, :, -1], block[:, :, 0])


def edges_flat(flat, rows, cols):
    return (flat[:, (rows - 1) * cols :], flat[:, :cols], flat[:, cols - 1 :: cols], flat[:, ::cols])


def exchange(edge_sets):
    fwd_x, bwd_x = shift_pairs(lax.axis_size("gx"))
    fwd_y, bwd_y = shift_pairs(lax.axis_size(Y_AXES))
    last_rows = jnp.concatenate([e[0] for e in edge_sets], axis=1)
    first_rows = jnp.concatenate([e[1] for e in edge_sets], axis=1)
    last_cols = jnp.concatenate([e[2] for e in edge_sets], axis=1)
    first_cols = jnp.concatenate([e[3] for e in edge_sets], axis=1)
    above = lax.ppermute(last_rows, "gx", fwd_x)
    below = lax.ppermute(first_rows, "gx", bwd_x)
    left = lax.ppermute(last_cols, Y_AXES, fwd_y)
    right = lax.ppermute(first_cols, Y_AXES, bwd_y)
    out = []
    xo = 0
    yo = 0
    for e in edge_sets:
        w, h = e[0].shape[1], e[2].shape[1]
        out.append(
            (above[:, xo : xo + w], below[:, xo : xo + w], left[:, yo : yo + h], right[:, yo : yo + h])
        )
        xo += w
        yo += h
    return out


def per_row(values, rows, cols):
    if values.ndim == 1:
        return jnp.broadcast_to(values[:, None], (rows, cols)).reshape(rows * cols)
    return jnp.broadcast_to(values[:, :, None], values.shape + (cols,)).reshape(
        values.shape[0], rows * cols
    )


def flat_stencil(flat, rows, cols, halo, up_w=None, down_w=None):
    above, below, left, right = (h.astype(flat.dtype) for h in halo)
    levels = flat.shape[0]
    up = jnp.concatenate([above, flat[:, :-cols]], axis=1)
    down = jnp.concatenate([flat[:, cols:], below], axis=1)
    col = lax.broadcasted_iota(jnp.int32, (1, rows * cols), 1) % cols
    zero = jnp.zeros((levels, 1), flat.dtype)
    west = jnp.where(col == 0, per_row(left, rows, cols), jnp.concatenate([zero, flat[:, :-1]], axis=1))
    east = jnp.where(
        col == cols - 1, per_row(right, rows, cols), jnp.concatenate([flat[:, 1:], zero], axis=1)
    )
    if down_w is not None:
        down = down * down_w[None, :]
        up = up * up_w[None, :]
    return down + up + east + west - 4.0 * flat


def step_kernel(*refs, rows, cols, nest):
    if nest:
        (state_ref, above_ref, below_ref, left_ref, right_ref, forcing_ref, upw_ref, dnw_ref,
         nu_ref, relax_ref, vm_ref, new_ref, lrow_ref, frow_ref, lcol_ref, fcol_ref, up_sc, dn_sc) = refs
    else:
        (state_ref, above_ref, below_ref, left_ref, right_ref, nu_ref, vm_ref,
         new_ref, lrow_ref, frow_ref, lcol_ref, fcol_ref, up_sc, dn_sc) = refs
    n = rows * cols
    state = state_ref[...].astype(jnp.float32)
    levels = state.shape[0]
    up_sc[:, 0:cols] = above_ref[...].astype(jnp.float32)
    up_sc[:, cols:n] = state[:, 0 : n - cols]
    dn_sc[:, 0 : n - cols] = state[:, cols:n]
    dn_sc[:, n - cols : n] = below_ref[...].astype(jnp.float32)
    up = up_sc[...]
    down = dn_sc[...]
    lane = lax.broadcasted_iota(jnp.int32, (levels, n), 1)
    left = left_ref[...].astype(jnp.float32)
    right = right_ref[...].astype(jnp.float32)
    west = pltpu.roll(state, 1, 1)
    east = pltpu.roll(state, n - 1, 1)
    for r in range(rows):
        west = jnp.where(lane == r * cols, left[:, r : r + 1], west)
        east = jnp.where(lane == r * cols + cols - 1, right[:, r : r + 1], east)
    if nest:
        down = down * dnw_ref[...]
        up = up * upw_ref[...]
    stencil = down + up + east + west - 4.0 * state
    moved = state + nu_ref[...] * stencil
    if nest:
        moved = moved + relax_ref[...] * (forcing_ref[...] - moved)
    new = jnp.dot(vm_ref[...], moved, precision=HI, preferred_element_type=jnp.float32)
    new_ref[...] = new
    lrow_ref[...] = new[:, n - cols : n].astype(jnp.bfloat16)
    frow_ref[...] = new[:, 0:cols].astype(jnp.bfloat16)
    narrow = new.astype(jnp.bfloat16)
    p = lax.broadcasted_iota(jnp.int32, (n, rows), 0)
    j = lax.broadcasted_iota(jnp.int32, (n, rows), 1)
    last_sel = (p == j * cols + (cols - 1)).astype(jnp.bfloat16)
    first_sel = (p == j * cols).astype(jnp.bfloat16)
    lcol_ref[...] = jnp.dot(narrow, last_sel, preferred_element_type=jnp.float32).astype(jnp.bfloat16)
    fcol_ref[...] = jnp.dot(narrow, first_sel, preferred_element_type=jnp.float32).astype(jnp.bfloat16)


def stencil_step(state, halo, nu, vert_mix, rows, cols, forcing=None, up_w=None, down_w=None, relax=None):
    levels = state.shape[0]
    n = rows * cols
    nest = forcing is not None
    above, below, left, right = halo
    if nest:
        args = (state, above, below, left, right, forcing, up_w[None, :], down_w[None, :],
                nu[:, None], relax[:, None], vert_mix)
    else:
        args = (state, above, below, left, right, nu[:, None], vert_mix)
    out_shape = (
        jax.ShapeDtypeStruct((levels, n), jnp.float32),
        jax.ShapeDtypeStruct((levels, cols), jnp.bfloat16),
        jax.ShapeDtypeStruct((levels, cols), jnp.bfloat16),
        jax.ShapeDtypeStruct((levels, rows), jnp.bfloat16),
        jax.ShapeDtypeStruct((levels, rows), jnp.bfloat16),
    )
    flops = 2 * levels * levels * n * 6 + 4 * levels * n * rows + 20 * levels * n
    moved_bytes = sum(int(a.size) * a.dtype.itemsize for a in args) + levels * n * 4
    new, lrow, frow, lcol, fcol = pl.pallas_call(
        functools.partial(step_kernel, rows=rows, cols=cols, nest=nest),
        out_shape=out_shape,
        scratch_shapes=[pltpu.VMEM((levels, n), jnp.float32), pltpu.VMEM((levels, n), jnp.float32)],
        cost_estimate=pl.CostEstimate(flops=flops, bytes_accessed=moved_bytes, transcendentals=0),
    )(*args)
    return new, (lrow, frow, lcol, fcol)


def mix_levels(matrix, flat):
    return jnp.dot(matrix, flat, precision=HI, preferred_element_type=jnp.float32)


def nest_segments(nest_of, first, count):
    index_rows = first + jnp.arange(count, dtype=jnp.int32)
    inside = (index_rows >= 0) & (index_rows < nest_of.shape[0])
    return jnp.where(inside, nest_of[jnp.clip(index_rows, 0, nest_of.shape[0] - 1)], -1)


def row_weights(segments):
    left_w = (segments[:-2] == segments[1:-1]).astype(jnp.float32)
    right_w = (segments[2:] == segments[1:-1]).astype(jnp.float32)
    return (left_w, right_w)


def column_expansion(block_cols, cols, zero):
    b = lax.broadcasted_iota(jnp.int32, (block_cols, cols), 0) + zero
    c = lax.broadcasted_iota(jnp.int32, (block_cols, cols), 1)
    return (c // 3 == b).astype(jnp.float32)


def expand_blocks(block_flat, block_rows, block_cols, cols, expand):
    pieces = []
    for a in range(block_rows):
        wide = jnp.dot(
            block_flat[:, a * block_cols : (a + 1) * block_cols],
            expand,
            precision=HI,
            preferred_element_type=jnp.float32,
        )
        pieces += [wide, wide, wide]
    return jnp.concatenate(pieces, axis=1)


def block_sums(flat, block_rows, cols, expand):
    pieces = []
    for a in range(block_rows):
        rows3 = (
            flat[:, (3 * a) * cols : (3 * a + 1) * cols]
            + flat[:, (3 * a + 1) * cols : (3 * a + 2) * cols]
        ) + flat[:, (3 * a + 2) * cols : (3 * a + 3) * cols]
        pieces.append(
            lax.dot_general(
                rows3, expand, (((1,), (1,)), ((), ())), precision=HI,
                preferred_element_type=jnp.float32,
            )
        )
    return jnp.concatenate(pieces, axis=1)


def split3(values):
    hi = values.astype(jnp.bfloat16)
    rest = values - hi.astype(jnp.float32)
    mid = rest.astype(jnp.bfloat16)
    lo = (rest - mid.astype(jnp.float32)).astype(jnp.bfloat16)
    return hi, mid, lo


def shifted_pairs(count, shift):
    return [(i, (i + shift) % count) for i in range(count)]


def gather_columns(values, ids):
    levels, width = values.shape
    onehot = (lax.broadcasted_iota(jnp.int32, (width, 1), 0) == ids[None, :]).astype(jnp.bfloat16)
    parts = jnp.concatenate(split3(values), axis=0)
    total = jnp.dot(parts, onehot, preferred_element_type=jnp.float32)
    return (total[:levels] + total[levels : 2 * levels]) + total[2 * levels :]


def scatter_add_columns(values, ids, width):
    levels = values.shape[0]
    onehot = (ids[:, None] == lax.broadcasted_iota(jnp.int32, (1, width), 1)).astype(jnp.bfloat16)
    parts = jnp.concatenate(split3(values), axis=0)
    total = jnp.dot(parts, onehot, preferred_element_type=jnp.float32)
    return (total[:levels] + total[levels : 2 * levels]) + total[2 * levels :]


def body(parent, nest, nu_parent, nu_nest, relax, feedback, vert_mix, fp_owner, fp_cell, nest_of):
    levels, p_rows, p_cols = parent.shape
    _, n_rows, n_cols = nest.shape
    tiles_x = lax.axis_size("gx")
    here_x = lax.axis_index("gx")
    zero = jnp.minimum(here_x, 0)

    parent_halo, nest_halo = exchange([edges_3d(parent), edges_3d(nest)])
    flat_parent, _ = stencil_step(
        parent.reshape(levels, p_rows * p_cols), parent_halo, nu_parent, vert_mix, p_rows, p_cols
    )

    owners = fp_owner.reshape(-1)
    cells = fp_cell.reshape(-1)
    requests = owners.shape[0]
    slots = 4 * requests // tiles_x
    by_shift = slots >= requests
    if by_shift:
        rel = (owners - here_x + tiles_x) % tiles_x
        chosen = rel[None, :] == jnp.arange(tiles_x, dtype=jnp.int32)[:, None]
        wanted = jnp.where(chosen, cells[None, :], 0)
        served = [wanted[0]] + [
            lax.ppermute(wanted[s], "gx", shifted_pairs(tiles_x, s)) for s in range(1, tiles_x)
        ]
        served_ids = jnp.concatenate(served, axis=0)
        replies = gather_columns(flat_parent, served_ids)
        back = [replies[:, 0:requests]] + [
            lax.ppermute(replies[:, s * requests : (s + 1) * requests], "gx", shifted_pairs(tiles_x, -s))
            for s in range(1, tiles_x)
        ]
        forcing_flat = back[0]
        for s in range(1, tiles_x):
            forcing_flat = jnp.where(chosen[s][None, :], back[s], forcing_flat)
    else:
        owner_ids = jnp.arange(tiles_x, dtype=jnp.int32)
        onehot = (owners[:, None] == owner_ids[None, :]).astype(jnp.int32)
        before = jnp.cumsum(onehot, axis=0) - onehot
        order_in = jnp.sum(before * onehot, axis=1)
        places = owners * slots + order_in
        wanted = jnp.zeros((tiles_x * slots,), jnp.int32).at[places].set(cells)
        served_ids = lax.all_to_all(wanted, "gx", split_axis=0, concat_axis=0, tiled=True)
        answers = lax.all_to_all(
            gather_columns(flat_parent, served_ids), "gx", split_axis=1, concat_axis=1, tiled=True
        )
        forcing_flat = jnp.take(answers, places, axis=1)

    block_rows = n_rows // 3
    block_cols = n_cols // 3
    expand = column_expansion(block_cols, n_cols, zero)
    forcing_full = expand_blocks(forcing_flat, block_rows, block_cols, n_cols, expand)
    row_start = here_x * n_rows
    left_w, right_w = row_weights(nest_segments(nest_of, row_start - 1, n_rows + 2))
    up_w = per_row(left_w, n_rows, n_cols)
    down_w = per_row(right_w, n_rows, n_cols)

    nest_state = nest.reshape(levels, n_rows * n_cols)
    halo = nest_halo
    for turn_no in range(3):
        if turn_no > 0:
            (halo,) = exchange([edges])
        nest_state, edges = stencil_step(
            nest_state, halo, nu_nest, vert_mix, n_rows, n_cols, forcing_full, up_w, down_w, relax
        )

    block_sum = block_sums(nest_state, block_rows, n_cols, expand)
    nudge_gap = block_sum / 9.0 - forcing_flat
    if by_shift:
        outgoing = jnp.where(chosen[:, None, :], nudge_gap[None, :, :], 0.0)
        incoming = jnp.concatenate(
            [outgoing[0]]
            + [lax.ppermute(outgoing[s], "gx", shifted_pairs(tiles_x, s)) for s in range(1, tiles_x)],
            axis=1,
        )
    else:
        outgoing = jnp.zeros((levels, tiles_x * slots), jnp.float32).at[:, places].set(nudge_gap)
        incoming = lax.all_to_all(outgoing, "gx", split_axis=1, concat_axis=1, tiled=True)
    summed = scatter_add_columns(incoming, served_ids, flat_parent.shape[1])
    parent_out = (flat_parent + feedback[:, None] * summed).astype(jnp.bfloat16)
    return (
        parent_out.reshape(levels, p_rows, p_cols),
        nest_state.astype(jnp.bfloat16).reshape(levels, n_rows, n_cols),
    )


def solution(mesh):
    placed = (
        P("groups", "gx", Y_AXES),
        P("groups", "gx", Y_AXES),
        P(),
        P(),
        P(),
        P(),
        P(),
        P("gx", Y_AXES, None, None),
        P("gx", Y_AXES, None),
        P(),
    )
    return jax.shard_map(
        body,
        mesh=mesh,
        in_specs=placed,
        out_specs=(P("groups", "gx", Y_AXES), P("groups", "gx", Y_AXES)),
        check_vma=False,
    )
```

```python
import functools

import jax
import jax.numpy as jnp
from jax import lax
from jax.experimental import pallas as pl
from jax.experimental.pallas import tpu as pltpu
from jax.sharding import PartitionSpec as P

Y_AXES = ("gy", "gz")
HI = lax.Precision.HIGHEST


def shift_pairs(count):
    forward = [(i, i + 1) for i in range(count - 1)]
    backward = [(i + 1, i) for i in range(count - 1)]
    return forward, backward


def edges_3d(block):
    return (block[:, -1, :], block[:, 0, :], block[:, :, -1], block[:, :, 0])


def edges_flat(flat, rows, cols):
    return (flat[:, (rows - 1) * cols :], flat[:, :cols], flat[:, cols - 1 :: cols], flat[:, ::cols])


def exchange(edge_sets):
    fwd_x, bwd_x = shift_pairs(lax.axis_size("gx"))
    fwd_y, bwd_y = shift_pairs(lax.axis_size(Y_AXES))
    last_rows = jnp.concatenate([e[0] for e in edge_sets], axis=1)
    first_rows = jnp.concatenate([e[1] for e in edge_sets], axis=1)
    last_cols = jnp.concatenate([e[2] for e in edge_sets], axis=1)
    first_cols = jnp.concatenate([e[3] for e in edge_sets], axis=1)
    above = lax.ppermute(last_rows, "gx", fwd_x)
    below = lax.ppermute(first_rows, "gx", bwd_x)
    left = lax.ppermute(last_cols, Y_AXES, fwd_y)
    right = lax.ppermute(first_cols, Y_AXES, bwd_y)
    out = []
    xo = 0
    yo = 0
    for e in edge_sets:
        w, h = e[0].shape[1], e[2].shape[1]
        out.append(
            (above[:, xo : xo + w], below[:, xo : xo + w], left[:, yo : yo + h], right[:, yo : yo + h])
        )
        xo += w
        yo += h
    return out


def per_row(values, rows, cols):
    if values.ndim == 1:
        return jnp.broadcast_to(values[:, None], (rows, cols)).reshape(rows * cols)
    return jnp.broadcast_to(values[:, :, None], values.shape + (cols,)).reshape(
        values.shape[0], rows * cols
    )


def flat_stencil(flat, rows, cols, halo, up_w=None, down_w=None):
    above, below, left, right = (h.astype(flat.dtype) for h in halo)
    levels = flat.shape[0]
    up = jnp.concatenate([above, flat[:, :-cols]], axis=1)
    down = jnp.concatenate([flat[:, cols:], below], axis=1)
    col = lax.broadcasted_iota(jnp.int32, (1, rows * cols), 1) % cols
    zero = jnp.zeros((levels, 1), flat.dtype)
    west = jnp.where(col == 0, per_row(left, rows, cols), jnp.concatenate([zero, flat[:, :-1]], axis=1))
    east = jnp.where(
        col == cols - 1, per_row(right, rows, cols), jnp.concatenate([flat[:, 1:], zero], axis=1)
    )
    if down_w is not None:
        down = down * down_w[None, :]
        up = up * up_w[None, :]
    return down + up + east + west - 4.0 * flat


def step_kernel(*refs, rows, cols, nest):
    if nest:
        (state_ref, above_ref, below_ref, left_ref, right_ref, forcing_ref, upw_ref, dnw_ref,
         nu_ref, relax_ref, vm_ref, new_ref, lrow_ref, frow_ref, lcol_ref, fcol_ref, up_sc, dn_sc) = refs
    else:
        (state_ref, above_ref, below_ref, left_ref, right_ref, nu_ref, vm_ref,
         new_ref, lrow_ref, frow_ref, lcol_ref, fcol_ref, up_sc, dn_sc) = refs
    n = rows * cols
    state = state_ref[...].astype(jnp.float32)
    levels = state.shape[0]
    up_sc[:, 0:cols] = above_ref[...].astype(jnp.float32)
    up_sc[:, cols:n] = state[:, 0 : n - cols]
    dn_sc[:, 0 : n - cols] = state[:, cols:n]
    dn_sc[:, n - cols : n] = below_ref[...].astype(jnp.float32)
    up = up_sc[...]
    down = dn_sc[...]
    lane = lax.broadcasted_iota(jnp.int32, (levels, n), 1)
    left = left_ref[...].astype(jnp.float32)
    right = right_ref[...].astype(jnp.float32)
    west = pltpu.roll(state, 1, 1)
    east = pltpu.roll(state, n - 1, 1)
    for r in range(rows):
        west = jnp.where(lane == r * cols, left[:, r : r + 1], west)
        east = jnp.where(lane == r * cols + cols - 1, right[:, r : r + 1], east)
    if nest:
        down = down * dnw_ref[...]
        up = up * upw_ref[...]
    stencil = down + up + east + west - 4.0 * state
    moved = state + nu_ref[...] * stencil
    if nest:
        moved = moved + relax_ref[...] * (forcing_ref[...] - moved)
    new = jnp.dot(vm_ref[...], moved, precision=HI, preferred_element_type=jnp.float32)
    new_ref[...] = new
    lrow_ref[...] = new[:, n - cols : n].astype(jnp.bfloat16)
    frow_ref[...] = new[:, 0:cols].astype(jnp.bfloat16)
    narrow = new.astype(jnp.bfloat16)
    p = lax.broadcasted_iota(jnp.int32, (n, rows), 0)
    j = lax.broadcasted_iota(jnp.int32, (n, rows), 1)
    last_sel = (p == j * cols + (cols - 1)).astype(jnp.bfloat16)
    first_sel = (p == j * cols).astype(jnp.bfloat16)
    lcol_ref[...] = jnp.dot(narrow, last_sel, preferred_element_type=jnp.float32).astype(jnp.bfloat16)
    fcol_ref[...] = jnp.dot(narrow, first_sel, preferred_element_type=jnp.float32).astype(jnp.bfloat16)


def stencil_step(state, halo, nu, vert_mix, rows, cols, forcing=None, up_w=None, down_w=None, relax=None):
    levels = state.shape[0]
    n = rows * cols
    nest = forcing is not None
    above, below, left, right = halo
    if nest:
        args = (state, above, below, left, right, forcing, up_w[None, :], down_w[None, :],
                nu[:, None], relax[:, None], vert_mix)
    else:
        args = (state, above, below, left, right, nu[:, None], vert_mix)
    out_shape = (
        jax.ShapeDtypeStruct((levels, n), jnp.float32),
        jax.ShapeDtypeStruct((levels, cols), jnp.bfloat16),
        jax.ShapeDtypeStruct((levels, cols), jnp.bfloat16),
        jax.ShapeDtypeStruct((levels, rows), jnp.bfloat16),
        jax.ShapeDtypeStruct((levels, rows), jnp.bfloat16),
    )
    flops = 2 * levels * levels * n * 6 + 4 * levels * n * rows + 20 * levels * n
    moved_bytes = sum(int(a.size) * a.dtype.itemsize for a in args) + levels * n * 4
    new, lrow, frow, lcol, fcol = pl.pallas_call(
        functools.partial(step_kernel, rows=rows, cols=cols, nest=nest),
        out_shape=out_shape,
        scratch_shapes=[pltpu.VMEM((levels, n), jnp.float32), pltpu.VMEM((levels, n), jnp.float32)],
        cost_estimate=pl.CostEstimate(flops=flops, bytes_accessed=moved_bytes, transcendentals=0),
    )(*args)
    return new, (lrow, frow, lcol, fcol)


def mix_levels(matrix, flat):
    return jnp.dot(matrix, flat, precision=HI, preferred_element_type=jnp.float32)


def nest_segments(nest_of, first, count):
    index_rows = first + jnp.arange(count, dtype=jnp.int32)
    inside = (index_rows >= 0) & (index_rows < nest_of.shape[0])
    return jnp.where(inside, nest_of[jnp.clip(index_rows, 0, nest_of.shape[0] - 1)], -1)


def row_weights(segments):
    left_w = (segments[:-2] == segments[1:-1]).astype(jnp.float32)
    right_w = (segments[2:] == segments[1:-1]).astype(jnp.float32)
    return (left_w, right_w)


def column_expansion(block_cols, cols, zero):
    b = lax.broadcasted_iota(jnp.int32, (block_cols, cols), 0) + zero
    c = lax.broadcasted_iota(jnp.int32, (block_cols, cols), 1)
    return (c // 3 == b).astype(jnp.float32)


def expand_blocks(block_flat, block_rows, block_cols, cols, expand):
    pieces = []
    for a in range(block_rows):
        wide = jnp.dot(
            block_flat[:, a * block_cols : (a + 1) * block_cols],
            expand,
            precision=HI,
            preferred_element_type=jnp.float32,
        )
        pieces += [wide, wide, wide]
    return jnp.concatenate(pieces, axis=1)


def block_sums(flat, block_rows, cols, expand):
    pieces = []
    for a in range(block_rows):
        rows3 = (
            flat[:, (3 * a) * cols : (3 * a + 1) * cols]
            + flat[:, (3 * a + 1) * cols : (3 * a + 2) * cols]
        ) + flat[:, (3 * a + 2) * cols : (3 * a + 3) * cols]
        pieces.append(
            lax.dot_general(
                rows3, expand, (((1,), (1,)), ((), ())), precision=HI,
                preferred_element_type=jnp.float32,
            )
        )
    return jnp.concatenate(pieces, axis=1)


def split3(values):
    hi = lax.reduce_precision(values, exponent_bits=8, mantissa_bits=7)
    rest = values - hi
    mid = lax.reduce_precision(rest, exponent_bits=8, mantissa_bits=7)
    lo = rest - mid
    return hi.astype(jnp.bfloat16), mid.astype(jnp.bfloat16), lo.astype(jnp.bfloat16)


def shifted_pairs(count, shift):
    return [(i, (i + shift) % count) for i in range(count)]


def gather_columns(values, ids):
    levels, width = values.shape
    onehot = (lax.broadcasted_iota(jnp.int32, (width, 1), 0) == ids[None, :]).astype(jnp.bfloat16)
    parts = jnp.concatenate(split3(values), axis=0)
    total = jnp.dot(parts, onehot, preferred_element_type=jnp.float32)
    return (total[:levels] + total[levels : 2 * levels]) + total[2 * levels :]


def scatter_add_columns(values, ids, width):
    levels = values.shape[0]
    onehot = (ids[:, None] == lax.broadcasted_iota(jnp.int32, (1, width), 1)).astype(jnp.bfloat16)
    parts = jnp.concatenate(split3(values), axis=0)
    total = jnp.dot(parts, onehot, preferred_element_type=jnp.float32)
    return (total[:levels] + total[levels : 2 * levels]) + total[2 * levels :]


def body(parent, nest, nu_parent, nu_nest, relax, feedback, vert_mix, fp_owner, fp_cell, nest_of):
    levels, p_rows, p_cols = parent.shape
    _, n_rows, n_cols = nest.shape
    tiles_x = lax.axis_size("gx")
    here_x = lax.axis_index("gx")
    zero = jnp.minimum(here_x, 0)

    parent_halo, nest_halo = exchange([edges_3d(parent), edges_3d(nest)])
    flat_parent, _ = stencil_step(
        parent.reshape(levels, p_rows * p_cols), parent_halo, nu_parent, vert_mix, p_rows, p_cols
    )

    owners = fp_owner.reshape(-1)
    cells = fp_cell.reshape(-1)
    requests = owners.shape[0]
    slots = 4 * requests // tiles_x
    by_shift = slots >= requests
    if by_shift:
        rel = (owners - here_x + tiles_x) % tiles_x
        chosen = rel[None, :] == jnp.arange(tiles_x, dtype=jnp.int32)[:, None]
        wanted = jnp.where(chosen, cells[None, :], 0)
        served = [wanted[0]] + [
            lax.ppermute(wanted[s], "gx", shifted_pairs(tiles_x, s)) for s in range(1, tiles_x)
        ]
        served_ids = jnp.concatenate(served, axis=0)
        replies = gather_columns(flat_parent, served_ids)
        back = [replies[:, 0:requests]] + [
            lax.ppermute(replies[:, s * requests : (s + 1) * requests], "gx", shifted_pairs(tiles_x, -s))
            for s in range(1, tiles_x)
        ]
        forcing_flat = back[0]
        for s in range(1, tiles_x):
            forcing_flat = jnp.where(chosen[s][None, :], back[s], forcing_flat)
    else:
        owner_ids = jnp.arange(tiles_x, dtype=jnp.int32)
        onehot = (owners[:, None] == owner_ids[None, :]).astype(jnp.int32)
        before = jnp.cumsum(onehot, axis=0) - onehot
        order_in = jnp.sum(before * onehot, axis=1)
        places = owners * slots + order_in
        wanted = jnp.zeros((tiles_x * slots,), jnp.int32).at[places].set(cells)
        served_ids = lax.all_to_all(wanted, "gx", split_axis=0, concat_axis=0, tiled=True)
        answers = lax.all_to_all(
            gather_columns(flat_parent, served_ids), "gx", split_axis=1, concat_axis=1, tiled=True
        )
        forcing_flat = jnp.take(answers, places, axis=1)

    block_rows = n_rows // 3
    block_cols = n_cols // 3
    expand = column_expansion(block_cols, n_cols, zero)
    forcing_full = expand_blocks(forcing_flat, block_rows, block_cols, n_cols, expand)
    row_start = here_x * n_rows
    left_w, right_w = row_weights(nest_segments(nest_of, row_start - 1, n_rows + 2))
    up_w = per_row(left_w, n_rows, n_cols)
    down_w = per_row(right_w, n_rows, n_cols)

    nest_state = nest.reshape(levels, n_rows * n_cols)
    halo = nest_halo
    for turn_no in range(3):
        if turn_no > 0:
            (halo,) = exchange([edges])
        nest_state, edges = stencil_step(
            nest_state, halo, nu_nest, vert_mix, n_rows, n_cols, forcing_full, up_w, down_w, relax
        )

    block_sum = block_sums(nest_state, block_rows, n_cols, expand)
    nudge_gap = block_sum / 9.0 - forcing_flat
    if by_shift:
        outgoing = jnp.where(chosen[:, None, :], nudge_gap[None, :, :], 0.0)
        incoming = jnp.concatenate(
            [outgoing[0]]
            + [lax.ppermute(outgoing[s], "gx", shifted_pairs(tiles_x, s)) for s in range(1, tiles_x)],
            axis=1,
        )
    else:
        outgoing = jnp.zeros((levels, tiles_x * slots), jnp.float32).at[:, places].set(nudge_gap)
        incoming = lax.all_to_all(outgoing, "gx", split_axis=1, concat_axis=1, tiled=True)
    summed = scatter_add_columns(incoming, served_ids, flat_parent.shape[1])
    parent_out = (flat_parent + feedback[:, None] * summed).astype(jnp.bfloat16)
    return (
        parent_out.reshape(levels, p_rows, p_cols),
        nest_state.astype(jnp.bfloat16).reshape(levels, n_rows, n_cols),
    )


def solution(mesh):
    placed = (
        P("groups", "gx", Y_AXES),
        P("groups", "gx", Y_AXES),
        P(),
        P(),
        P(),
        P(),
        P(),
        P("gx", Y_AXES, None, None),
        P("gx", Y_AXES, None),
        P(),
    )
    return jax.shard_map(
        body,
        mesh=mesh,
        in_specs=placed,
        out_specs=(P("groups", "gx", Y_AXES), P("groups", "gx", Y_AXES)),
        check_vma=False,
    )
```

```python
import functools

import jax
import jax.numpy as jnp
from jax import lax
from jax.experimental import pallas as pl
from jax.experimental.pallas import tpu as pltpu
from jax.sharding import PartitionSpec as P

Y_AXES = ("gy", "gz")
HI = lax.Precision.HIGHEST


def shift_pairs(count):
    forward = [(i, i + 1) for i in range(count - 1)]
    backward = [(i + 1, i) for i in range(count - 1)]
    return forward, backward


def edges_3d(block):
    return (block[:, -1, :], block[:, 0, :], block[:, :, -1], block[:, :, 0])


def edges_flat(flat, rows, cols):
    return (flat[:, (rows - 1) * cols :], flat[:, :cols], flat[:, cols - 1 :: cols], flat[:, ::cols])


def exchange(edge_sets):
    fwd_x, bwd_x = shift_pairs(lax.axis_size("gx"))
    fwd_y, bwd_y = shift_pairs(lax.axis_size(Y_AXES))
    last_rows = jnp.concatenate([e[0] for e in edge_sets], axis=1)
    first_rows = jnp.concatenate([e[1] for e in edge_sets], axis=1)
    last_cols = jnp.concatenate([e[2] for e in edge_sets], axis=1)
    first_cols = jnp.concatenate([e[3] for e in edge_sets], axis=1)
    above = lax.ppermute(last_rows, "gx", fwd_x)
    below = lax.ppermute(first_rows, "gx", bwd_x)
    left = lax.ppermute(last_cols, Y_AXES, fwd_y)
    right = lax.ppermute(first_cols, Y_AXES, bwd_y)
    out = []
    xo = 0
    yo = 0
    for e in edge_sets:
        out.append(((above, below, left, right), xo, yo))
        xo += e[0].shape[1]
        yo += e[2].shape[1]
    return out


def per_row(values, rows, cols):
    if values.ndim == 1:
        return jnp.broadcast_to(values[:, None], (rows, cols)).reshape(rows * cols)
    return jnp.broadcast_to(values[:, :, None], values.shape + (cols,)).reshape(
        values.shape[0], rows * cols
    )


def flat_stencil(flat, rows, cols, halo, up_w=None, down_w=None):
    above, below, left, right = (h.astype(flat.dtype) for h in halo)
    levels = flat.shape[0]
    up = jnp.concatenate([above, flat[:, :-cols]], axis=1)
    down = jnp.concatenate([flat[:, cols:], below], axis=1)
    col = lax.broadcasted_iota(jnp.int32, (1, rows * cols), 1) % cols
    zero = jnp.zeros((levels, 1), flat.dtype)
    west = jnp.where(col == 0, per_row(left, rows, cols), jnp.concatenate([zero, flat[:, :-1]], axis=1))
    east = jnp.where(
        col == cols - 1, per_row(right, rows, cols), jnp.concatenate([flat[:, 1:], zero], axis=1)
    )
    if down_w is not None:
        down = down * down_w[None, :]
        up = up * up_w[None, :]
    return down + up + east + west - 4.0 * flat


def step_kernel(*refs, rows, cols, xo, nu_k, relax_k, nest):
    if nest:
        (state_ref, above_ref, below_ref, left_ref, right_ref, inj_first_ref, inj_last_ref,
         sel_first_ref, sel_last_ref, coef_ref, vm_ref, forcing_ref, upw_ref, dnw_ref,
         new_ref, lrow_ref, frow_ref, lcol_ref, fcol_ref, up_sc, dn_sc) = refs
    else:
        (state_ref, above_ref, below_ref, left_ref, right_ref, inj_first_ref, inj_last_ref,
         sel_first_ref, sel_last_ref, coef_ref, vm_ref,
         new_ref, lrow_ref, frow_ref, lcol_ref, fcol_ref, up_sc, dn_sc) = refs
    n = rows * cols
    state = state_ref[...].astype(jnp.float32)
    up_sc[:, 0:cols] = above_ref[:, xo : xo + cols].astype(jnp.float32)
    up_sc[:, cols:n] = state[:, 0 : n - cols]
    dn_sc[:, 0 : n - cols] = state[:, cols:n]
    dn_sc[:, n - cols : n] = below_ref[:, xo : xo + cols].astype(jnp.float32)
    up = up_sc[...]
    down = dn_sc[...]
    sel_first = sel_first_ref[...]
    sel_last = sel_last_ref[...]
    at_first = jnp.sum(sel_first.astype(jnp.float32), axis=0, keepdims=True) > 0.5
    at_last = jnp.sum(sel_last.astype(jnp.float32), axis=0, keepdims=True) > 0.5
    left_full = jnp.dot(
        left_ref[...].astype(jnp.bfloat16), inj_first_ref[...], preferred_element_type=jnp.float32
    )
    right_full = jnp.dot(
        right_ref[...].astype(jnp.bfloat16), inj_last_ref[...], preferred_element_type=jnp.float32
    )
    west = jnp.where(at_first, left_full, pltpu.roll(state, 1, 1))
    east = jnp.where(at_last, right_full, pltpu.roll(state, n - 1, 1))
    if nest:
        down = down * dnw_ref[...]
        up = up * upw_ref[...]
    stencil = down + up + east + west - 4.0 * state
    moved = state + coef_ref[:, nu_k : nu_k + 1] * stencil
    if nest:
        moved = moved + coef_ref[:, relax_k : relax_k + 1] * (forcing_ref[...] - moved)
    new = jnp.dot(vm_ref[...], moved, precision=HI, preferred_element_type=jnp.float32)
    new_ref[...] = new
    lrow_ref[...] = new[:, n - cols : n].astype(jnp.bfloat16)
    frow_ref[...] = new[:, 0:cols].astype(jnp.bfloat16)
    narrow = new.astype(jnp.bfloat16)
    pick = (((1,), (1,)), ((), ()))
    lcol_ref[...] = lax.dot_general(
        narrow, sel_last, pick, preferred_element_type=jnp.float32
    ).astype(jnp.bfloat16)
    fcol_ref[...] = lax.dot_general(
        narrow, sel_first, pick, preferred_element_type=jnp.float32
    ).astype(jnp.bfloat16)


def row_onehots(width, offset, rows, cols, zero):
    j = lax.broadcasted_iota(jnp.int32, (width, rows * cols), 0) + zero
    p = lax.broadcasted_iota(jnp.int32, (width, rows * cols), 1)
    inside = (j >= offset) & (j < offset + rows)
    first = inside & (p == (j - offset) * cols)
    last = inside & (p == (j - offset) * cols + (cols - 1))
    return first.astype(jnp.bfloat16), last.astype(jnp.bfloat16)


def stencil_step(state, halo, xo, yo, coefs, nu_k, vert_mix, rows, cols, zero,
                 forcing=None, up_w=None, down_w=None, relax_k=0):
    levels = state.shape[0]
    n = rows * cols
    nest = forcing is not None
    above, below, left, right = halo
    inj_first, inj_last = row_onehots(left.shape[1], yo, rows, cols, zero)
    sel_first, sel_last = row_onehots(rows, 0, rows, cols, zero)
    args = (state, above, below, left, right, inj_first, inj_last, sel_first, sel_last, coefs, vert_mix)
    if nest:
        args = args + (forcing, up_w[None, :], down_w[None, :])
    out_shape = (
        jax.ShapeDtypeStruct((levels, n), jnp.float32),
        jax.ShapeDtypeStruct((levels, cols), jnp.bfloat16),
        jax.ShapeDtypeStruct((levels, cols), jnp.bfloat16),
        jax.ShapeDtypeStruct((levels, rows), jnp.bfloat16),
        jax.ShapeDtypeStruct((levels, rows), jnp.bfloat16),
    )
    flops = 2 * levels * levels * n * 6 + 4 * levels * n * 16 + 20 * levels * n
    moved_bytes = sum(int(a.size) * a.dtype.itemsize for a in args) + levels * n * 4
    new, lrow, frow, lcol, fcol = pl.pallas_call(
        functools.partial(
            step_kernel, rows=rows, cols=cols, xo=xo, nu_k=nu_k, relax_k=relax_k, nest=nest
        ),
        out_shape=out_shape,
        scratch_shapes=[pltpu.VMEM((levels, n), jnp.float32), pltpu.VMEM((levels, n), jnp.float32)],
        cost_estimate=pl.CostEstimate(flops=flops, bytes_accessed=moved_bytes, transcendentals=0),
    )(*args)
    return new, (lrow, frow, lcol, fcol)


def mix_levels(matrix, flat):
    return jnp.dot(matrix, flat, precision=HI, preferred_element_type=jnp.float32)


def nest_segments(nest_of, first, count):
    index_rows = first + jnp.arange(count, dtype=jnp.int32)
    inside = (index_rows >= 0) & (index_rows < nest_of.shape[0])
    return jnp.where(inside, nest_of[jnp.clip(index_rows, 0, nest_of.shape[0] - 1)], -1)


def row_weights(segments):
    left_w = (segments[:-2] == segments[1:-1]).astype(jnp.float32)
    right_w = (segments[2:] == segments[1:-1]).astype(jnp.float32)
    return (left_w, right_w)


def column_expansion(block_cols, cols, zero):
    b = lax.broadcasted_iota(jnp.int32, (block_cols, cols), 0) + zero
    c = lax.broadcasted_iota(jnp.int32, (block_cols, cols), 1)
    return (c // 3 == b).astype(jnp.float32)


def expand_blocks(block_flat, block_rows, block_cols, cols, expand):
    pieces = []
    for a in range(block_rows):
        wide = jnp.dot(
            block_flat[:, a * block_cols : (a + 1) * block_cols],
            expand,
            precision=HI,
            preferred_element_type=jnp.float32,
        )
        pieces += [wide, wide, wide]
    return jnp.concatenate(pieces, axis=1)


def block_sums(flat, block_rows, cols, expand):
    pieces = []
    for a in range(block_rows):
        rows3 = (
            flat[:, (3 * a) * cols : (3 * a + 1) * cols]
            + flat[:, (3 * a + 1) * cols : (3 * a + 2) * cols]
        ) + flat[:, (3 * a + 2) * cols : (3 * a + 3) * cols]
        pieces.append(
            lax.dot_general(
                rows3, expand, (((1,), (1,)), ((), ())), precision=HI,
                preferred_element_type=jnp.float32,
            )
        )
    return jnp.concatenate(pieces, axis=1)


def split3(values):
    hi = lax.reduce_precision(values, exponent_bits=8, mantissa_bits=7)
    rest = values - hi
    mid = lax.reduce_precision(rest, exponent_bits=8, mantissa_bits=7)
    lo = rest - mid
    return hi.astype(jnp.bfloat16), mid.astype(jnp.bfloat16), lo.astype(jnp.bfloat16)


def shifted_pairs(count, shift):
    return [(i, (i + shift) % count) for i in range(count)]


def gather_columns(values, ids):
    levels, width = values.shape
    onehot = (lax.broadcasted_iota(jnp.int32, (width, 1), 0) == ids[None, :]).astype(jnp.bfloat16)
    parts = jnp.concatenate(split3(values), axis=0)
    total = jnp.dot(parts, onehot, preferred_element_type=jnp.float32)
    return (total[:levels] + total[levels : 2 * levels]) + total[2 * levels :]


def scatter_add_columns(values, ids, width):
    levels = values.shape[0]
    onehot = (ids[:, None] == lax.broadcasted_iota(jnp.int32, (1, width), 1)).astype(jnp.bfloat16)
    parts = jnp.concatenate(split3(values), axis=0)
    total = jnp.dot(parts, onehot, preferred_element_type=jnp.float32)
    return (total[:levels] + total[levels : 2 * levels]) + total[2 * levels :]


def body(parent, nest, nu_parent, nu_nest, relax, feedback, vert_mix, fp_owner, fp_cell, nest_of):
    levels, p_rows, p_cols = parent.shape
    _, n_rows, n_cols = nest.shape
    tiles_x = lax.axis_size("gx")
    here_x = lax.axis_index("gx")
    zero = jnp.minimum(here_x, 0)

    parent_halo, nest_halo = exchange([edges_3d(parent), edges_3d(nest)])
    coefs = jnp.stack([nu_parent, nu_nest, relax], axis=1)
    flat_parent, _ = stencil_step(
        parent.reshape(levels, p_rows * p_cols), parent_halo[0], parent_halo[1], parent_halo[2],
        coefs, 0, vert_mix, p_rows, p_cols, zero,
    )

    owners = fp_owner.reshape(-1)
    cells = fp_cell.reshape(-1)
    requests = owners.shape[0]
    slots = 4 * requests // tiles_x
    by_shift = slots >= requests
    if by_shift:
        rel = (owners - here_x + tiles_x) % tiles_x
        chosen = rel[None, :] == jnp.arange(tiles_x, dtype=jnp.int32)[:, None]
        wanted = jnp.where(chosen, cells[None, :], 0)
        served = [wanted[0]] + [
            lax.ppermute(wanted[s], "gx", shifted_pairs(tiles_x, s)) for s in range(1, tiles_x)
        ]
        served_ids = jnp.concatenate(served, axis=0)
        replies = gather_columns(flat_parent, served_ids)
        back = [replies[:, 0:requests]] + [
            lax.ppermute(replies[:, s * requests : (s + 1) * requests], "gx", shifted_pairs(tiles_x, -s))
            for s in range(1, tiles_x)
        ]
        forcing_flat = back[0]
        for s in range(1, tiles_x):
            forcing_flat = jnp.where(chosen[s][None, :], back[s], forcing_flat)
    else:
        owner_ids = jnp.arange(tiles_x, dtype=jnp.int32)
        onehot = (owners[:, None] == owner_ids[None, :]).astype(jnp.int32)
        before = jnp.cumsum(onehot, axis=0) - onehot
        order_in = jnp.sum(before * onehot, axis=1)
        places = owners * slots + order_in
        wanted = jnp.zeros((tiles_x * slots,), jnp.int32).at[places].set(cells)
        served_ids = lax.all_to_all(wanted, "gx", split_axis=0, concat_axis=0, tiled=True)
        answers = lax.all_to_all(
            gather_columns(flat_parent, served_ids), "gx", split_axis=1, concat_axis=1, tiled=True
        )
        forcing_flat = jnp.take(answers, places, axis=1)

    block_rows = n_rows // 3
    block_cols = n_cols // 3
    expand = column_expansion(block_cols, n_cols, zero)
    forcing_full = expand_blocks(forcing_flat, block_rows, block_cols, n_cols, expand)
    row_start = here_x * n_rows
    left_w, right_w = row_weights(nest_segments(nest_of, row_start - 1, n_rows + 2))
    up_w = per_row(left_w, n_rows, n_cols)
    down_w = per_row(right_w, n_rows, n_cols)

    nest_state = nest.reshape(levels, n_rows * n_cols)
    halo = nest_halo
    for turn_no in range(3):
        if turn_no > 0:
            (halo,) = exchange([edges])
        nest_state, edges = stencil_step(
            nest_state, halo[0], halo[1], halo[2], coefs, 1, vert_mix, n_rows, n_cols, zero,
            forcing_full, up_w, down_w, 2,
        )

    block_sum = block_sums(nest_state, block_rows, n_cols, expand)
    nudge_gap = block_sum / 9.0 - forcing_flat
    if by_shift:
        outgoing = jnp.where(chosen[:, None, :], nudge_gap[None, :, :], 0.0)
        incoming = jnp.concatenate(
            [outgoing[0]]
            + [lax.ppermute(outgoing[s], "gx", shifted_pairs(tiles_x, s)) for s in range(1, tiles_x)],
            axis=1,
        )
    else:
        outgoing = jnp.zeros((levels, tiles_x * slots), jnp.float32).at[:, places].set(nudge_gap)
        incoming = lax.all_to_all(outgoing, "gx", split_axis=1, concat_axis=1, tiled=True)
    summed = scatter_add_columns(incoming, served_ids, flat_parent.shape[1])
    parent_out = (flat_parent + feedback[:, None] * summed).astype(jnp.bfloat16)
    return (
        parent_out.reshape(levels, p_rows, p_cols),
        nest_state.astype(jnp.bfloat16).reshape(levels, n_rows, n_cols),
    )


def solution(mesh):
    placed = (
        P("groups", "gx", Y_AXES),
        P("groups", "gx", Y_AXES),
        P(),
        P(),
        P(),
        P(),
        P(),
        P("gx", Y_AXES, None, None),
        P("gx", Y_AXES, None),
        P(),
    )
    return jax.shard_map(
        body,
        mesh=mesh,
        in_specs=placed,
        out_specs=(P("groups", "gx", Y_AXES), P("groups", "gx", Y_AXES)),
        check_vma=False,
    )
```

```python
import functools

import jax
import jax.numpy as jnp
from jax import lax
from jax.experimental import pallas as pl
from jax.experimental.pallas import tpu as pltpu
from jax.sharding import PartitionSpec as P

Y_AXES = ("gy", "gz")
HI = lax.Precision.HIGHEST


def shift_pairs(count):
    forward = [(i, i + 1) for i in range(count - 1)]
    backward = [(i + 1, i) for i in range(count - 1)]
    return forward, backward


def edges_3d(block):
    return (block[:, -1, :], block[:, 0, :], block[:, :, -1], block[:, :, 0])


def edges_flat(flat, rows, cols):
    return (flat[:, (rows - 1) * cols :], flat[:, :cols], flat[:, cols - 1 :: cols], flat[:, ::cols])


def exchange(edge_sets):
    fwd_x, bwd_x = shift_pairs(lax.axis_size("gx"))
    fwd_y, bwd_y = shift_pairs(lax.axis_size(Y_AXES))
    last_rows = jnp.concatenate([e[0] for e in edge_sets], axis=1)
    first_rows = jnp.concatenate([e[1] for e in edge_sets], axis=1)
    last_cols = jnp.concatenate([e[2] for e in edge_sets], axis=1)
    first_cols = jnp.concatenate([e[3] for e in edge_sets], axis=1)
    above = lax.ppermute(last_rows, "gx", fwd_x)
    below = lax.ppermute(first_rows, "gx", bwd_x)
    left = lax.ppermute(last_cols, Y_AXES, fwd_y)
    right = lax.ppermute(first_cols, Y_AXES, bwd_y)
    out = []
    xo = 0
    yo = 0
    for e in edge_sets:
        w, h = e[0].shape[1], e[2].shape[1]
        out.append(
            (above[:, xo : xo + w], below[:, xo : xo + w], left[:, yo : yo + h], right[:, yo : yo + h])
        )
        xo += w
        yo += h
    return out


def per_row(values, rows, cols):
    if values.ndim == 1:
        return jnp.broadcast_to(values[:, None], (rows, cols)).reshape(rows * cols)
    return jnp.broadcast_to(values[:, :, None], values.shape + (cols,)).reshape(
        values.shape[0], rows * cols
    )


def flat_stencil(flat, rows, cols, halo, up_w=None, down_w=None):
    above, below, left, right = (h.astype(flat.dtype) for h in halo)
    levels = flat.shape[0]
    up = jnp.concatenate([above, flat[:, :-cols]], axis=1)
    down = jnp.concatenate([flat[:, cols:], below], axis=1)
    col = lax.broadcasted_iota(jnp.int32, (1, rows * cols), 1) % cols
    zero = jnp.zeros((levels, 1), flat.dtype)
    west = jnp.where(col == 0, per_row(left, rows, cols), jnp.concatenate([zero, flat[:, :-1]], axis=1))
    east = jnp.where(
        col == cols - 1, per_row(right, rows, cols), jnp.concatenate([flat[:, 1:], zero], axis=1)
    )
    if down_w is not None:
        down = down * down_w[None, :]
        up = up * up_w[None, :]
    return down + up + east + west - 4.0 * flat


def step_kernel(*refs, rows, cols, nest):
    if nest:
        (state_ref, above_ref, below_ref, left_ref, right_ref, forcing_ref, upw_ref, dnw_ref,
         nu_ref, relax_ref, vm_ref, new_ref, lrow_ref, frow_ref, lcol_ref, fcol_ref, up_sc, dn_sc) = refs
    else:
        (state_ref, above_ref, below_ref, left_ref, right_ref, nu_ref, vm_ref,
         new_ref, lrow_ref, frow_ref, lcol_ref, fcol_ref, up_sc, dn_sc) = refs
    n = rows * cols
    state = state_ref[...].astype(jnp.float32)
    levels = state.shape[0]
    up_sc[:, 0:cols] = above_ref[...].astype(jnp.float32)
    up_sc[:, cols:n] = state[:, 0 : n - cols]
    dn_sc[:, 0 : n - cols] = state[:, cols:n]
    dn_sc[:, n - cols : n] = below_ref[...].astype(jnp.float32)
    up = up_sc[...]
    down = dn_sc[...]
    lane = lax.broadcasted_iota(jnp.int32, (levels, n), 1)
    left = left_ref[...].astype(jnp.float32)
    right = right_ref[...].astype(jnp.float32)
    west = pltpu.roll(state, 1, 1)
    east = pltpu.roll(state, n - 1, 1)
    for r in range(rows):
        west = jnp.where(lane == r * cols, left[:, r : r + 1], west)
        east = jnp.where(lane == r * cols + cols - 1, right[:, r : r + 1], east)
    if nest:
        down = down * dnw_ref[...]
        up = up * upw_ref[...]
    stencil = down + up + east + west - 4.0 * state
    moved = state + nu_ref[...] * stencil
    if nest:
        moved = moved + relax_ref[...] * (forcing_ref[...] - moved)
    new = jnp.dot(vm_ref[...], moved, precision=lax.Precision.HIGH, preferred_element_type=jnp.float32)
    new_ref[...] = new
    lrow_ref[...] = new[:, n - cols : n].astype(jnp.bfloat16)
    frow_ref[...] = new[:, 0:cols].astype(jnp.bfloat16)
    narrow = new.astype(jnp.bfloat16)
    p = lax.broadcasted_iota(jnp.int32, (n, rows), 0)
    j = lax.broadcasted_iota(jnp.int32, (n, rows), 1)
    last_sel = (p == j * cols + (cols - 1)).astype(jnp.bfloat16)
    first_sel = (p == j * cols).astype(jnp.bfloat16)
    lcol_ref[...] = jnp.dot(narrow, last_sel, preferred_element_type=jnp.float32).astype(jnp.bfloat16)
    fcol_ref[...] = jnp.dot(narrow, first_sel, preferred_element_type=jnp.float32).astype(jnp.bfloat16)


def stencil_step(state, halo, nu, vert_mix, rows, cols, forcing=None, up_w=None, down_w=None, relax=None):
    levels = state.shape[0]
    n = rows * cols
    nest = forcing is not None
    above, below, left, right = halo
    if nest:
        args = (state, above, below, left, right, forcing, up_w[None, :], down_w[None, :],
                nu[:, None], relax[:, None], vert_mix)
    else:
        args = (state, above, below, left, right, nu[:, None], vert_mix)
    out_shape = (
        jax.ShapeDtypeStruct((levels, n), jnp.float32),
        jax.ShapeDtypeStruct((levels, cols), jnp.bfloat16),
        jax.ShapeDtypeStruct((levels, cols), jnp.bfloat16),
        jax.ShapeDtypeStruct((levels, rows), jnp.bfloat16),
        jax.ShapeDtypeStruct((levels, rows), jnp.bfloat16),
    )
    flops = 2 * levels * levels * n * 6 + 4 * levels * n * rows + 20 * levels * n
    moved_bytes = sum(int(a.size) * a.dtype.itemsize for a in args) + levels * n * 4
    new, lrow, frow, lcol, fcol = pl.pallas_call(
        functools.partial(step_kernel, rows=rows, cols=cols, nest=nest),
        out_shape=out_shape,
        scratch_shapes=[pltpu.VMEM((levels, n), jnp.float32), pltpu.VMEM((levels, n), jnp.float32)],
        cost_estimate=pl.CostEstimate(flops=flops, bytes_accessed=moved_bytes, transcendentals=0),
    )(*args)
    return new, (lrow, frow, lcol, fcol)


def mix_levels(matrix, flat):
    return jnp.dot(matrix, flat, precision=HI, preferred_element_type=jnp.float32)


def nest_segments(nest_of, first, count):
    index_rows = first + jnp.arange(count, dtype=jnp.int32)
    inside = (index_rows >= 0) & (index_rows < nest_of.shape[0])
    return jnp.where(inside, nest_of[jnp.clip(index_rows, 0, nest_of.shape[0] - 1)], -1)


def row_weights(segments):
    left_w = (segments[:-2] == segments[1:-1]).astype(jnp.float32)
    right_w = (segments[2:] == segments[1:-1]).astype(jnp.float32)
    return (left_w, right_w)


def column_expansion(block_cols, cols, zero):
    b = lax.broadcasted_iota(jnp.int32, (block_cols, cols), 0) + zero
    c = lax.broadcasted_iota(jnp.int32, (block_cols, cols), 1)
    return (c // 3 == b).astype(jnp.float32)


def expand_blocks(block_flat, block_rows, block_cols, cols, expand):
    pieces = []
    for a in range(block_rows):
        wide = jnp.dot(
            block_flat[:, a * block_cols : (a + 1) * block_cols],
            expand,
            precision=HI,
            preferred_element_type=jnp.float32,
        )
        pieces += [wide, wide, wide]
    return jnp.concatenate(pieces, axis=1)


def block_sums(flat, block_rows, cols, expand):
    pieces = []
    for a in range(block_rows):
        rows3 = (
            flat[:, (3 * a) * cols : (3 * a + 1) * cols]
            + flat[:, (3 * a + 1) * cols : (3 * a + 2) * cols]
        ) + flat[:, (3 * a + 2) * cols : (3 * a + 3) * cols]
        pieces.append(
            lax.dot_general(
                rows3, expand, (((1,), (1,)), ((), ())), precision=HI,
                preferred_element_type=jnp.float32,
            )
        )
    return jnp.concatenate(pieces, axis=1)


def split3(values):
    hi = lax.reduce_precision(values, exponent_bits=8, mantissa_bits=7)
    rest = values - hi
    mid = lax.reduce_precision(rest, exponent_bits=8, mantissa_bits=7)
    lo = rest - mid
    return hi.astype(jnp.bfloat16), mid.astype(jnp.bfloat16), lo.astype(jnp.bfloat16)


def shifted_pairs(count, shift):
    return [(i, (i + shift) % count) for i in range(count)]


def gather_columns(values, ids):
    levels, width = values.shape
    onehot = (lax.broadcasted_iota(jnp.int32, (width, 1), 0) == ids[None, :]).astype(jnp.bfloat16)
    parts = jnp.concatenate(split3(values), axis=0)
    total = jnp.dot(parts, onehot, preferred_element_type=jnp.float32)
    return (total[:levels] + total[levels : 2 * levels]) + total[2 * levels :]


def scatter_add_columns(values, ids, width):
    levels = values.shape[0]
    onehot = (ids[:, None] == lax.broadcasted_iota(jnp.int32, (1, width), 1)).astype(jnp.bfloat16)
    parts = jnp.concatenate(split3(values), axis=0)
    total = jnp.dot(parts, onehot, preferred_element_type=jnp.float32)
    return (total[:levels] + total[levels : 2 * levels]) + total[2 * levels :]


def body(parent, nest, nu_parent, nu_nest, relax, feedback, vert_mix, fp_owner, fp_cell, nest_of):
    levels, p_rows, p_cols = parent.shape
    _, n_rows, n_cols = nest.shape
    tiles_x = lax.axis_size("gx")
    here_x = lax.axis_index("gx")
    zero = jnp.minimum(here_x, 0)

    parent_halo, nest_halo = exchange([edges_3d(parent), edges_3d(nest)])
    flat_parent, _ = stencil_step(
        parent.reshape(levels, p_rows * p_cols), parent_halo, nu_parent, vert_mix, p_rows, p_cols
    )

    owners = fp_owner.reshape(-1)
    cells = fp_cell.reshape(-1)
    requests = owners.shape[0]
    slots = 4 * requests // tiles_x
    by_shift = slots >= requests
    if by_shift:
        rel = (owners - here_x + tiles_x) % tiles_x
        chosen = rel[None, :] == jnp.arange(tiles_x, dtype=jnp.int32)[:, None]
        wanted = jnp.where(chosen, cells[None, :], 0)
        served = [wanted[0]] + [
            lax.ppermute(wanted[s], "gx", shifted_pairs(tiles_x, s)) for s in range(1, tiles_x)
        ]
        served_ids = jnp.concatenate(served, axis=0)
        replies = gather_columns(flat_parent, served_ids)
        back = [replies[:, 0:requests]] + [
            lax.ppermute(replies[:, s * requests : (s + 1) * requests], "gx", shifted_pairs(tiles_x, -s))
            for s in range(1, tiles_x)
        ]
        forcing_flat = back[0]
        for s in range(1, tiles_x):
            forcing_flat = jnp.where(chosen[s][None, :], back[s], forcing_flat)
    else:
        owner_ids = jnp.arange(tiles_x, dtype=jnp.int32)
        onehot = (owners[:, None] == owner_ids[None, :]).astype(jnp.int32)
        before = jnp.cumsum(onehot, axis=0) - onehot
        order_in = jnp.sum(before * onehot, axis=1)
        places = owners * slots + order_in
        wanted = jnp.zeros((tiles_x * slots,), jnp.int32).at[places].set(cells)
        served_ids = lax.all_to_all(wanted, "gx", split_axis=0, concat_axis=0, tiled=True)
        answers = lax.all_to_all(
            gather_columns(flat_parent, served_ids), "gx", split_axis=1, concat_axis=1, tiled=True
        )
        forcing_flat = jnp.take(answers, places, axis=1)

    block_rows = n_rows // 3
    block_cols = n_cols // 3
    expand = column_expansion(block_cols, n_cols, zero)
    forcing_full = expand_blocks(forcing_flat, block_rows, block_cols, n_cols, expand)
    row_start = here_x * n_rows
    left_w, right_w = row_weights(nest_segments(nest_of, row_start - 1, n_rows + 2))
    up_w = per_row(left_w, n_rows, n_cols)
    down_w = per_row(right_w, n_rows, n_cols)

    nest_state = nest.reshape(levels, n_rows * n_cols)
    halo = nest_halo
    for turn_no in range(3):
        if turn_no > 0:
            (halo,) = exchange([edges])
        nest_state, edges = stencil_step(
            nest_state, halo, nu_nest, vert_mix, n_rows, n_cols, forcing_full, up_w, down_w, relax
        )

    block_sum = block_sums(nest_state, block_rows, n_cols, expand)
    nudge_gap = block_sum / 9.0 - forcing_flat
    if by_shift:
        outgoing = jnp.where(chosen[:, None, :], nudge_gap[None, :, :], 0.0)
        incoming = jnp.concatenate(
            [outgoing[0]]
            + [lax.ppermute(outgoing[s], "gx", shifted_pairs(tiles_x, s)) for s in range(1, tiles_x)],
            axis=1,
        )
    else:
        outgoing = jnp.zeros((levels, tiles_x * slots), jnp.float32).at[:, places].set(nudge_gap)
        incoming = lax.all_to_all(outgoing, "gx", split_axis=1, concat_axis=1, tiled=True)
    summed = scatter_add_columns(incoming, served_ids, flat_parent.shape[1])
    parent_out = (flat_parent + feedback[:, None] * summed).astype(jnp.bfloat16)
    return (
        parent_out.reshape(levels, p_rows, p_cols),
        nest_state.astype(jnp.bfloat16).reshape(levels, n_rows, n_cols),
    )


def solution(mesh):
    placed = (
        P("groups", "gx", Y_AXES),
        P("groups", "gx", Y_AXES),
        P(),
        P(),
        P(),
        P(),
        P(),
        P("gx", Y_AXES, None, None),
        P("gx", Y_AXES, None),
        P(),
    )
    return jax.shard_map(
        body,
        mesh=mesh,
        in_specs=placed,
        out_specs=(P("groups", "gx", Y_AXES), P("groups", "gx", Y_AXES)),
        check_vma=False,
    )
```

```python
import functools

import jax
import jax.numpy as jnp
from jax import lax
from jax.experimental import pallas as pl
from jax.experimental.pallas import tpu as pltpu
from jax.sharding import PartitionSpec as P

Y_AXES = ("gy", "gz")
HI = lax.Precision.HIGHEST


def shift_pairs(count):
    forward = [(i, i + 1) for i in range(count - 1)]
    backward = [(i + 1, i) for i in range(count - 1)]
    return forward, backward


def edges_3d(block):
    return (block[:, -1, :], block[:, 0, :], block[:, :, -1], block[:, :, 0])


def edges_flat(flat, rows, cols):
    return (flat[:, (rows - 1) * cols :], flat[:, :cols], flat[:, cols - 1 :: cols], flat[:, ::cols])


def exchange(edge_sets):
    fwd_x, bwd_x = shift_pairs(lax.axis_size("gx"))
    fwd_y, bwd_y = shift_pairs(lax.axis_size(Y_AXES))
    last_rows = jnp.concatenate([e[0] for e in edge_sets], axis=1)
    first_rows = jnp.concatenate([e[1] for e in edge_sets], axis=1)
    last_cols = jnp.concatenate([e[2] for e in edge_sets], axis=1)
    first_cols = jnp.concatenate([e[3] for e in edge_sets], axis=1)
    above = lax.ppermute(last_rows, "gx", fwd_x)
    below = lax.ppermute(first_rows, "gx", bwd_x)
    left = lax.ppermute(last_cols, Y_AXES, fwd_y)
    right = lax.ppermute(first_cols, Y_AXES, bwd_y)
    out = []
    xo = 0
    yo = 0
    for e in edge_sets:
        w, h = e[0].shape[1], e[2].shape[1]
        out.append(
            (above[:, xo : xo + w], below[:, xo : xo + w], left[:, yo : yo + h], right[:, yo : yo + h])
        )
        xo += w
        yo += h
    return out


def per_row(values, rows, cols):
    if values.ndim == 1:
        return jnp.broadcast_to(values[:, None], (rows, cols)).reshape(rows * cols)
    return jnp.broadcast_to(values[:, :, None], values.shape + (cols,)).reshape(
        values.shape[0], rows * cols
    )


def flat_stencil(flat, rows, cols, halo, up_w=None, down_w=None):
    above, below, left, right = (h.astype(flat.dtype) for h in halo)
    levels = flat.shape[0]
    up = jnp.concatenate([above, flat[:, :-cols]], axis=1)
    down = jnp.concatenate([flat[:, cols:], below], axis=1)
    col = lax.broadcasted_iota(jnp.int32, (1, rows * cols), 1) % cols
    zero = jnp.zeros((levels, 1), flat.dtype)
    west = jnp.where(col == 0, per_row(left, rows, cols), jnp.concatenate([zero, flat[:, :-1]], axis=1))
    east = jnp.where(
        col == cols - 1, per_row(right, rows, cols), jnp.concatenate([flat[:, 1:], zero], axis=1)
    )
    if down_w is not None:
        down = down * down_w[None, :]
        up = up * up_w[None, :]
    return down + up + east + west - 4.0 * flat


def step_kernel(*refs, rows, cols, nest, split, gap):
    refs = list(refs)
    if gap:
        expand_ref, fblock_ref = refs[:2]
        refs = refs[2:]
    if nest:
        (state_ref, above_ref, below_ref, left_ref, right_ref, forcing_ref, upw_ref, dnw_ref,
         nu_ref, relax_ref, vm_ref, new_ref, lrow_ref, frow_ref, lcol_ref, fcol_ref) = refs[:16]
        refs = refs[16:]
    else:
        (state_ref, above_ref, below_ref, left_ref, right_ref, nu_ref, vm_ref,
         new_ref, lrow_ref, frow_ref, lcol_ref, fcol_ref) = refs[:12]
        refs = refs[12:]
    if split:
        parts_ref = refs[0]
        refs = refs[1:]
    if gap:
        gap_ref = refs[0]
        refs = refs[1:]
    up_sc, dn_sc = refs
    n = rows * cols
    state = state_ref[...].astype(jnp.float32)
    levels = state.shape[0]
    up_sc[:, 0:cols] = above_ref[...].astype(jnp.float32)
    up_sc[:, cols:n] = state[:, 0 : n - cols]
    dn_sc[:, 0 : n - cols] = state[:, cols:n]
    dn_sc[:, n - cols : n] = below_ref[...].astype(jnp.float32)
    up = up_sc[...]
    down = dn_sc[...]
    lane = lax.broadcasted_iota(jnp.int32, (levels, n), 1)
    left = left_ref[...].astype(jnp.float32)
    right = right_ref[...].astype(jnp.float32)
    west = pltpu.roll(state, 1, 1)
    east = pltpu.roll(state, n - 1, 1)
    for r in range(rows):
        west = jnp.where(lane == r * cols, left[:, r : r + 1], west)
        east = jnp.where(lane == r * cols + cols - 1, right[:, r : r + 1], east)
    if nest:
        down = down * dnw_ref[...]
        up = up * upw_ref[...]
    stencil = down + up + east + west - 4.0 * state
    moved = state + nu_ref[...] * stencil
    if nest:
        moved = moved + relax_ref[...] * (forcing_ref[...] - moved)
    new = jnp.dot(vm_ref[...], moved, precision=lax.Precision.HIGH, preferred_element_type=jnp.float32)
    new_ref[...] = new
    lrow_ref[...] = new[:, n - cols : n].astype(jnp.bfloat16)
    frow_ref[...] = new[:, 0:cols].astype(jnp.bfloat16)
    narrow = new.astype(jnp.bfloat16)
    p = lax.broadcasted_iota(jnp.int32, (n, rows), 0)
    j = lax.broadcasted_iota(jnp.int32, (n, rows), 1)
    last_sel = (p == j * cols + (cols - 1)).astype(jnp.bfloat16)
    first_sel = (p == j * cols).astype(jnp.bfloat16)
    lcol_ref[...] = jnp.dot(narrow, last_sel, preferred_element_type=jnp.float32).astype(jnp.bfloat16)
    fcol_ref[...] = jnp.dot(narrow, first_sel, preferred_element_type=jnp.float32).astype(jnp.bfloat16)
    if split:
        hi = new.astype(jnp.bfloat16)
        rest = new - hi.astype(jnp.float32)
        mid = rest.astype(jnp.bfloat16)
        lo = (rest - mid.astype(jnp.float32)).astype(jnp.bfloat16)
        parts_ref[0:levels, :] = hi
        parts_ref[levels : 2 * levels, :] = mid
        parts_ref[2 * levels : 3 * levels, :] = lo
    if gap:
        expand = expand_ref[...]
        block_cols = expand.shape[0]
        pick = (((1,), (1,)), ((), ()))
        for a in range(rows // 3):
            rows3 = (
                new[:, (3 * a) * cols : (3 * a + 1) * cols]
                + new[:, (3 * a + 1) * cols : (3 * a + 2) * cols]
            ) + new[:, (3 * a + 2) * cols : (3 * a + 3) * cols]
            sums = lax.dot_general(rows3, expand, pick, precision=HI, preferred_element_type=jnp.float32)
            gap_ref[:, a * block_cols : (a + 1) * block_cols] = (
                sums / 9.0 - fblock_ref[:, a * block_cols : (a + 1) * block_cols]
            )


def stencil_step(state, halo, nu, vert_mix, rows, cols, forcing=None, up_w=None, down_w=None, relax=None,
                 split=False, gap_of=None):
    levels = state.shape[0]
    n = rows * cols
    nest = forcing is not None
    above, below, left, right = halo
    if nest:
        args = (state, above, below, left, right, forcing, up_w[None, :], down_w[None, :],
                nu[:, None], relax[:, None], vert_mix)
    else:
        args = (state, above, below, left, right, nu[:, None], vert_mix)
    out_shape = (
        jax.ShapeDtypeStruct((levels, n), jnp.float32),
        jax.ShapeDtypeStruct((levels, cols), jnp.bfloat16),
        jax.ShapeDtypeStruct((levels, cols), jnp.bfloat16),
        jax.ShapeDtypeStruct((levels, rows), jnp.bfloat16),
        jax.ShapeDtypeStruct((levels, rows), jnp.bfloat16),
    )
    gap = gap_of is not None
    if split:
        out_shape = out_shape + (jax.ShapeDtypeStruct((3 * levels, n), jnp.bfloat16),)
    if gap:
        args = tuple(gap_of) + args
        out_shape = out_shape + (jax.ShapeDtypeStruct(gap_of[1].shape, jnp.float32),)
    flops = 2 * levels * levels * n * 6 + 4 * levels * n * rows + 20 * levels * n
    moved_bytes = sum(int(a.size) * a.dtype.itemsize for a in args) + levels * n * 4
    outs = pl.pallas_call(
        functools.partial(step_kernel, rows=rows, cols=cols, nest=nest, split=split, gap=gap),
        out_shape=out_shape,
        scratch_shapes=[pltpu.VMEM((levels, n), jnp.float32), pltpu.VMEM((levels, n), jnp.float32)],
        cost_estimate=pl.CostEstimate(flops=flops, bytes_accessed=moved_bytes, transcendentals=0),
    )(*args)
    return outs[0], tuple(outs[1:5]), outs[5:]


def mix_levels(matrix, flat):
    return jnp.dot(matrix, flat, precision=HI, preferred_element_type=jnp.float32)


def nest_segments(nest_of, first, count):
    index_rows = first + jnp.arange(count, dtype=jnp.int32)
    inside = (index_rows >= 0) & (index_rows < nest_of.shape[0])
    return jnp.where(inside, nest_of[jnp.clip(index_rows, 0, nest_of.shape[0] - 1)], -1)


def row_weights(segments):
    left_w = (segments[:-2] == segments[1:-1]).astype(jnp.float32)
    right_w = (segments[2:] == segments[1:-1]).astype(jnp.float32)
    return (left_w, right_w)


def column_expansion(block_cols, cols, zero):
    b = lax.broadcasted_iota(jnp.int32, (block_cols, cols), 0) + zero
    c = lax.broadcasted_iota(jnp.int32, (block_cols, cols), 1)
    return (c // 3 == b).astype(jnp.float32)


def expand_blocks(block_flat, block_rows, block_cols, cols, expand):
    pieces = []
    for a in range(block_rows):
        wide = jnp.dot(
            block_flat[:, a * block_cols : (a + 1) * block_cols],
            expand,
            precision=HI,
            preferred_element_type=jnp.float32,
        )
        pieces += [wide, wide, wide]
    return jnp.concatenate(pieces, axis=1)


def block_sums(flat, block_rows, cols, expand):
    pieces = []
    for a in range(block_rows):
        rows3 = (
            flat[:, (3 * a) * cols : (3 * a + 1) * cols]
            + flat[:, (3 * a + 1) * cols : (3 * a + 2) * cols]
        ) + flat[:, (3 * a + 2) * cols : (3 * a + 3) * cols]
        pieces.append(
            lax.dot_general(
                rows3, expand, (((1,), (1,)), ((), ())), precision=HI,
                preferred_element_type=jnp.float32,
            )
        )
    return jnp.concatenate(pieces, axis=1)


def split3(values):
    hi = lax.reduce_precision(values, exponent_bits=8, mantissa_bits=7)
    rest = values - hi
    mid = lax.reduce_precision(rest, exponent_bits=8, mantissa_bits=7)
    lo = rest - mid
    return hi.astype(jnp.bfloat16), mid.astype(jnp.bfloat16), lo.astype(jnp.bfloat16)


def shifted_pairs(count, shift):
    return [(i, (i + shift) % count) for i in range(count)]


def gather_columns(values, ids):
    levels, width = values.shape
    onehot = (lax.broadcasted_iota(jnp.int32, (width, 1), 0) == ids[None, :]).astype(jnp.bfloat16)
    parts = jnp.concatenate(split3(values), axis=0)
    total = jnp.dot(parts, onehot, preferred_element_type=jnp.float32)
    return (total[:levels] + total[levels : 2 * levels]) + total[2 * levels :]


def gather_parts(parts, ids):
    levels = parts.shape[0] // 3
    width = parts.shape[1]
    onehot = (lax.broadcasted_iota(jnp.int32, (width, 1), 0) == ids[None, :]).astype(jnp.bfloat16)
    total = jnp.dot(parts, onehot, preferred_element_type=jnp.float32)
    return (total[:levels] + total[levels : 2 * levels]) + total[2 * levels :]


def scatter_add_columns(values, ids, width):
    levels = values.shape[0]
    onehot = (ids[:, None] == lax.broadcasted_iota(jnp.int32, (1, width), 1)).astype(jnp.bfloat16)
    parts = jnp.concatenate(split3(values), axis=0)
    total = jnp.dot(parts, onehot, preferred_element_type=jnp.float32)
    return (total[:levels] + total[levels : 2 * levels]) + total[2 * levels :]


def body(parent, nest, nu_parent, nu_nest, relax, feedback, vert_mix, fp_owner, fp_cell, nest_of):
    levels, p_rows, p_cols = parent.shape
    _, n_rows, n_cols = nest.shape
    tiles_x = lax.axis_size("gx")
    here_x = lax.axis_index("gx")
    zero = jnp.minimum(here_x, 0)

    parent_halo, nest_halo = exchange([edges_3d(parent), edges_3d(nest)])
    flat_parent, _, (parent_parts,) = stencil_step(
        parent.reshape(levels, p_rows * p_cols), parent_halo, nu_parent, vert_mix, p_rows, p_cols,
        split=True,
    )

    owners = fp_owner.reshape(-1)
    cells = fp_cell.reshape(-1)
    requests = owners.shape[0]
    slots = 4 * requests // tiles_x
    by_shift = slots >= requests
    if by_shift:
        rel = (owners - here_x + tiles_x) % tiles_x
        chosen = rel[None, :] == jnp.arange(tiles_x, dtype=jnp.int32)[:, None]
        wanted = jnp.where(chosen, cells[None, :], 0)
        served = [wanted[0]] + [
            lax.ppermute(wanted[s], "gx", shifted_pairs(tiles_x, s)) for s in range(1, tiles_x)
        ]
        served_ids = jnp.concatenate(served, axis=0)
        replies = gather_parts(parent_parts, served_ids)
        back = [replies[:, 0:requests]] + [
            lax.ppermute(replies[:, s * requests : (s + 1) * requests], "gx", shifted_pairs(tiles_x, -s))
            for s in range(1, tiles_x)
        ]
        forcing_flat = back[0]
        for s in range(1, tiles_x):
            forcing_flat = jnp.where(chosen[s][None, :], back[s], forcing_flat)
    else:
        owner_ids = jnp.arange(tiles_x, dtype=jnp.int32)
        onehot = (owners[:, None] == owner_ids[None, :]).astype(jnp.int32)
        before = jnp.cumsum(onehot, axis=0) - onehot
        order_in = jnp.sum(before * onehot, axis=1)
        places = owners * slots + order_in
        wanted = jnp.zeros((tiles_x * slots,), jnp.int32).at[places].set(cells)
        served_ids = lax.all_to_all(wanted, "gx", split_axis=0, concat_axis=0, tiled=True)
        answers = lax.all_to_all(
            gather_parts(parent_parts, served_ids), "gx", split_axis=1, concat_axis=1, tiled=True
        )
        forcing_flat = jnp.take(answers, places, axis=1)

    block_rows = n_rows // 3
    block_cols = n_cols // 3
    expand = column_expansion(block_cols, n_cols, zero)
    forcing_full = expand_blocks(forcing_flat, block_rows, block_cols, n_cols, expand)
    row_start = here_x * n_rows
    left_w, right_w = row_weights(nest_segments(nest_of, row_start - 1, n_rows + 2))
    up_w = per_row(left_w, n_rows, n_cols)
    down_w = per_row(right_w, n_rows, n_cols)

    nest_state = nest.reshape(levels, n_rows * n_cols)
    halo = nest_halo
    for turn_no in range(3):
        if turn_no > 0:
            (halo,) = exchange([edges])
        nest_state, edges, extra = stencil_step(
            nest_state, halo, nu_nest, vert_mix, n_rows, n_cols, forcing_full, up_w, down_w, relax,
            gap_of=(expand, forcing_flat) if turn_no == 2 else None,
        )
    (nudge_gap,) = extra
    if by_shift:
        outgoing = jnp.where(chosen[:, None, :], nudge_gap[None, :, :], 0.0)
        incoming = jnp.concatenate(
            [outgoing[0]]
            + [lax.ppermute(outgoing[s], "gx", shifted_pairs(tiles_x, s)) for s in range(1, tiles_x)],
            axis=1,
        )
    else:
        outgoing = jnp.zeros((levels, tiles_x * slots), jnp.float32).at[:, places].set(nudge_gap)
        incoming = lax.all_to_all(outgoing, "gx", split_axis=1, concat_axis=1, tiled=True)
    summed = scatter_add_columns(incoming, served_ids, flat_parent.shape[1])
    parent_out = (flat_parent + feedback[:, None] * summed).astype(jnp.bfloat16)
    return (
        parent_out.reshape(levels, p_rows, p_cols),
        nest_state.astype(jnp.bfloat16).reshape(levels, n_rows, n_cols),
    )


def solution(mesh):
    placed = (
        P("groups", "gx", Y_AXES),
        P("groups", "gx", Y_AXES),
        P(),
        P(),
        P(),
        P(),
        P(),
        P("gx", Y_AXES, None, None),
        P("gx", Y_AXES, None),
        P(),
    )
    return jax.shard_map(
        body,
        mesh=mesh,
        in_specs=placed,
        out_specs=(P("groups", "gx", Y_AXES), P("groups", "gx", Y_AXES)),
        check_vma=False,
    )
```

```python
import functools

import jax
import jax.numpy as jnp
from jax import lax
from jax.experimental import pallas as pl
from jax.experimental.pallas import tpu as pltpu
from jax.sharding import PartitionSpec as P

Y_AXES = ("gy", "gz")
HI = lax.Precision.HIGHEST


def shift_pairs(count):
    forward = [(i, i + 1) for i in range(count - 1)]
    backward = [(i + 1, i) for i in range(count - 1)]
    return forward, backward


def edges_3d(block):
    return (block[:, -1, :], block[:, 0, :], block[:, :, -1], block[:, :, 0])


def edges_flat(flat, rows, cols):
    return (flat[:, (rows - 1) * cols :], flat[:, :cols], flat[:, cols - 1 :: cols], flat[:, ::cols])


def exchange(edge_sets):
    fwd_x, bwd_x = shift_pairs(lax.axis_size("gx"))
    fwd_y, bwd_y = shift_pairs(lax.axis_size(Y_AXES))
    last_rows = jnp.concatenate([e[0] for e in edge_sets], axis=1)
    first_rows = jnp.concatenate([e[1] for e in edge_sets], axis=1)
    last_cols = jnp.concatenate([e[2] for e in edge_sets], axis=1)
    first_cols = jnp.concatenate([e[3] for e in edge_sets], axis=1)
    above = lax.ppermute(last_rows, "gx", fwd_x)
    below = lax.ppermute(first_rows, "gx", bwd_x)
    left = lax.ppermute(last_cols, Y_AXES, fwd_y)
    right = lax.ppermute(first_cols, Y_AXES, bwd_y)
    out = []
    xo = 0
    yo = 0
    for e in edge_sets:
        out.append(((above, below, left, right), xo, yo))
        xo += e[0].shape[1]
        yo += e[2].shape[1]
    return out


def per_row(values, rows, cols):
    if values.ndim == 1:
        return jnp.broadcast_to(values[:, None], (rows, cols)).reshape(rows * cols)
    return jnp.broadcast_to(values[:, :, None], values.shape + (cols,)).reshape(
        values.shape[0], rows * cols
    )


def flat_stencil(flat, rows, cols, halo, up_w=None, down_w=None):
    above, below, left, right = (h.astype(flat.dtype) for h in halo)
    levels = flat.shape[0]
    up = jnp.concatenate([above, flat[:, :-cols]], axis=1)
    down = jnp.concatenate([flat[:, cols:], below], axis=1)
    col = lax.broadcasted_iota(jnp.int32, (1, rows * cols), 1) % cols
    zero = jnp.zeros((levels, 1), flat.dtype)
    west = jnp.where(col == 0, per_row(left, rows, cols), jnp.concatenate([zero, flat[:, :-1]], axis=1))
    east = jnp.where(
        col == cols - 1, per_row(right, rows, cols), jnp.concatenate([flat[:, 1:], zero], axis=1)
    )
    if down_w is not None:
        down = down * down_w[None, :]
        up = up * up_w[None, :]
    return down + up + east + west - 4.0 * flat


def step_kernel(*refs, rows, cols, xo, yo, nest, split, gap):
    refs = list(refs)
    if gap:
        expand_ref, fblock_ref = refs[:2]
        refs = refs[2:]
    if nest:
        (state_ref, above_ref, below_ref, left_ref, right_ref, forcing_ref, upw_ref, dnw_ref,
         nu_ref, relax_ref, vm_ref, new_ref, lrow_ref, frow_ref, lcol_ref, fcol_ref) = refs[:16]
        refs = refs[16:]
    else:
        (state_ref, above_ref, below_ref, left_ref, right_ref, nu_ref, vm_ref,
         new_ref, lrow_ref, frow_ref, lcol_ref, fcol_ref) = refs[:12]
        refs = refs[12:]
    if split:
        parts_ref = refs[0]
        refs = refs[1:]
    if gap:
        gap_ref = refs[0]
        refs = refs[1:]
    up_sc, dn_sc = refs
    n = rows * cols
    state = state_ref[...].astype(jnp.float32)
    levels = state.shape[0]
    up_sc[:, 0:cols] = above_ref[:, xo : xo + cols].astype(jnp.float32)
    up_sc[:, cols:n] = state[:, 0 : n - cols]
    dn_sc[:, 0 : n - cols] = state[:, cols:n]
    dn_sc[:, n - cols : n] = below_ref[:, xo : xo + cols].astype(jnp.float32)
    up = up_sc[...]
    down = dn_sc[...]
    lane = lax.broadcasted_iota(jnp.int32, (levels, n), 1)
    left = left_ref[...].astype(jnp.float32)
    right = right_ref[...].astype(jnp.float32)
    west = pltpu.roll(state, 1, 1)
    east = pltpu.roll(state, n - 1, 1)
    for r in range(rows):
        west = jnp.where(lane == r * cols, left[:, yo + r : yo + r + 1], west)
        east = jnp.where(lane == r * cols + cols - 1, right[:, yo + r : yo + r + 1], east)
    if nest:
        down = down * dnw_ref[...]
        up = up * upw_ref[...]
    stencil = down + up + east + west - 4.0 * state
    moved = state + nu_ref[...] * stencil
    if nest:
        moved = moved + relax_ref[...] * (forcing_ref[...] - moved)
    new = jnp.dot(vm_ref[...], moved, precision=lax.Precision.HIGH, preferred_element_type=jnp.float32)
    new_ref[...] = new
    lrow_ref[...] = new[:, n - cols : n].astype(jnp.bfloat16)
    frow_ref[...] = new[:, 0:cols].astype(jnp.bfloat16)
    narrow = new.astype(jnp.bfloat16)
    p = lax.broadcasted_iota(jnp.int32, (n, rows), 0)
    j = lax.broadcasted_iota(jnp.int32, (n, rows), 1)
    last_sel = (p == j * cols + (cols - 1)).astype(jnp.bfloat16)
    first_sel = (p == j * cols).astype(jnp.bfloat16)
    lcol_ref[...] = jnp.dot(narrow, last_sel, preferred_element_type=jnp.float32).astype(jnp.bfloat16)
    fcol_ref[...] = jnp.dot(narrow, first_sel, preferred_element_type=jnp.float32).astype(jnp.bfloat16)
    if split:
        hi = new.astype(jnp.bfloat16)
        rest = new - hi.astype(jnp.float32)
        mid = rest.astype(jnp.bfloat16)
        lo = (rest - mid.astype(jnp.float32)).astype(jnp.bfloat16)
        parts_ref[0:levels, :] = hi
        parts_ref[levels : 2 * levels, :] = mid
        parts_ref[2 * levels : 3 * levels, :] = lo
    if gap:
        expand = expand_ref[...]
        block_cols = expand.shape[0]
        pick = (((1,), (1,)), ((), ()))
        for a in range(rows // 3):
            rows3 = (
                new[:, (3 * a) * cols : (3 * a + 1) * cols]
                + new[:, (3 * a + 1) * cols : (3 * a + 2) * cols]
            ) + new[:, (3 * a + 2) * cols : (3 * a + 3) * cols]
            sums = lax.dot_general(rows3, expand, pick, precision=HI, preferred_element_type=jnp.float32)
            gap_ref[:, a * block_cols : (a + 1) * block_cols] = (
                sums / 9.0 - fblock_ref[:, a * block_cols : (a + 1) * block_cols]
            )


def stencil_step(state, placed_halo, nu, vert_mix, rows, cols, forcing=None, up_w=None, down_w=None,
                 relax=None, split=False, gap_of=None):
    levels = state.shape[0]
    n = rows * cols
    nest = forcing is not None
    (above, below, left, right), xo, yo = placed_halo
    if nest:
        args = (state, above, below, left, right, forcing, up_w[None, :], down_w[None, :],
                nu[:, None], relax[:, None], vert_mix)
    else:
        args = (state, above, below, left, right, nu[:, None], vert_mix)
    out_shape = (
        jax.ShapeDtypeStruct((levels, n), jnp.float32),
        jax.ShapeDtypeStruct((levels, cols), jnp.bfloat16),
        jax.ShapeDtypeStruct((levels, cols), jnp.bfloat16),
        jax.ShapeDtypeStruct((levels, rows), jnp.bfloat16),
        jax.ShapeDtypeStruct((levels, rows), jnp.bfloat16),
    )
    gap = gap_of is not None
    if split:
        out_shape = out_shape + (jax.ShapeDtypeStruct((3 * levels, n), jnp.bfloat16),)
    if gap:
        args = tuple(gap_of) + args
        out_shape = out_shape + (jax.ShapeDtypeStruct(gap_of[1].shape, jnp.float32),)
    flops = 2 * levels * levels * n * 6 + 4 * levels * n * rows + 20 * levels * n
    moved_bytes = sum(int(a.size) * a.dtype.itemsize for a in args) + levels * n * 4
    outs = pl.pallas_call(
        functools.partial(
            step_kernel, rows=rows, cols=cols, xo=xo, yo=yo, nest=nest, split=split, gap=gap
        ),
        out_shape=out_shape,
        scratch_shapes=[pltpu.VMEM((levels, n), jnp.float32), pltpu.VMEM((levels, n), jnp.float32)],
        cost_estimate=pl.CostEstimate(flops=flops, bytes_accessed=moved_bytes, transcendentals=0),
    )(*args)
    return outs[0], tuple(outs[1:5]), outs[5:]


def mix_levels(matrix, flat):
    return jnp.dot(matrix, flat, precision=HI, preferred_element_type=jnp.float32)


def nest_segments(nest_of, first, count):
    index_rows = first + jnp.arange(count, dtype=jnp.int32)
    inside = (index_rows >= 0) & (index_rows < nest_of.shape[0])
    return jnp.where(inside, nest_of[jnp.clip(index_rows, 0, nest_of.shape[0] - 1)], -1)


def row_weights(segments):
    left_w = (segments[:-2] == segments[1:-1]).astype(jnp.float32)
    right_w = (segments[2:] == segments[1:-1]).astype(jnp.float32)
    return (left_w, right_w)


def column_expansion(block_cols, cols, zero):
    b = lax.broadcasted_iota(jnp.int32, (block_cols, cols), 0) + zero
    c = lax.broadcasted_iota(jnp.int32, (block_cols, cols), 1)
    return (c // 3 == b).astype(jnp.float32)


def expand_blocks(block_flat, block_rows, block_cols, cols, expand):
    pieces = []
    for a in range(block_rows):
        wide = jnp.dot(
            block_flat[:, a * block_cols : (a + 1) * block_cols],
            expand,
            precision=HI,
            preferred_element_type=jnp.float32,
        )
        pieces += [wide, wide, wide]
    return jnp.concatenate(pieces, axis=1)


def block_sums(flat, block_rows, cols, expand):
    pieces = []
    for a in range(block_rows):
        rows3 = (
            flat[:, (3 * a) * cols : (3 * a + 1) * cols]
            + flat[:, (3 * a + 1) * cols : (3 * a + 2) * cols]
        ) + flat[:, (3 * a + 2) * cols : (3 * a + 3) * cols]
        pieces.append(
            lax.dot_general(
                rows3, expand, (((1,), (1,)), ((), ())), precision=HI,
                preferred_element_type=jnp.float32,
            )
        )
    return jnp.concatenate(pieces, axis=1)


def split3(values):
    hi = lax.reduce_precision(values, exponent_bits=8, mantissa_bits=7)
    rest = values - hi
    mid = lax.reduce_precision(rest, exponent_bits=8, mantissa_bits=7)
    lo = rest - mid
    return hi.astype(jnp.bfloat16), mid.astype(jnp.bfloat16), lo.astype(jnp.bfloat16)


def shifted_pairs(count, shift):
    return [(i, (i + shift) % count) for i in range(count)]


def gather_columns(values, ids):
    levels, width = values.shape
    onehot = (lax.broadcasted_iota(jnp.int32, (width, 1), 0) == ids[None, :]).astype(jnp.bfloat16)
    parts = jnp.concatenate(split3(values), axis=0)
    total = jnp.dot(parts, onehot, preferred_element_type=jnp.float32)
    return (total[:levels] + total[levels : 2 * levels]) + total[2 * levels :]


def gather_parts(parts, ids):
    levels = parts.shape[0] // 3
    width = parts.shape[1]
    onehot = (lax.broadcasted_iota(jnp.int32, (width, 1), 0) == ids[None, :]).astype(jnp.bfloat16)
    total = jnp.dot(parts, onehot, preferred_element_type=jnp.float32)
    return (total[:levels] + total[levels : 2 * levels]) + total[2 * levels :]


def scatter_add_columns(values, ids, width):
    levels = values.shape[0]
    onehot = (ids[:, None] == lax.broadcasted_iota(jnp.int32, (1, width), 1)).astype(jnp.bfloat16)
    parts = jnp.concatenate(split3(values), axis=0)
    total = jnp.dot(parts, onehot, preferred_element_type=jnp.float32)
    return (total[:levels] + total[levels : 2 * levels]) + total[2 * levels :]


def body(parent, nest, nu_parent, nu_nest, relax, feedback, vert_mix, fp_owner, fp_cell, nest_of):
    levels, p_rows, p_cols = parent.shape
    _, n_rows, n_cols = nest.shape
    tiles_x = lax.axis_size("gx")
    here_x = lax.axis_index("gx")
    zero = jnp.minimum(here_x, 0)

    parent_halo, nest_halo = exchange([edges_3d(parent), edges_3d(nest)])
    flat_parent, _, (parent_parts,) = stencil_step(
        parent.reshape(levels, p_rows * p_cols), parent_halo, nu_parent, vert_mix, p_rows, p_cols,
        split=True,
    )

    owners = fp_owner.reshape(-1)
    cells = fp_cell.reshape(-1)
    requests = owners.shape[0]
    slots = 4 * requests // tiles_x
    by_shift = slots >= requests
    if by_shift:
        rel = (owners - here_x + tiles_x) % tiles_x
        chosen = rel[None, :] == jnp.arange(tiles_x, dtype=jnp.int32)[:, None]
        wanted = jnp.where(chosen, cells[None, :], 0)
        served = [wanted[0]] + [
            lax.ppermute(wanted[s], "gx", shifted_pairs(tiles_x, s)) for s in range(1, tiles_x)
        ]
        served_ids = jnp.concatenate(served, axis=0)
        back = [None] + [
            lax.ppermute(gather_parts(parent_parts, served[s]), "gx", shifted_pairs(tiles_x, -s))
            for s in range(1, tiles_x)
        ]
        back[0] = gather_parts(parent_parts, served[0])
        forcing_flat = back[0]
        for s in range(1, tiles_x):
            forcing_flat = jnp.where(chosen[s][None, :], back[s], forcing_flat)
    else:
        owner_ids = jnp.arange(tiles_x, dtype=jnp.int32)
        onehot = (owners[:, None] == owner_ids[None, :]).astype(jnp.int32)
        before = jnp.cumsum(onehot, axis=0) - onehot
        order_in = jnp.sum(before * onehot, axis=1)
        places = owners * slots + order_in
        wanted = jnp.zeros((tiles_x * slots,), jnp.int32).at[places].set(cells)
        served_ids = lax.all_to_all(wanted, "gx", split_axis=0, concat_axis=0, tiled=True)
        answers = lax.all_to_all(
            gather_parts(parent_parts, served_ids), "gx", split_axis=1, concat_axis=1, tiled=True
        )
        forcing_flat = jnp.take(answers, places, axis=1)

    block_rows = n_rows // 3
    block_cols = n_cols // 3
    expand = column_expansion(block_cols, n_cols, zero)
    forcing_full = expand_blocks(forcing_flat, block_rows, block_cols, n_cols, expand)
    row_start = here_x * n_rows
    left_w, right_w = row_weights(nest_segments(nest_of, row_start - 1, n_rows + 2))
    up_w = per_row(left_w, n_rows, n_cols)
    down_w = per_row(right_w, n_rows, n_cols)

    nest_state = nest.reshape(levels, n_rows * n_cols)
    halo = nest_halo
    for turn_no in range(3):
        if turn_no > 0:
            (halo,) = exchange([edges])
        nest_state, edges, extra = stencil_step(
            nest_state, halo, nu_nest, vert_mix, n_rows, n_cols, forcing_full, up_w, down_w, relax,
            gap_of=(expand, forcing_flat) if turn_no == 2 else None,
        )
    (nudge_gap,) = extra
    if by_shift:
        outgoing = jnp.where(chosen[:, None, :], nudge_gap[None, :, :], 0.0)
        incoming = jnp.concatenate(
            [outgoing[0]]
            + [lax.ppermute(outgoing[s], "gx", shifted_pairs(tiles_x, s)) for s in range(1, tiles_x)],
            axis=1,
        )
    else:
        outgoing = jnp.zeros((levels, tiles_x * slots), jnp.float32).at[:, places].set(nudge_gap)
        incoming = lax.all_to_all(outgoing, "gx", split_axis=1, concat_axis=1, tiled=True)
    summed = scatter_add_columns(incoming, served_ids, flat_parent.shape[1])
    parent_out = (flat_parent + feedback[:, None] * summed).astype(jnp.bfloat16)
    return (
        parent_out.reshape(levels, p_rows, p_cols),
        nest_state.astype(jnp.bfloat16).reshape(levels, n_rows, n_cols),
    )


def solution(mesh):
    placed = (
        P("groups", "gx", Y_AXES),
        P("groups", "gx", Y_AXES),
        P(),
        P(),
        P(),
        P(),
        P(),
        P("gx", Y_AXES, None, None),
        P("gx", Y_AXES, None),
        P(),
    )
    return jax.shard_map(
        body,
        mesh=mesh,
        in_specs=placed,
        out_specs=(P("groups", "gx", Y_AXES), P("groups", "gx", Y_AXES)),
        check_vma=False,
    )
```

```python
import functools

import jax
import jax.numpy as jnp
from jax import lax
from jax.experimental import pallas as pl
from jax.experimental.pallas import tpu as pltpu
from jax.sharding import PartitionSpec as P

Y_AXES = ("gy", "gz")
HI = lax.Precision.HIGHEST


def shift_pairs(count):
    forward = [(i, i + 1) for i in range(count - 1)]
    backward = [(i + 1, i) for i in range(count - 1)]
    return forward, backward


def edges_3d(block):
    return (block[:, -1, :], block[:, 0, :], block[:, :, -1], block[:, :, 0])


def edges_flat(flat, rows, cols):
    return (flat[:, (rows - 1) * cols :], flat[:, :cols], flat[:, cols - 1 :: cols], flat[:, ::cols])


def exchange(edge_sets):
    fwd_x, bwd_x = shift_pairs(lax.axis_size("gx"))
    fwd_y, bwd_y = shift_pairs(lax.axis_size(Y_AXES))
    last_rows = jnp.concatenate([e[0] for e in edge_sets], axis=1)
    first_rows = jnp.concatenate([e[1] for e in edge_sets], axis=1)
    last_cols = jnp.concatenate([e[2] for e in edge_sets], axis=1)
    first_cols = jnp.concatenate([e[3] for e in edge_sets], axis=1)
    above = lax.ppermute(last_rows, "gx", fwd_x)
    below = lax.ppermute(first_rows, "gx", bwd_x)
    left = lax.ppermute(last_cols, Y_AXES, fwd_y)
    right = lax.ppermute(first_cols, Y_AXES, bwd_y)
    out = []
    xo = 0
    yo = 0
    for e in edge_sets:
        out.append(((above, below, left, right), xo, yo))
        xo += e[0].shape[1]
        yo += e[2].shape[1]
    return out


def per_row(values, rows, cols):
    if values.ndim == 1:
        return jnp.broadcast_to(values[:, None], (rows, cols)).reshape(rows * cols)
    return jnp.broadcast_to(values[:, :, None], values.shape + (cols,)).reshape(
        values.shape[0], rows * cols
    )


def flat_stencil(flat, rows, cols, halo, up_w=None, down_w=None):
    above, below, left, right = (h.astype(flat.dtype) for h in halo)
    levels = flat.shape[0]
    up = jnp.concatenate([above, flat[:, :-cols]], axis=1)
    down = jnp.concatenate([flat[:, cols:], below], axis=1)
    col = lax.broadcasted_iota(jnp.int32, (1, rows * cols), 1) % cols
    zero = jnp.zeros((levels, 1), flat.dtype)
    west = jnp.where(col == 0, per_row(left, rows, cols), jnp.concatenate([zero, flat[:, :-1]], axis=1))
    east = jnp.where(
        col == cols - 1, per_row(right, rows, cols), jnp.concatenate([flat[:, 1:], zero], axis=1)
    )
    if down_w is not None:
        down = down * down_w[None, :]
        up = up * up_w[None, :]
    return down + up + east + west - 4.0 * flat


def step_kernel(*refs, rows, cols, xo, yo, nest, split, gap):
    refs = list(refs)
    if gap:
        expand_ref, fblock_ref = refs[:2]
        refs = refs[2:]
    if nest:
        (state_ref, above_ref, below_ref, left_ref, right_ref, forcing_ref, upw_ref, dnw_ref,
         nu_ref, relax_ref, vm_ref, new_ref, lrow_ref, frow_ref, lcol_ref, fcol_ref) = refs[:16]
        refs = refs[16:]
    else:
        (state_ref, above_ref, below_ref, left_ref, right_ref, nu_ref, vm_ref,
         new_ref, lrow_ref, frow_ref, lcol_ref, fcol_ref) = refs[:12]
        refs = refs[12:]
    if split:
        parts_ref = refs[0]
        refs = refs[1:]
    if gap:
        gap_ref = refs[0]
        refs = refs[1:]
    up_sc, dn_sc = refs
    n = rows * cols
    state = state_ref[...].astype(jnp.float32)
    levels = state.shape[0]
    up_sc[:, 0:cols] = above_ref[:, xo : xo + cols].astype(jnp.float32)
    up_sc[:, cols:n] = state[:, 0 : n - cols]
    dn_sc[:, 0 : n - cols] = state[:, cols:n]
    dn_sc[:, n - cols : n] = below_ref[:, xo : xo + cols].astype(jnp.float32)
    up = up_sc[...]
    down = dn_sc[...]
    lane = lax.broadcasted_iota(jnp.int32, (levels, n), 1)
    left = left_ref[...].astype(jnp.float32)
    right = right_ref[...].astype(jnp.float32)
    west = pltpu.roll(state, 1, 1)
    east = pltpu.roll(state, n - 1, 1)
    for r in range(rows):
        west = jnp.where(lane == r * cols, left[:, yo + r : yo + r + 1], west)
        east = jnp.where(lane == r * cols + cols - 1, right[:, yo + r : yo + r + 1], east)
    if nest:
        down = down * dnw_ref[...]
        up = up * upw_ref[...]
    stencil = down + up + east + west - 4.0 * state
    moved = state + nu_ref[...] * stencil
    if nest:
        moved = moved + relax_ref[...] * (forcing_ref[...] - moved)
    new = jnp.dot(vm_ref[...], moved, precision=lax.Precision.HIGH, preferred_element_type=jnp.float32)
    new_ref[...] = new
    lrow_ref[...] = new[:, n - cols : n].astype(jnp.bfloat16)
    frow_ref[...] = new[:, 0:cols].astype(jnp.bfloat16)
    narrow = new.astype(jnp.bfloat16)
    p = lax.broadcasted_iota(jnp.int32, (n, rows), 0)
    j = lax.broadcasted_iota(jnp.int32, (n, rows), 1)
    last_sel = (p == j * cols + (cols - 1)).astype(jnp.bfloat16)
    first_sel = (p == j * cols).astype(jnp.bfloat16)
    lcol_ref[...] = jnp.dot(narrow, last_sel, preferred_element_type=jnp.float32).astype(jnp.bfloat16)
    fcol_ref[...] = jnp.dot(narrow, first_sel, preferred_element_type=jnp.float32).astype(jnp.bfloat16)
    if split:
        hi = new.astype(jnp.bfloat16)
        rest = new - hi.astype(jnp.float32)
        mid = rest.astype(jnp.bfloat16)
        lo = (rest - mid.astype(jnp.float32)).astype(jnp.bfloat16)
        parts_ref[0:levels, :] = hi
        parts_ref[levels : 2 * levels, :] = mid
        parts_ref[2 * levels : 3 * levels, :] = lo
    if gap:
        expand = expand_ref[...]
        block_cols = expand.shape[0]
        pick = (((1,), (1,)), ((), ()))
        for a in range(rows // 3):
            rows3 = (
                new[:, (3 * a) * cols : (3 * a + 1) * cols]
                + new[:, (3 * a + 1) * cols : (3 * a + 2) * cols]
            ) + new[:, (3 * a + 2) * cols : (3 * a + 3) * cols]
            sums = lax.dot_general(rows3, expand, pick, precision=HI, preferred_element_type=jnp.float32)
            gap_ref[:, a * block_cols : (a + 1) * block_cols] = (
                sums / 9.0 - fblock_ref[:, a * block_cols : (a + 1) * block_cols]
            )


def stencil_step(state, placed_halo, nu, vert_mix, rows, cols, forcing=None, up_w=None, down_w=None,
                 relax=None, split=False, gap_of=None):
    levels = state.shape[0]
    n = rows * cols
    nest = forcing is not None
    (above, below, left, right), xo, yo = placed_halo
    if nest:
        args = (state, above, below, left, right, forcing, up_w[None, :], down_w[None, :],
                nu[:, None], relax[:, None], vert_mix)
    else:
        args = (state, above, below, left, right, nu[:, None], vert_mix)
    out_shape = (
        jax.ShapeDtypeStruct((levels, n), jnp.float32),
        jax.ShapeDtypeStruct((levels, cols), jnp.bfloat16),
        jax.ShapeDtypeStruct((levels, cols), jnp.bfloat16),
        jax.ShapeDtypeStruct((levels, rows), jnp.bfloat16),
        jax.ShapeDtypeStruct((levels, rows), jnp.bfloat16),
    )
    gap = gap_of is not None
    if split:
        out_shape = out_shape + (jax.ShapeDtypeStruct((3 * levels, n), jnp.bfloat16),)
    if gap:
        args = tuple(gap_of) + args
        out_shape = out_shape + (jax.ShapeDtypeStruct(gap_of[1].shape, jnp.float32),)
    flops = 2 * levels * levels * n * 6 + 4 * levels * n * rows + 20 * levels * n
    moved_bytes = sum(int(a.size) * a.dtype.itemsize for a in args) + levels * n * 4
    outs = pl.pallas_call(
        functools.partial(
            step_kernel, rows=rows, cols=cols, xo=xo, yo=yo, nest=nest, split=split, gap=gap
        ),
        out_shape=out_shape,
        scratch_shapes=[pltpu.VMEM((levels, n), jnp.float32), pltpu.VMEM((levels, n), jnp.float32)],
        cost_estimate=pl.CostEstimate(flops=flops, bytes_accessed=moved_bytes, transcendentals=0),
    )(*args)
    return outs[0], tuple(outs[1:5]), outs[5:]


def mix_levels(matrix, flat):
    return jnp.dot(matrix, flat, precision=HI, preferred_element_type=jnp.float32)


def nest_segments(nest_of, first, count):
    index_rows = first + jnp.arange(count, dtype=jnp.int32)
    inside = (index_rows >= 0) & (index_rows < nest_of.shape[0])
    return jnp.where(inside, nest_of[jnp.clip(index_rows, 0, nest_of.shape[0] - 1)], -1)


def row_weights(segments):
    left_w = (segments[:-2] == segments[1:-1]).astype(jnp.float32)
    right_w = (segments[2:] == segments[1:-1]).astype(jnp.float32)
    return (left_w, right_w)


def column_expansion(block_cols, cols, zero):
    b = lax.broadcasted_iota(jnp.int32, (block_cols, cols), 0) + zero
    c = lax.broadcasted_iota(jnp.int32, (block_cols, cols), 1)
    return (c // 3 == b).astype(jnp.float32)


def expand_blocks(block_flat, block_rows, block_cols, cols, expand):
    pieces = []
    for a in range(block_rows):
        wide = jnp.dot(
            block_flat[:, a * block_cols : (a + 1) * block_cols],
            expand,
            precision=HI,
            preferred_element_type=jnp.float32,
        )
        pieces += [wide, wide, wide]
    return jnp.concatenate(pieces, axis=1)


def block_sums(flat, block_rows, cols, expand):
    pieces = []
    for a in range(block_rows):
        rows3 = (
            flat[:, (3 * a) * cols : (3 * a + 1) * cols]
            + flat[:, (3 * a + 1) * cols : (3 * a + 2) * cols]
        ) + flat[:, (3 * a + 2) * cols : (3 * a + 3) * cols]
        pieces.append(
            lax.dot_general(
                rows3, expand, (((1,), (1,)), ((), ())), precision=HI,
                preferred_element_type=jnp.float32,
            )
        )
    return jnp.concatenate(pieces, axis=1)


def split3(values):
    hi = lax.reduce_precision(values, exponent_bits=8, mantissa_bits=7)
    rest = values - hi
    mid = lax.reduce_precision(rest, exponent_bits=8, mantissa_bits=7)
    lo = rest - mid
    return hi.astype(jnp.bfloat16), mid.astype(jnp.bfloat16), lo.astype(jnp.bfloat16)


def shifted_pairs(count, shift):
    return [(i, (i + shift) % count) for i in range(count)]


def gather_columns(values, ids):
    levels, width = values.shape
    onehot = (lax.broadcasted_iota(jnp.int32, (width, 1), 0) == ids[None, :]).astype(jnp.bfloat16)
    parts = jnp.concatenate(split3(values), axis=0)
    total = jnp.dot(parts, onehot, preferred_element_type=jnp.float32)
    return (total[:levels] + total[levels : 2 * levels]) + total[2 * levels :]


def gather_parts(parts, ids):
    levels = parts.shape[0] // 3
    width = parts.shape[1]
    onehot = (lax.broadcasted_iota(jnp.int32, (width, 1), 0) == ids[None, :]).astype(jnp.bfloat16)
    total = jnp.dot(parts, onehot, preferred_element_type=jnp.float32)
    return (total[:levels] + total[levels : 2 * levels]) + total[2 * levels :]


def scatter_add_columns(values, ids, width):
    levels = values.shape[0]
    onehot = (ids[:, None] == lax.broadcasted_iota(jnp.int32, (1, width), 1)).astype(jnp.bfloat16)
    if values.dtype == jnp.bfloat16:
        return jnp.dot(values, onehot, preferred_element_type=jnp.float32)
    parts = jnp.concatenate(split3(values), axis=0)
    total = jnp.dot(parts, onehot, preferred_element_type=jnp.float32)
    return (total[:levels] + total[levels : 2 * levels]) + total[2 * levels :]


def body(parent, nest, nu_parent, nu_nest, relax, feedback, vert_mix, fp_owner, fp_cell, nest_of):
    levels, p_rows, p_cols = parent.shape
    _, n_rows, n_cols = nest.shape
    tiles_x = lax.axis_size("gx")
    here_x = lax.axis_index("gx")
    zero = jnp.minimum(here_x, 0)

    parent_halo, nest_halo = exchange([edges_3d(parent), edges_3d(nest)])
    flat_parent, _, (parent_parts,) = stencil_step(
        parent.reshape(levels, p_rows * p_cols), parent_halo, nu_parent, vert_mix, p_rows, p_cols,
        split=True,
    )

    owners = fp_owner.reshape(-1)
    cells = fp_cell.reshape(-1)
    requests = owners.shape[0]
    slots = 4 * requests // tiles_x
    by_shift = slots >= requests
    if by_shift:
        rel = (owners - here_x + tiles_x) % tiles_x
        chosen = rel[None, :] == jnp.arange(tiles_x, dtype=jnp.int32)[:, None]
        wanted = jnp.where(chosen, cells[None, :], 0)
        served = [wanted[0]] + [
            lax.ppermute(wanted[s], "gx", shifted_pairs(tiles_x, s)) for s in range(1, tiles_x)
        ]
        served_ids = jnp.concatenate(served, axis=0)
        back = [None] + [
            lax.ppermute(gather_parts(parent_parts, served[s]), "gx", shifted_pairs(tiles_x, -s))
            for s in range(1, tiles_x)
        ]
        back[0] = gather_parts(parent_parts, served[0])
        forcing_flat = back[0]
        for s in range(1, tiles_x):
            forcing_flat = jnp.where(chosen[s][None, :], back[s], forcing_flat)
    else:
        owner_ids = jnp.arange(tiles_x, dtype=jnp.int32)
        onehot = (owners[:, None] == owner_ids[None, :]).astype(jnp.int32)
        before = jnp.cumsum(onehot, axis=0) - onehot
        order_in = jnp.sum(before * onehot, axis=1)
        places = owners * slots + order_in
        wanted = jnp.zeros((tiles_x * slots,), jnp.int32).at[places].set(cells)
        served_ids = lax.all_to_all(wanted, "gx", split_axis=0, concat_axis=0, tiled=True)
        answers = lax.all_to_all(
            gather_parts(parent_parts, served_ids), "gx", split_axis=1, concat_axis=1, tiled=True
        )
        forcing_flat = jnp.take(answers, places, axis=1)

    block_rows = n_rows // 3
    block_cols = n_cols // 3
    expand = column_expansion(block_cols, n_cols, zero)
    forcing_full = expand_blocks(forcing_flat, block_rows, block_cols, n_cols, expand)
    row_start = here_x * n_rows
    left_w, right_w = row_weights(nest_segments(nest_of, row_start - 1, n_rows + 2))
    up_w = per_row(left_w, n_rows, n_cols)
    down_w = per_row(right_w, n_rows, n_cols)

    nest_state = nest.reshape(levels, n_rows * n_cols)
    halo = nest_halo
    for turn_no in range(3):
        if turn_no > 0:
            (halo,) = exchange([edges])
        nest_state, edges, extra = stencil_step(
            nest_state, halo, nu_nest, vert_mix, n_rows, n_cols, forcing_full, up_w, down_w, relax,
            gap_of=(expand, forcing_flat) if turn_no == 2 else None,
        )
    (nudge_gap,) = extra
    if by_shift:
        outgoing = jnp.where(chosen[:, None, :], nudge_gap[None, :, :], 0.0).astype(jnp.bfloat16)
        incoming = jnp.concatenate(
            [outgoing[0]]
            + [lax.ppermute(outgoing[s], "gx", shifted_pairs(tiles_x, s)) for s in range(1, tiles_x)],
            axis=1,
        )
    else:
        outgoing = jnp.zeros((levels, tiles_x * slots), jnp.float32).at[:, places].set(nudge_gap)
        incoming = lax.all_to_all(outgoing, "gx", split_axis=1, concat_axis=1, tiled=True)
    summed = scatter_add_columns(incoming, served_ids, flat_parent.shape[1])
    parent_out = (flat_parent + feedback[:, None] * summed).astype(jnp.bfloat16)
    return (
        parent_out.reshape(levels, p_rows, p_cols),
        nest_state.astype(jnp.bfloat16).reshape(levels, n_rows, n_cols),
    )


def solution(mesh):
    placed = (
        P("groups", "gx", Y_AXES),
        P("groups", "gx", Y_AXES),
        P(),
        P(),
        P(),
        P(),
        P(),
        P("gx", Y_AXES, None, None),
        P("gx", Y_AXES, None),
        P(),
    )
    return jax.shard_map(
        body,
        mesh=mesh,
        in_specs=placed,
        out_specs=(P("groups", "gx", Y_AXES), P("groups", "gx", Y_AXES)),
        check_vma=False,
    )
```

```python
import functools

import jax
import jax.numpy as jnp
from jax import lax
from jax.experimental import pallas as pl
from jax.experimental.pallas import tpu as pltpu
from jax.sharding import PartitionSpec as P


Y_AXES = ("gy", "gz")
HI = lax.Precision.HIGHEST


def shift_pairs(count):
    forward = [(i, i + 1) for i in range(count - 1)]
    backward = [(i + 1, i) for i in range(count - 1)]
    return forward, backward


def edges_3d(block):
    return (block[:, -1, :], block[:, 0, :], block[:, :, -1], block[:, :, 0])


def exchange(edge_sets):
    fwd_x, bwd_x = shift_pairs(lax.axis_size("gx"))
    fwd_y, bwd_y = shift_pairs(lax.axis_size(Y_AXES))
    last_rows = jnp.concatenate([e[0] for e in edge_sets], axis=1)
    first_rows = jnp.concatenate([e[1] for e in edge_sets], axis=1)
    last_cols = jnp.concatenate([e[2] for e in edge_sets], axis=1)
    first_cols = jnp.concatenate([e[3] for e in edge_sets], axis=1)
    above = lax.ppermute(last_rows, "gx", fwd_x)
    below = lax.ppermute(first_rows, "gx", bwd_x)
    left = lax.ppermute(last_cols, Y_AXES, fwd_y)
    right = lax.ppermute(first_cols, Y_AXES, bwd_y)
    out = []
    xo = 0
    yo = 0
    for e in edge_sets:
        out.append(((above, below, left, right), xo, yo))
        xo += e[0].shape[1]
        yo += e[2].shape[1]
    return out


def per_row(values, rows, cols):
    if values.ndim == 1:
        return jnp.broadcast_to(values[:, None], (rows, cols)).reshape(rows * cols)
    return jnp.broadcast_to(values[:, :, None], values.shape + (cols,)).reshape(
        values.shape[0], rows * cols
    )


def step_kernel(*refs, rows, cols, xo, yo, nest, split, gap):
    refs = list(refs)
    if gap:
        expand_ref, fblock_ref = refs[:2]
        refs = refs[2:]
    if nest:
        (state_ref, above_ref, below_ref, left_ref, right_ref, forcing_ref, upw_ref, dnw_ref,
         nu_ref, relax_ref, vm_ref, new_ref, lrow_ref, frow_ref, lcol_ref, fcol_ref) = refs[:16]
        refs = refs[16:]
    else:
        (state_ref, above_ref, below_ref, left_ref, right_ref, nu_ref, vm_ref,
         new_ref, lrow_ref, frow_ref, lcol_ref, fcol_ref) = refs[:12]
        refs = refs[12:]
    if split:
        parts_ref = refs[0]
        refs = refs[1:]
    if gap:
        gap_ref = refs[0]
        refs = refs[1:]
    up_sc, dn_sc = refs
    n = rows * cols
    state = state_ref[...].astype(jnp.float32)
    levels = state.shape[0]
    up_sc[:, 0:cols] = above_ref[:, xo : xo + cols].astype(jnp.float32)
    up_sc[:, cols:n] = state[:, 0 : n - cols]
    dn_sc[:, 0 : n - cols] = state[:, cols:n]
    dn_sc[:, n - cols : n] = below_ref[:, xo : xo + cols].astype(jnp.float32)
    up = up_sc[...]
    down = dn_sc[...]
    lane = lax.broadcasted_iota(jnp.int32, (levels, n), 1)
    left = left_ref[...].astype(jnp.float32)
    right = right_ref[...].astype(jnp.float32)
    west = pltpu.roll(state, 1, 1)
    east = pltpu.roll(state, n - 1, 1)
    for r in range(rows):
        west = jnp.where(lane == r * cols, left[:, yo + r : yo + r + 1], west)
        east = jnp.where(lane == r * cols + cols - 1, right[:, yo + r : yo + r + 1], east)
    if nest:
        down = down * dnw_ref[...]
        up = up * upw_ref[...]
    stencil = down + up + east + west - 4.0 * state
    moved = state + nu_ref[...] * stencil
    if nest:
        moved = moved + relax_ref[...] * (forcing_ref[...] - moved)
    new = jnp.dot(vm_ref[...], moved, precision=lax.Precision.HIGH, preferred_element_type=jnp.float32)
    new_ref[...] = new
    lrow_ref[...] = new[:, n - cols : n].astype(jnp.bfloat16)
    frow_ref[...] = new[:, 0:cols].astype(jnp.bfloat16)
    narrow = new.astype(jnp.bfloat16)
    p = lax.broadcasted_iota(jnp.int32, (n, rows), 0)
    j = lax.broadcasted_iota(jnp.int32, (n, rows), 1)
    last_sel = (p == j * cols + (cols - 1)).astype(jnp.bfloat16)
    first_sel = (p == j * cols).astype(jnp.bfloat16)
    lcol_ref[...] = jnp.dot(narrow, last_sel, preferred_element_type=jnp.float32).astype(jnp.bfloat16)
    fcol_ref[...] = jnp.dot(narrow, first_sel, preferred_element_type=jnp.float32).astype(jnp.bfloat16)
    if split:
        hi = new.astype(jnp.bfloat16)
        rest = new - hi.astype(jnp.float32)
        mid = rest.astype(jnp.bfloat16)
        lo = (rest - mid.astype(jnp.float32)).astype(jnp.bfloat16)
        parts_ref[0:levels, :] = hi
        parts_ref[levels : 2 * levels, :] = mid
        parts_ref[2 * levels : 3 * levels, :] = lo
    if gap:
        expand = expand_ref[...]
        block_cols = expand.shape[0]
        pick = (((1,), (1,)), ((), ()))
        for a in range(rows // 3):
            rows3 = (
                new[:, (3 * a) * cols : (3 * a + 1) * cols]
                + new[:, (3 * a + 1) * cols : (3 * a + 2) * cols]
            ) + new[:, (3 * a + 2) * cols : (3 * a + 3) * cols]
            sums = lax.dot_general(rows3, expand, pick, precision=HI, preferred_element_type=jnp.float32)
            gap_ref[:, a * block_cols : (a + 1) * block_cols] = (
                sums / 9.0 - fblock_ref[:, a * block_cols : (a + 1) * block_cols]
            )


def stencil_step(state, placed_halo, nu, vert_mix, rows, cols, forcing=None, up_w=None, down_w=None,
                 relax=None, split=False, gap_of=None):
    levels = state.shape[0]
    n = rows * cols
    nest = forcing is not None
    (above, below, left, right), xo, yo = placed_halo
    if nest:
        args = (state, above, below, left, right, forcing, up_w[None, :], down_w[None, :],
                nu[:, None], relax[:, None], vert_mix)
    else:
        args = (state, above, below, left, right, nu[:, None], vert_mix)
    out_shape = (
        jax.ShapeDtypeStruct((levels, n), jnp.float32),
        jax.ShapeDtypeStruct((levels, cols), jnp.bfloat16),
        jax.ShapeDtypeStruct((levels, cols), jnp.bfloat16),
        jax.ShapeDtypeStruct((levels, rows), jnp.bfloat16),
        jax.ShapeDtypeStruct((levels, rows), jnp.bfloat16),
    )
    gap = gap_of is not None
    if split:
        out_shape = out_shape + (jax.ShapeDtypeStruct((3 * levels, n), jnp.bfloat16),)
    if gap:
        args = tuple(gap_of) + args
        out_shape = out_shape + (jax.ShapeDtypeStruct(gap_of[1].shape, jnp.float32),)
    flops = 2 * levels * levels * n * 6 + 4 * levels * n * rows + 20 * levels * n
    moved_bytes = sum(int(a.size) * a.dtype.itemsize for a in args) + levels * n * 4
    outs = pl.pallas_call(
        functools.partial(
            step_kernel, rows=rows, cols=cols, xo=xo, yo=yo, nest=nest, split=split, gap=gap
        ),
        out_shape=out_shape,
        scratch_shapes=[pltpu.VMEM((levels, n), jnp.float32), pltpu.VMEM((levels, n), jnp.float32)],
        cost_estimate=pl.CostEstimate(flops=flops, bytes_accessed=moved_bytes, transcendentals=0),
    )(*args)
    return outs[0], tuple(outs[1:5]), outs[5:]


def nest_segments(nest_of, first, count):
    index_rows = first + jnp.arange(count, dtype=jnp.int32)
    inside = (index_rows >= 0) & (index_rows < nest_of.shape[0])
    return jnp.where(inside, nest_of[jnp.clip(index_rows, 0, nest_of.shape[0] - 1)], -1)


def row_weights(segments):
    left_w = (segments[:-2] == segments[1:-1]).astype(jnp.float32)
    right_w = (segments[2:] == segments[1:-1]).astype(jnp.float32)
    return (left_w, right_w)


def column_expansion(block_cols, cols, zero):
    b = lax.broadcasted_iota(jnp.int32, (block_cols, cols), 0) + zero
    c = lax.broadcasted_iota(jnp.int32, (block_cols, cols), 1)
    return (c // 3 == b).astype(jnp.float32)


def expand_blocks(block_flat, block_rows, block_cols, expand):
    pieces = []
    for a in range(block_rows):
        wide = jnp.dot(
            block_flat[:, a * block_cols : (a + 1) * block_cols],
            expand,
            precision=HI,
            preferred_element_type=jnp.float32,
        )
        pieces += [wide, wide, wide]
    return jnp.concatenate(pieces, axis=1)


def split3(values):
    hi = lax.reduce_precision(values, exponent_bits=8, mantissa_bits=7)
    rest = values - hi
    mid = lax.reduce_precision(rest, exponent_bits=8, mantissa_bits=7)
    lo = rest - mid
    return hi.astype(jnp.bfloat16), mid.astype(jnp.bfloat16), lo.astype(jnp.bfloat16)


def shifted_pairs(count, shift):
    return [(i, (i + shift) % count) for i in range(count)]


def gather_parts(parts, ids):
    levels = parts.shape[0] // 3
    width = parts.shape[1]
    onehot = (lax.broadcasted_iota(jnp.int32, (width, 1), 0) == ids[None, :]).astype(jnp.bfloat16)
    total = jnp.dot(parts, onehot, preferred_element_type=jnp.float32)
    return (total[:levels] + total[levels : 2 * levels]) + total[2 * levels :]


def scatter_add_columns(values, ids, width):
    levels = values.shape[0]
    onehot = (ids[:, None] == lax.broadcasted_iota(jnp.int32, (1, width), 1)).astype(jnp.bfloat16)
    if values.dtype == jnp.bfloat16:
        return jnp.dot(values, onehot, preferred_element_type=jnp.float32)
    parts = jnp.concatenate(split3(values), axis=0)
    total = jnp.dot(parts, onehot, preferred_element_type=jnp.float32)
    return (total[:levels] + total[levels : 2 * levels]) + total[2 * levels :]


def body_steps(parent, nest, nu_parent, nu_nest, relax, feedback, vert_mix, fp_owner, fp_cell, nest_of):
    levels, p_rows, p_cols = parent.shape
    _, n_rows, n_cols = nest.shape
    tiles_x = lax.axis_size("gx")
    here_x = lax.axis_index("gx")
    zero = jnp.minimum(here_x, 0)

    parent_halo, nest_halo = exchange([edges_3d(parent), edges_3d(nest)])
    flat_parent, _, (parent_parts,) = stencil_step(
        parent.reshape(levels, p_rows * p_cols), parent_halo, nu_parent, vert_mix, p_rows, p_cols,
        split=True,
    )

    owners = fp_owner.reshape(-1)
    cells = fp_cell.reshape(-1)
    requests = owners.shape[0]
    slots = 4 * requests // tiles_x
    by_shift = slots >= requests
    if by_shift:
        rel = (owners - here_x + tiles_x) % tiles_x
        chosen = rel[None, :] == jnp.arange(tiles_x, dtype=jnp.int32)[:, None]
        wanted = jnp.where(chosen, cells[None, :], 0)
        served = [wanted[0]] + [
            lax.ppermute(wanted[s], "gx", shifted_pairs(tiles_x, s)) for s in range(1, tiles_x)
        ]
        served_ids = jnp.concatenate(served, axis=0)
        back = [None] + [
            lax.ppermute(gather_parts(parent_parts, served[s]), "gx", shifted_pairs(tiles_x, -s))
            for s in range(1, tiles_x)
        ]
        back[0] = gather_parts(parent_parts, served[0])
        forcing_flat = back[0]
        for s in range(1, tiles_x):
            forcing_flat = jnp.where(chosen[s][None, :], back[s], forcing_flat)
    else:
        owner_ids = jnp.arange(tiles_x, dtype=jnp.int32)
        onehot = (owners[:, None] == owner_ids[None, :]).astype(jnp.int32)
        before = jnp.cumsum(onehot, axis=0) - onehot
        order_in = jnp.sum(before * onehot, axis=1)
        places = owners * slots + order_in
        wanted = jnp.zeros((tiles_x * slots,), jnp.int32).at[places].set(cells)
        served_ids = lax.all_to_all(wanted, "gx", split_axis=0, concat_axis=0, tiled=True)
        answers = lax.all_to_all(
            gather_parts(parent_parts, served_ids), "gx", split_axis=1, concat_axis=1, tiled=True
        )
        forcing_flat = jnp.take(answers, places, axis=1)

    block_rows = n_rows // 3
    block_cols = n_cols // 3
    expand = column_expansion(block_cols, n_cols, zero)
    forcing_full = expand_blocks(forcing_flat, block_rows, block_cols, expand)
    row_start = here_x * n_rows
    left_w, right_w = row_weights(nest_segments(nest_of, row_start - 1, n_rows + 2))
    up_w = per_row(left_w, n_rows, n_cols)
    down_w = per_row(right_w, n_rows, n_cols)

    nest_state = nest.reshape(levels, n_rows * n_cols)
    halo = nest_halo
    for turn_no in range(3):
        if turn_no > 0:
            (halo,) = exchange([edges])
        nest_state, edges, extra = stencil_step(
            nest_state, halo, nu_nest, vert_mix, n_rows, n_cols, forcing_full, up_w, down_w, relax,
            gap_of=(expand, forcing_flat) if turn_no == 2 else None,
        )
    (nudge_gap,) = extra
    if by_shift:
        outgoing = jnp.where(chosen[:, None, :], nudge_gap[None, :, :], 0.0)
        incoming = jnp.concatenate(
            [outgoing[0]]
            + [
                lax.ppermute(outgoing[s].astype(jnp.float16), "gx", shifted_pairs(tiles_x, s)).astype(
                    jnp.float32
                )
                for s in range(1, tiles_x)
            ],
            axis=1,
        )
    else:
        outgoing = jnp.zeros((levels, tiles_x * slots), jnp.float32).at[:, places].set(nudge_gap)
        incoming = lax.all_to_all(outgoing, "gx", split_axis=1, concat_axis=1, tiled=True)
    summed = scatter_add_columns(incoming, served_ids, flat_parent.shape[1])
    parent_out = (flat_parent + feedback[:, None] * summed).astype(jnp.bfloat16)
    return (
        parent_out.reshape(levels, p_rows, p_cols),
        nest_state.astype(jnp.bfloat16).reshape(levels, n_rows, n_cols),
    )


def solution(mesh):
    placed = (
        P("groups", "gx", Y_AXES),
        P("groups", "gx", Y_AXES),
        P(),
        P(),
        P(),
        P(),
        P(),
        P("gx", Y_AXES, None, None),
        P("gx", Y_AXES, None),
        P(),
    )
    return jax.shard_map(
        body_steps,
        mesh=mesh,
        in_specs=placed,
        out_specs=(P("groups", "gx", Y_AXES), P("groups", "gx", Y_AXES)),
        check_vma=False,
    )
```

```python
import functools

import jax
import jax.numpy as jnp
from jax import lax
from jax.experimental import pallas as pl
from jax.experimental.pallas import tpu as pltpu
from jax.sharding import PartitionSpec as P


Y_AXES = ("gy", "gz")
HI = lax.Precision.HIGHEST


def shift_pairs(count):
    forward = [(i, i + 1) for i in range(count - 1)]
    backward = [(i + 1, i) for i in range(count - 1)]
    return forward, backward


def edges_3d(block):
    return (block[:, -1, :], block[:, 0, :], block[:, :, -1], block[:, :, 0])


def exchange(edge_sets):
    fwd_x, bwd_x = shift_pairs(lax.axis_size("gx"))
    fwd_y, bwd_y = shift_pairs(lax.axis_size(Y_AXES))
    last_rows = jnp.concatenate([e[0] for e in edge_sets], axis=1)
    first_rows = jnp.concatenate([e[1] for e in edge_sets], axis=1)
    last_cols = jnp.concatenate([e[2] for e in edge_sets], axis=1)
    first_cols = jnp.concatenate([e[3] for e in edge_sets], axis=1)
    above = lax.ppermute(last_rows, "gx", fwd_x)
    below = lax.ppermute(first_rows, "gx", bwd_x)
    left = lax.ppermute(last_cols, Y_AXES, fwd_y)
    right = lax.ppermute(first_cols, Y_AXES, bwd_y)
    out = []
    xo = 0
    yo = 0
    for e in edge_sets:
        out.append(((above, below, left, right), xo, yo))
        xo += e[0].shape[1]
        yo += e[2].shape[1]
    return out


def per_row(values, rows, cols):
    if values.ndim == 1:
        return jnp.broadcast_to(values[:, None], (rows, cols)).reshape(rows * cols)
    return jnp.broadcast_to(values[:, :, None], values.shape + (cols,)).reshape(
        values.shape[0], rows * cols
    )


def step_kernel(*refs, rows, cols, xo, yo, nest, split, gap):
    refs = list(refs)
    if gap:
        expand_ref, fblock_ref = refs[:2]
        refs = refs[2:]
    if nest:
        (state_ref, above_ref, below_ref, left_ref, right_ref, forcing_ref, upw_ref, dnw_ref,
         nu_ref, relax_ref, vm_ref, new_ref, lrow_ref, frow_ref, lcol_ref, fcol_ref) = refs[:16]
        refs = refs[16:]
    else:
        (state_ref, above_ref, below_ref, left_ref, right_ref, nu_ref, vm_ref,
         new_ref, lrow_ref, frow_ref, lcol_ref, fcol_ref) = refs[:12]
        refs = refs[12:]
    if split:
        parts_ref = refs[0]
        refs = refs[1:]
    if gap:
        gap_ref = refs[0]
        refs = refs[1:]
    up_sc, dn_sc = refs
    n = rows * cols
    state = state_ref[...].astype(jnp.float32)
    levels = state.shape[0]
    up_sc[:, 0:cols] = above_ref[:, xo : xo + cols].astype(jnp.float32)
    up_sc[:, cols:n] = state[:, 0 : n - cols]
    dn_sc[:, 0 : n - cols] = state[:, cols:n]
    dn_sc[:, n - cols : n] = below_ref[:, xo : xo + cols].astype(jnp.float32)
    up = up_sc[...]
    down = dn_sc[...]
    lane = lax.broadcasted_iota(jnp.int32, (levels, n), 1)
    left = left_ref[...].astype(jnp.float32)
    right = right_ref[...].astype(jnp.float32)
    west = pltpu.roll(state, 1, 1)
    east = pltpu.roll(state, n - 1, 1)
    for r in range(rows):
        west = jnp.where(lane == r * cols, left[:, yo + r : yo + r + 1], west)
        east = jnp.where(lane == r * cols + cols - 1, right[:, yo + r : yo + r + 1], east)
    if nest:
        down = down * dnw_ref[...]
        up = up * upw_ref[...]
    stencil = down + up + east + west - 4.0 * state
    moved = state + nu_ref[...] * stencil
    if nest:
        moved = moved + relax_ref[...] * (forcing_ref[...] - moved)
    new = jnp.dot(vm_ref[...], moved, precision=lax.Precision.HIGH, preferred_element_type=jnp.float32)
    new_ref[...] = new
    lrow_ref[...] = new[:, n - cols : n].astype(jnp.bfloat16)
    frow_ref[...] = new[:, 0:cols].astype(jnp.bfloat16)
    narrow = new.astype(jnp.bfloat16)
    p = lax.broadcasted_iota(jnp.int32, (n, rows), 0)
    j = lax.broadcasted_iota(jnp.int32, (n, rows), 1)
    last_sel = (p == j * cols + (cols - 1)).astype(jnp.bfloat16)
    first_sel = (p == j * cols).astype(jnp.bfloat16)
    lcol_ref[...] = jnp.dot(narrow, last_sel, preferred_element_type=jnp.float32).astype(jnp.bfloat16)
    fcol_ref[...] = jnp.dot(narrow, first_sel, preferred_element_type=jnp.float32).astype(jnp.bfloat16)
    if split:
        hi = new.astype(jnp.bfloat16)
        rest = new - hi.astype(jnp.float32)
        mid = rest.astype(jnp.bfloat16)
        lo = (rest - mid.astype(jnp.float32)).astype(jnp.bfloat16)
        parts_ref[0:levels, :] = hi
        parts_ref[levels : 2 * levels, :] = mid
        parts_ref[2 * levels : 3 * levels, :] = lo
    if gap:
        expand = expand_ref[...]
        block_cols = expand.shape[0]
        pick = (((1,), (1,)), ((), ()))
        for a in range(rows // 3):
            rows3 = (
                new[:, (3 * a) * cols : (3 * a + 1) * cols]
                + new[:, (3 * a + 1) * cols : (3 * a + 2) * cols]
            ) + new[:, (3 * a + 2) * cols : (3 * a + 3) * cols]
            sums = lax.dot_general(rows3, expand, pick, precision=HI, preferred_element_type=jnp.float32)
            gap_ref[:, a * block_cols : (a + 1) * block_cols] = (
                sums / 9.0 - fblock_ref[:, a * block_cols : (a + 1) * block_cols]
            )


def stencil_step(state, placed_halo, nu, vert_mix, rows, cols, forcing=None, up_w=None, down_w=None,
                 relax=None, split=False, gap_of=None):
    levels = state.shape[0]
    n = rows * cols
    nest = forcing is not None
    (above, below, left, right), xo, yo = placed_halo
    if nest:
        args = (state, above, below, left, right, forcing, up_w[None, :], down_w[None, :],
                nu[:, None], relax[:, None], vert_mix)
    else:
        args = (state, above, below, left, right, nu[:, None], vert_mix)
    out_shape = (
        jax.ShapeDtypeStruct((levels, n), jnp.float32),
        jax.ShapeDtypeStruct((levels, cols), jnp.bfloat16),
        jax.ShapeDtypeStruct((levels, cols), jnp.bfloat16),
        jax.ShapeDtypeStruct((levels, rows), jnp.bfloat16),
        jax.ShapeDtypeStruct((levels, rows), jnp.bfloat16),
    )
    gap = gap_of is not None
    if split:
        out_shape = out_shape + (jax.ShapeDtypeStruct((3 * levels, n), jnp.bfloat16),)
    if gap:
        args = tuple(gap_of) + args
        out_shape = out_shape + (jax.ShapeDtypeStruct(gap_of[1].shape, jnp.float32),)
    flops = 2 * levels * levels * n * 6 + 4 * levels * n * rows + 20 * levels * n
    moved_bytes = sum(int(a.size) * a.dtype.itemsize for a in args) + levels * n * 4
    outs = pl.pallas_call(
        functools.partial(
            step_kernel, rows=rows, cols=cols, xo=xo, yo=yo, nest=nest, split=split, gap=gap
        ),
        out_shape=out_shape,
        scratch_shapes=[pltpu.VMEM((levels, n), jnp.float32), pltpu.VMEM((levels, n), jnp.float32)],
        cost_estimate=pl.CostEstimate(flops=flops, bytes_accessed=moved_bytes, transcendentals=0),
    )(*args)
    return outs[0], tuple(outs[1:5]), outs[5:]


def nest_segments(nest_of, first, count):
    index_rows = first + jnp.arange(count, dtype=jnp.int32)
    inside = (index_rows >= 0) & (index_rows < nest_of.shape[0])
    return jnp.where(inside, nest_of[jnp.clip(index_rows, 0, nest_of.shape[0] - 1)], -1)


def row_weights(segments):
    left_w = (segments[:-2] == segments[1:-1]).astype(jnp.float32)
    right_w = (segments[2:] == segments[1:-1]).astype(jnp.float32)
    return (left_w, right_w)


def column_expansion(block_cols, cols, zero):
    b = lax.broadcasted_iota(jnp.int32, (block_cols, cols), 0) + zero
    c = lax.broadcasted_iota(jnp.int32, (block_cols, cols), 1)
    return (c // 3 == b).astype(jnp.float32)


def expand_blocks(block_flat, block_rows, block_cols, expand):
    pieces = []
    for a in range(block_rows):
        wide = jnp.dot(
            block_flat[:, a * block_cols : (a + 1) * block_cols],
            expand,
            precision=HI,
            preferred_element_type=jnp.float32,
        )
        pieces += [wide, wide, wide]
    return jnp.concatenate(pieces, axis=1)


def split3(values):
    hi = lax.reduce_precision(values, exponent_bits=8, mantissa_bits=7)
    rest = values - hi
    mid = lax.reduce_precision(rest, exponent_bits=8, mantissa_bits=7)
    lo = rest - mid
    return hi.astype(jnp.bfloat16), mid.astype(jnp.bfloat16), lo.astype(jnp.bfloat16)


def shifted_pairs(count, shift):
    return [(i, (i + shift) % count) for i in range(count)]


def gather_parts(parts, ids):
    levels = parts.shape[0] // 3
    width = parts.shape[1]
    onehot = (lax.broadcasted_iota(jnp.int32, (width, 1), 0) == ids[None, :]).astype(jnp.bfloat16)
    total = jnp.dot(parts, onehot, preferred_element_type=jnp.float32)
    return (total[:levels] + total[levels : 2 * levels]) + total[2 * levels :]


def scatter_add_columns(values, ids, width):
    levels = values.shape[0]
    onehot = (ids[:, None] == lax.broadcasted_iota(jnp.int32, (1, width), 1)).astype(jnp.bfloat16)
    if values.dtype == jnp.bfloat16:
        return jnp.dot(values, onehot, preferred_element_type=jnp.float32)
    parts = jnp.concatenate(split3(values), axis=0)
    total = jnp.dot(parts, onehot, preferred_element_type=jnp.float32)
    return (total[:levels] + total[levels : 2 * levels]) + total[2 * levels :]


def body_steps(parent, nest, nu_parent, nu_nest, relax, feedback, vert_mix, fp_owner, fp_cell, nest_of):
    levels, p_rows, p_cols = parent.shape
    _, n_rows, n_cols = nest.shape
    tiles_x = lax.axis_size("gx")
    here_x = lax.axis_index("gx")
    zero = jnp.minimum(here_x, 0)

    parent_halo, nest_halo = exchange([edges_3d(parent), edges_3d(nest)])
    flat_parent, _, (parent_parts,) = stencil_step(
        parent.reshape(levels, p_rows * p_cols), parent_halo, nu_parent, vert_mix, p_rows, p_cols,
        split=True,
    )

    owners = fp_owner.reshape(-1)
    cells = fp_cell.reshape(-1)
    requests = owners.shape[0]
    slots = 4 * requests // tiles_x
    by_shift = slots >= requests
    if by_shift:
        rel = (owners - here_x + tiles_x) % tiles_x
        chosen = rel[None, :] == jnp.arange(tiles_x, dtype=jnp.int32)[:, None]
        wanted = jnp.where(chosen, cells[None, :], 0)
        served = [wanted[0]] + [
            lax.ppermute(wanted[s], "gx", shifted_pairs(tiles_x, s)) for s in range(1, tiles_x)
        ]
        served_ids = jnp.concatenate(served, axis=0)
        back = [None] + [
            lax.ppermute(gather_parts(parent_parts, served[s]), "gx", shifted_pairs(tiles_x, -s))
            for s in range(1, tiles_x)
        ]
        back[0] = gather_parts(parent_parts, served[0])
        forcing_flat = back[0]
        for s in range(1, tiles_x):
            forcing_flat = jnp.where(chosen[s][None, :], back[s], forcing_flat)
    else:
        owner_ids = jnp.arange(tiles_x, dtype=jnp.int32)
        onehot = (owners[:, None] == owner_ids[None, :]).astype(jnp.int32)
        before = jnp.cumsum(onehot, axis=0) - onehot
        order_in = jnp.sum(before * onehot, axis=1)
        places = owners * slots + order_in
        wanted = jnp.zeros((tiles_x * slots,), jnp.int32).at[places].set(cells)
        served_ids = lax.all_to_all(wanted, "gx", split_axis=0, concat_axis=0, tiled=True)
        answers = lax.all_to_all(
            gather_parts(parent_parts, served_ids), "gx", split_axis=1, concat_axis=1, tiled=True
        )
        forcing_flat = jnp.take(answers, places, axis=1)

    block_rows = n_rows // 3
    block_cols = n_cols // 3
    expand = column_expansion(block_cols, n_cols, zero)
    forcing_full = expand_blocks(forcing_flat, block_rows, block_cols, expand)
    row_start = here_x * n_rows
    left_w, right_w = row_weights(nest_segments(nest_of, row_start - 1, n_rows + 2))
    up_w = per_row(left_w, n_rows, n_cols)
    down_w = per_row(right_w, n_rows, n_cols)

    nest_state = nest.reshape(levels, n_rows * n_cols)
    halo = nest_halo
    for turn_no in range(3):
        if turn_no > 0:
            (halo,) = exchange([edges])
        nest_state, edges, extra = stencil_step(
            nest_state, halo, nu_nest, vert_mix, n_rows, n_cols, forcing_full, up_w, down_w, relax,
            gap_of=(expand, forcing_flat) if turn_no == 2 else None,
        )
    (nudge_gap,) = extra
    if by_shift:
        outgoing = jnp.where(chosen[:, None, :], nudge_gap[None, :, :], 0.0).astype(jnp.bfloat16)
        incoming = jnp.concatenate(
            [outgoing[0]]
            + [lax.ppermute(outgoing[s], "gx", shifted_pairs(tiles_x, s)) for s in range(1, tiles_x)],
            axis=1,
        )
    else:
        outgoing = jnp.zeros((levels, tiles_x * slots), jnp.float32).at[:, places].set(nudge_gap)
        incoming = lax.all_to_all(outgoing, "gx", split_axis=1, concat_axis=1, tiled=True)
    summed = scatter_add_columns(incoming, served_ids, flat_parent.shape[1])
    parent_out = (flat_parent + feedback[:, None] * summed).astype(jnp.bfloat16)
    return (
        parent_out.reshape(levels, p_rows, p_cols),
        nest_state.astype(jnp.bfloat16).reshape(levels, n_rows, n_cols),
    )


def solution(mesh):
    placed = (
        P("groups", "gx", Y_AXES),
        P("groups", "gx", Y_AXES),
        P(),
        P(),
        P(),
        P(),
        P(),
        P("gx", Y_AXES, None, None),
        P("gx", Y_AXES, None),
        P(),
    )
    return jax.shard_map(
        body_steps,
        mesh=mesh,
        in_specs=placed,
        out_specs=(P("groups", "gx", Y_AXES), P("groups", "gx", Y_AXES)),
        check_vma=False,
    )
```

```python
import functools

import jax
import jax.numpy as jnp
from jax import lax
from jax.experimental import pallas as pl
from jax.experimental.pallas import tpu as pltpu
from jax.sharding import PartitionSpec as P


Y_AXES = ("gy", "gz")
HI = lax.Precision.HIGHEST


def shift_pairs(count):
    forward = [(i, i + 1) for i in range(count - 1)]
    backward = [(i + 1, i) for i in range(count - 1)]
    return forward, backward


def edges_3d(block):
    return (block[:, -1, :], block[:, 0, :], block[:, :, -1], block[:, :, 0])


def exchange(edge_sets):
    fwd_x, bwd_x = shift_pairs(lax.axis_size("gx"))
    fwd_y, bwd_y = shift_pairs(lax.axis_size(Y_AXES))
    last_rows = jnp.concatenate([e[0] for e in edge_sets], axis=1)
    first_rows = jnp.concatenate([e[1] for e in edge_sets], axis=1)
    last_cols = jnp.concatenate([e[2] for e in edge_sets], axis=1)
    first_cols = jnp.concatenate([e[3] for e in edge_sets], axis=1)
    above = lax.ppermute(last_rows, "gx", fwd_x)
    below = lax.ppermute(first_rows, "gx", bwd_x)
    left = lax.ppermute(last_cols, Y_AXES, fwd_y)
    right = lax.ppermute(first_cols, Y_AXES, bwd_y)
    out = []
    xo = 0
    yo = 0
    for e in edge_sets:
        out.append(((above, below, left, right), xo, yo))
        xo += e[0].shape[1]
        yo += e[2].shape[1]
    return out


def per_row(values, rows, cols):
    if values.ndim == 1:
        return jnp.broadcast_to(values[:, None], (rows, cols)).reshape(rows * cols)
    return jnp.broadcast_to(values[:, :, None], values.shape + (cols,)).reshape(
        values.shape[0], rows * cols
    )


def step_kernel(*refs, rows, cols, xo, yo, nest, split, gap, edges):
    refs = list(refs)
    if gap:
        expand_ref, fblock_ref = refs[:2]
        refs = refs[2:]
    if nest:
        (state_ref, above_ref, below_ref, left_ref, right_ref, forcing_ref, upw_ref, dnw_ref,
         nu_ref, relax_ref, vm_ref, new_ref) = refs[:12]
        refs = refs[12:]
    else:
        (state_ref, above_ref, below_ref, left_ref, right_ref, nu_ref, vm_ref, new_ref) = refs[:8]
        refs = refs[8:]
    if edges:
        lrow_ref, frow_ref, lcol_ref, fcol_ref = refs[:4]
        refs = refs[4:]
    if split:
        parts_ref = refs[0]
        refs = refs[1:]
    if gap:
        gap_ref = refs[0]
        refs = refs[1:]
    up_sc, dn_sc = refs
    n = rows * cols
    state = state_ref[...].astype(jnp.float32)
    levels = state.shape[0]
    up_sc[:, 0:cols] = above_ref[:, xo : xo + cols].astype(jnp.float32)
    up_sc[:, cols:n] = state[:, 0 : n - cols]
    dn_sc[:, 0 : n - cols] = state[:, cols:n]
    dn_sc[:, n - cols : n] = below_ref[:, xo : xo + cols].astype(jnp.float32)
    up = up_sc[...]
    down = dn_sc[...]
    lane = lax.broadcasted_iota(jnp.int32, (levels, n), 1)
    left = left_ref[...].astype(jnp.float32)
    right = right_ref[...].astype(jnp.float32)
    west = pltpu.roll(state, 1, 1)
    east = pltpu.roll(state, n - 1, 1)
    for r in range(rows):
        west = jnp.where(lane == r * cols, left[:, yo + r : yo + r + 1], west)
        east = jnp.where(lane == r * cols + cols - 1, right[:, yo + r : yo + r + 1], east)
    if nest:
        down = down * dnw_ref[...]
        up = up * upw_ref[...]
    stencil = down + up + east + west - 4.0 * state
    moved = state + nu_ref[...] * stencil
    if nest:
        moved = moved + relax_ref[...] * (forcing_ref[...] - moved)
    new = jnp.dot(vm_ref[...], moved, precision=lax.Precision.HIGH, preferred_element_type=jnp.float32)
    new_ref[...] = new
    if edges:
        lrow_ref[...] = new[:, n - cols : n].astype(jnp.bfloat16)
        frow_ref[...] = new[:, 0:cols].astype(jnp.bfloat16)
        narrow = new.astype(jnp.bfloat16)
        p = lax.broadcasted_iota(jnp.int32, (n, rows), 0)
        j = lax.broadcasted_iota(jnp.int32, (n, rows), 1)
        last_sel = (p == j * cols + (cols - 1)).astype(jnp.bfloat16)
        first_sel = (p == j * cols).astype(jnp.bfloat16)
        lcol_ref[...] = jnp.dot(narrow, last_sel, preferred_element_type=jnp.float32).astype(jnp.bfloat16)
        fcol_ref[...] = jnp.dot(narrow, first_sel, preferred_element_type=jnp.float32).astype(jnp.bfloat16)
    if split:
        hi = new.astype(jnp.bfloat16)
        rest = new - hi.astype(jnp.float32)
        mid = rest.astype(jnp.bfloat16)
        lo = (rest - mid.astype(jnp.float32)).astype(jnp.bfloat16)
        parts_ref[0:levels, :] = hi
        parts_ref[levels : 2 * levels, :] = mid
        parts_ref[2 * levels : 3 * levels, :] = lo
    if gap:
        expand = expand_ref[...]
        block_cols = expand.shape[0]
        pick = (((1,), (1,)), ((), ()))
        for a in range(rows // 3):
            rows3 = (
                new[:, (3 * a) * cols : (3 * a + 1) * cols]
                + new[:, (3 * a + 1) * cols : (3 * a + 2) * cols]
            ) + new[:, (3 * a + 2) * cols : (3 * a + 3) * cols]
            sums = lax.dot_general(rows3, expand, pick, precision=HI, preferred_element_type=jnp.float32)
            gap_ref[:, a * block_cols : (a + 1) * block_cols] = (
                sums / 9.0 - fblock_ref[:, a * block_cols : (a + 1) * block_cols]
            )


def stencil_step(state, placed_halo, nu, vert_mix, rows, cols, forcing=None, up_w=None, down_w=None,
                 relax=None, split=False, gap_of=None):
    levels = state.shape[0]
    n = rows * cols
    nest = forcing is not None
    (above, below, left, right), xo, yo = placed_halo
    if nest:
        args = (state, above, below, left, right, forcing, up_w[None, :], down_w[None, :],
                nu[:, None], relax[:, None], vert_mix)
    else:
        args = (state, above, below, left, right, nu[:, None], vert_mix)
    gap = gap_of is not None
    edges = not (split or gap)
    out_shape = (jax.ShapeDtypeStruct((levels, n), jnp.float32),)
    if edges:
        out_shape = out_shape + (
            jax.ShapeDtypeStruct((levels, cols), jnp.bfloat16),
            jax.ShapeDtypeStruct((levels, cols), jnp.bfloat16),
            jax.ShapeDtypeStruct((levels, rows), jnp.bfloat16),
            jax.ShapeDtypeStruct((levels, rows), jnp.bfloat16),
        )
    if split:
        out_shape = out_shape + (jax.ShapeDtypeStruct((3 * levels, n), jnp.bfloat16),)
    if gap:
        args = tuple(gap_of) + args
        out_shape = out_shape + (jax.ShapeDtypeStruct(gap_of[1].shape, jnp.float32),)
    flops = 2 * levels * levels * n * 6 + 4 * levels * n * rows + 20 * levels * n
    moved_bytes = sum(int(a.size) * a.dtype.itemsize for a in args) + levels * n * 4
    outs = pl.pallas_call(
        functools.partial(
            step_kernel, rows=rows, cols=cols, xo=xo, yo=yo, nest=nest, split=split, gap=gap,
            edges=edges,
        ),
        out_shape=out_shape,
        scratch_shapes=[pltpu.VMEM((levels, n), jnp.float32), pltpu.VMEM((levels, n), jnp.float32)],
        cost_estimate=pl.CostEstimate(flops=flops, bytes_accessed=moved_bytes, transcendentals=0),
    )(*args)
    if edges:
        return outs[0], tuple(outs[1:5]), outs[5:]
    return outs[0], None, outs[1:]


def nest_segments(nest_of, first, count):
    index_rows = first + jnp.arange(count, dtype=jnp.int32)
    inside = (index_rows >= 0) & (index_rows < nest_of.shape[0])
    return jnp.where(inside, nest_of[jnp.clip(index_rows, 0, nest_of.shape[0] - 1)], -1)


def row_weights(segments):
    left_w = (segments[:-2] == segments[1:-1]).astype(jnp.float32)
    right_w = (segments[2:] == segments[1:-1]).astype(jnp.float32)
    return (left_w, right_w)


def column_expansion(block_cols, cols, zero):
    b = lax.broadcasted_iota(jnp.int32, (block_cols, cols), 0) + zero
    c = lax.broadcasted_iota(jnp.int32, (block_cols, cols), 1)
    return (c // 3 == b).astype(jnp.float32)


def expand_blocks(block_flat, block_rows, block_cols, expand):
    pieces = []
    for a in range(block_rows):
        wide = jnp.dot(
            block_flat[:, a * block_cols : (a + 1) * block_cols],
            expand,
            precision=HI,
            preferred_element_type=jnp.float32,
        )
        pieces += [wide, wide, wide]
    return jnp.concatenate(pieces, axis=1)


def split3(values):
    hi = lax.reduce_precision(values, exponent_bits=8, mantissa_bits=7)
    rest = values - hi
    mid = lax.reduce_precision(rest, exponent_bits=8, mantissa_bits=7)
    lo = rest - mid
    return hi.astype(jnp.bfloat16), mid.astype(jnp.bfloat16), lo.astype(jnp.bfloat16)


def shifted_pairs(count, shift):
    return [(i, (i + shift) % count) for i in range(count)]


def gather_parts(parts, ids):
    levels = parts.shape[0] // 3
    width = parts.shape[1]
    onehot = (lax.broadcasted_iota(jnp.int32, (width, 1), 0) == ids[None, :]).astype(jnp.bfloat16)
    total = jnp.dot(parts, onehot, preferred_element_type=jnp.float32)
    return (total[:levels] + total[levels : 2 * levels]) + total[2 * levels :]


def scatter_add_columns(values, ids, width):
    levels = values.shape[0]
    onehot = (ids[:, None] == lax.broadcasted_iota(jnp.int32, (1, width), 1)).astype(jnp.bfloat16)
    if values.dtype == jnp.bfloat16:
        return jnp.dot(values, onehot, preferred_element_type=jnp.float32)
    parts = jnp.concatenate(split3(values), axis=0)
    total = jnp.dot(parts, onehot, preferred_element_type=jnp.float32)
    return (total[:levels] + total[levels : 2 * levels]) + total[2 * levels :]


def body_steps(parent, nest, nu_parent, nu_nest, relax, feedback, vert_mix, fp_owner, fp_cell, nest_of):
    levels, p_rows, p_cols = parent.shape
    _, n_rows, n_cols = nest.shape
    tiles_x = lax.axis_size("gx")
    here_x = lax.axis_index("gx")
    zero = jnp.minimum(here_x, 0)

    parent_halo, nest_halo = exchange([edges_3d(parent), edges_3d(nest)])
    flat_parent, _, (parent_parts,) = stencil_step(
        parent.reshape(levels, p_rows * p_cols), parent_halo, nu_parent, vert_mix, p_rows, p_cols,
        split=True,
    )

    owners = fp_owner.reshape(-1)
    cells = fp_cell.reshape(-1)
    requests = owners.shape[0]
    slots = 4 * requests // tiles_x
    by_shift = slots >= requests
    if by_shift:
        rel = (owners - here_x + tiles_x) % tiles_x
        chosen = rel[None, :] == jnp.arange(tiles_x, dtype=jnp.int32)[:, None]
        wanted = jnp.where(chosen, cells[None, :], 0)
        served = [wanted[0]] + [
            lax.ppermute(wanted[s], "gx", shifted_pairs(tiles_x, s)) for s in range(1, tiles_x)
        ]
        served_ids = jnp.concatenate(served, axis=0)
        back = [None] + [
            lax.ppermute(gather_parts(parent_parts, served[s]), "gx", shifted_pairs(tiles_x, -s))
            for s in range(1, tiles_x)
        ]
        back[0] = gather_parts(parent_parts, served[0])
        forcing_flat = back[0]
        for s in range(1, tiles_x):
            forcing_flat = jnp.where(chosen[s][None, :], back[s], forcing_flat)
    else:
        owner_ids = jnp.arange(tiles_x, dtype=jnp.int32)
        onehot = (owners[:, None] == owner_ids[None, :]).astype(jnp.int32)
        before = jnp.cumsum(onehot, axis=0) - onehot
        order_in = jnp.sum(before * onehot, axis=1)
        places = owners * slots + order_in
        wanted = jnp.zeros((tiles_x * slots,), jnp.int32).at[places].set(cells)
        served_ids = lax.all_to_all(wanted, "gx", split_axis=0, concat_axis=0, tiled=True)
        answers = lax.all_to_all(
            gather_parts(parent_parts, served_ids), "gx", split_axis=1, concat_axis=1, tiled=True
        )
        forcing_flat = jnp.take(answers, places, axis=1)

    block_rows = n_rows // 3
    block_cols = n_cols // 3
    expand = column_expansion(block_cols, n_cols, zero)
    forcing_full = expand_blocks(forcing_flat, block_rows, block_cols, expand)
    row_start = here_x * n_rows
    left_w, right_w = row_weights(nest_segments(nest_of, row_start - 1, n_rows + 2))
    up_w = per_row(left_w, n_rows, n_cols)
    down_w = per_row(right_w, n_rows, n_cols)

    nest_state = nest.reshape(levels, n_rows * n_cols)
    halo = nest_halo
    for turn_no in range(3):
        if turn_no > 0:
            (halo,) = exchange([edges])
        nest_state, edges, extra = stencil_step(
            nest_state, halo, nu_nest, vert_mix, n_rows, n_cols, forcing_full, up_w, down_w, relax,
            gap_of=(expand, forcing_flat) if turn_no == 2 else None,
        )
    (nudge_gap,) = extra
    if by_shift:
        outgoing = jnp.where(chosen[:, None, :], nudge_gap[None, :, :], 0.0).astype(jnp.bfloat16)
        incoming = jnp.concatenate(
            [outgoing[0]]
            + [lax.ppermute(outgoing[s], "gx", shifted_pairs(tiles_x, s)) for s in range(1, tiles_x)],
            axis=1,
        )
    else:
        outgoing = jnp.zeros((levels, tiles_x * slots), jnp.float32).at[:, places].set(nudge_gap)
        incoming = lax.all_to_all(outgoing, "gx", split_axis=1, concat_axis=1, tiled=True)
    summed = scatter_add_columns(incoming, served_ids, flat_parent.shape[1])
    parent_out = (flat_parent + feedback[:, None] * summed).astype(jnp.bfloat16)
    return (
        parent_out.reshape(levels, p_rows, p_cols),
        nest_state.astype(jnp.bfloat16).reshape(levels, n_rows, n_cols),
    )


def solution(mesh):
    placed = (
        P("groups", "gx", Y_AXES),
        P("groups", "gx", Y_AXES),
        P(),
        P(),
        P(),
        P(),
        P(),
        P("gx", Y_AXES, None, None),
        P("gx", Y_AXES, None),
        P(),
    )
    return jax.shard_map(
        body_steps,
        mesh=mesh,
        in_specs=placed,
        out_specs=(P("groups", "gx", Y_AXES), P("groups", "gx", Y_AXES)),
        check_vma=False,
    )
```

```python
import functools

import jax
import jax.numpy as jnp
from jax import lax
from jax.experimental import pallas as pl
from jax.experimental.pallas import tpu as pltpu
from jax.sharding import PartitionSpec as P


Y_AXES = ("gy", "gz")
HI = lax.Precision.HIGHEST


def shift_pairs(count):
    forward = [(i, i + 1) for i in range(count - 1)]
    backward = [(i + 1, i) for i in range(count - 1)]
    return forward, backward


def edges_3d(block):
    return (block[:, -1, :], block[:, 0, :], block[:, :, -1], block[:, :, 0])


def exchange(edge_sets):
    fwd_x, bwd_x = shift_pairs(lax.axis_size("gx"))
    fwd_y, bwd_y = shift_pairs(lax.axis_size(Y_AXES))
    last_rows = jnp.concatenate([e[0] for e in edge_sets], axis=1)
    first_rows = jnp.concatenate([e[1] for e in edge_sets], axis=1)
    last_cols = jnp.concatenate([e[2] for e in edge_sets], axis=1)
    first_cols = jnp.concatenate([e[3] for e in edge_sets], axis=1)
    above = lax.ppermute(last_rows, "gx", fwd_x)
    below = lax.ppermute(first_rows, "gx", bwd_x)
    left = lax.ppermute(last_cols, Y_AXES, fwd_y)
    right = lax.ppermute(first_cols, Y_AXES, bwd_y)
    out = []
    xo = 0
    yo = 0
    for e in edge_sets:
        out.append(((above, below, left, right), xo, yo))
        xo += e[0].shape[1]
        yo += e[2].shape[1]
    return out


def per_row(values, rows, cols):
    if values.ndim == 1:
        return jnp.broadcast_to(values[:, None], (rows, cols)).reshape(rows * cols)
    return jnp.broadcast_to(values[:, :, None], values.shape + (cols,)).reshape(
        values.shape[0], rows * cols
    )


def step_kernel(*refs, rows, cols, xo, yo, nest, split, gap, edges):
    refs = list(refs)
    if gap:
        expand_ref, fblock_ref = refs[:2]
        refs = refs[2:]
    if nest:
        (state_ref, above_ref, below_ref, left_ref, right_ref, forcing_ref, upw_ref, dnw_ref,
         nu_ref, relax_ref, vm_ref) = refs[:11]
        refs = refs[11:]
    else:
        (state_ref, above_ref, below_ref, left_ref, right_ref, nu_ref, vm_ref) = refs[:7]
        refs = refs[7:]
    if edges:
        last_sel_ref, first_sel_ref = refs[:2]
        refs = refs[2:]
    new_ref = refs[0]
    refs = refs[1:]
    if edges:
        lrow_ref, frow_ref, lcol_ref, fcol_ref = refs[:4]
        refs = refs[4:]
    if split:
        parts_ref = refs[0]
        refs = refs[1:]
    if gap:
        gap_ref = refs[0]
        refs = refs[1:]
    up_sc, dn_sc = refs
    n = rows * cols
    state = state_ref[...].astype(jnp.float32)
    levels = state.shape[0]
    up_sc[:, 0:cols] = above_ref[:, xo : xo + cols].astype(jnp.float32)
    up_sc[:, cols:n] = state[:, 0 : n - cols]
    dn_sc[:, 0 : n - cols] = state[:, cols:n]
    dn_sc[:, n - cols : n] = below_ref[:, xo : xo + cols].astype(jnp.float32)
    up = up_sc[...]
    down = dn_sc[...]
    lane = lax.broadcasted_iota(jnp.int32, (levels, n), 1)
    left = left_ref[...].astype(jnp.float32)
    right = right_ref[...].astype(jnp.float32)
    west = pltpu.roll(state, 1, 1)
    east = pltpu.roll(state, n - 1, 1)
    for r in range(rows):
        west = jnp.where(lane == r * cols, left[:, yo + r : yo + r + 1], west)
        east = jnp.where(lane == r * cols + cols - 1, right[:, yo + r : yo + r + 1], east)
    if nest:
        down = down * dnw_ref[...]
        up = up * upw_ref[...]
    stencil = down + up + east + west - 4.0 * state
    moved = state + nu_ref[...] * stencil
    if nest:
        moved = moved + relax_ref[...] * (forcing_ref[...] - moved)
    new = jnp.dot(vm_ref[...], moved, precision=lax.Precision.HIGH, preferred_element_type=jnp.float32)
    new_ref[...] = new
    if edges:
        lrow_ref[...] = new[:, n - cols : n].astype(jnp.bfloat16)
        frow_ref[...] = new[:, 0:cols].astype(jnp.bfloat16)
        narrow = new.astype(jnp.bfloat16)
        last_sel = last_sel_ref[...]
        first_sel = first_sel_ref[...]
        lcol_ref[...] = jnp.dot(narrow, last_sel, preferred_element_type=jnp.float32).astype(jnp.bfloat16)
        fcol_ref[...] = jnp.dot(narrow, first_sel, preferred_element_type=jnp.float32).astype(jnp.bfloat16)
    if split:
        hi = new.astype(jnp.bfloat16)
        rest = new - hi.astype(jnp.float32)
        mid = rest.astype(jnp.bfloat16)
        lo = (rest - mid.astype(jnp.float32)).astype(jnp.bfloat16)
        parts_ref[0:levels, :] = hi
        parts_ref[levels : 2 * levels, :] = mid
        parts_ref[2 * levels : 3 * levels, :] = lo
    if gap:
        expand = expand_ref[...]
        block_cols = expand.shape[0]
        pick = (((1,), (1,)), ((), ()))
        for a in range(rows // 3):
            rows3 = (
                new[:, (3 * a) * cols : (3 * a + 1) * cols]
                + new[:, (3 * a + 1) * cols : (3 * a + 2) * cols]
            ) + new[:, (3 * a + 2) * cols : (3 * a + 3) * cols]
            sums = lax.dot_general(rows3, expand, pick, precision=HI, preferred_element_type=jnp.float32)
            gap_ref[:, a * block_cols : (a + 1) * block_cols] = (
                sums / 9.0 - fblock_ref[:, a * block_cols : (a + 1) * block_cols]
            )


def stencil_step(state, placed_halo, nu, vert_mix, rows, cols, forcing=None, up_w=None, down_w=None,
                 relax=None, split=False, gap_of=None):
    levels = state.shape[0]
    n = rows * cols
    nest = forcing is not None
    (above, below, left, right), xo, yo = placed_halo
    if nest:
        args = (state, above, below, left, right, forcing, up_w[None, :], down_w[None, :],
                nu[:, None], relax[:, None], vert_mix)
    else:
        args = (state, above, below, left, right, nu[:, None], vert_mix)
    gap = gap_of is not None
    edges = not (split or gap)
    out_shape = (jax.ShapeDtypeStruct((levels, n), jnp.float32),)
    if edges:
        p = lax.broadcasted_iota(jnp.int32, (n, rows), 0)
        j = lax.broadcasted_iota(jnp.int32, (n, rows), 1) + jnp.minimum(lax.axis_index("gx"), 0)
        args = args + (
            (p == j * cols + (cols - 1)).astype(jnp.bfloat16),
            (p == j * cols).astype(jnp.bfloat16),
        )
        out_shape = out_shape + (
            jax.ShapeDtypeStruct((levels, cols), jnp.bfloat16),
            jax.ShapeDtypeStruct((levels, cols), jnp.bfloat16),
            jax.ShapeDtypeStruct((levels, rows), jnp.bfloat16),
            jax.ShapeDtypeStruct((levels, rows), jnp.bfloat16),
        )
    if split:
        out_shape = out_shape + (jax.ShapeDtypeStruct((3 * levels, n), jnp.bfloat16),)
    if gap:
        args = tuple(gap_of) + args
        out_shape = out_shape + (jax.ShapeDtypeStruct(gap_of[1].shape, jnp.float32),)
    flops = 2 * levels * levels * n * 6 + 4 * levels * n * rows + 20 * levels * n
    moved_bytes = sum(int(a.size) * a.dtype.itemsize for a in args) + levels * n * 4
    outs = pl.pallas_call(
        functools.partial(
            step_kernel, rows=rows, cols=cols, xo=xo, yo=yo, nest=nest, split=split, gap=gap,
            edges=edges,
        ),
        out_shape=out_shape,
        scratch_shapes=[pltpu.VMEM((levels, n), jnp.float32), pltpu.VMEM((levels, n), jnp.float32)],
        cost_estimate=pl.CostEstimate(flops=flops, bytes_accessed=moved_bytes, transcendentals=0),
    )(*args)
    if edges:
        return outs[0], tuple(outs[1:5]), outs[5:]
    return outs[0], None, outs[1:]


def nest_segments(nest_of, first, count):
    index_rows = first + jnp.arange(count, dtype=jnp.int32)
    inside = (index_rows >= 0) & (index_rows < nest_of.shape[0])
    return jnp.where(inside, nest_of[jnp.clip(index_rows, 0, nest_of.shape[0] - 1)], -1)


def row_weights(segments):
    left_w = (segments[:-2] == segments[1:-1]).astype(jnp.float32)
    right_w = (segments[2:] == segments[1:-1]).astype(jnp.float32)
    return (left_w, right_w)


def column_expansion(block_cols, cols, zero):
    b = lax.broadcasted_iota(jnp.int32, (block_cols, cols), 0) + zero
    c = lax.broadcasted_iota(jnp.int32, (block_cols, cols), 1)
    return (c // 3 == b).astype(jnp.float32)


def expand_blocks(block_flat, block_rows, block_cols, expand):
    pieces = []
    for a in range(block_rows):
        wide = jnp.dot(
            block_flat[:, a * block_cols : (a + 1) * block_cols],
            expand,
            precision=HI,
            preferred_element_type=jnp.float32,
        )
        pieces += [wide, wide, wide]
    return jnp.concatenate(pieces, axis=1)


def split3(values):
    hi = lax.reduce_precision(values, exponent_bits=8, mantissa_bits=7)
    rest = values - hi
    mid = lax.reduce_precision(rest, exponent_bits=8, mantissa_bits=7)
    lo = rest - mid
    return hi.astype(jnp.bfloat16), mid.astype(jnp.bfloat16), lo.astype(jnp.bfloat16)


def shifted_pairs(count, shift):
    return [(i, (i + shift) % count) for i in range(count)]


def gather_parts(parts, ids):
    levels = parts.shape[0] // 3
    width = parts.shape[1]
    onehot = (lax.broadcasted_iota(jnp.int32, (width, 1), 0) == ids[None, :]).astype(jnp.bfloat16)
    total = jnp.dot(parts, onehot, preferred_element_type=jnp.float32)
    return (total[:levels] + total[levels : 2 * levels]) + total[2 * levels :]


def scatter_add_columns(values, ids, width):
    levels = values.shape[0]
    onehot = (ids[:, None] == lax.broadcasted_iota(jnp.int32, (1, width), 1)).astype(jnp.bfloat16)
    if values.dtype == jnp.bfloat16:
        return jnp.dot(values, onehot, preferred_element_type=jnp.float32)
    parts = jnp.concatenate(split3(values), axis=0)
    total = jnp.dot(parts, onehot, preferred_element_type=jnp.float32)
    return (total[:levels] + total[levels : 2 * levels]) + total[2 * levels :]


def body_steps(parent, nest, nu_parent, nu_nest, relax, feedback, vert_mix, fp_owner, fp_cell, nest_of):
    levels, p_rows, p_cols = parent.shape
    _, n_rows, n_cols = nest.shape
    tiles_x = lax.axis_size("gx")
    here_x = lax.axis_index("gx")
    zero = jnp.minimum(here_x, 0)

    parent_halo, nest_halo = exchange([edges_3d(parent), edges_3d(nest)])
    flat_parent, _, (parent_parts,) = stencil_step(
        parent.reshape(levels, p_rows * p_cols), parent_halo, nu_parent, vert_mix, p_rows, p_cols,
        split=True,
    )

    owners = fp_owner.reshape(-1)
    cells = fp_cell.reshape(-1)
    requests = owners.shape[0]
    slots = 4 * requests // tiles_x
    by_shift = slots >= requests
    if by_shift:
        rel = (owners - here_x + tiles_x) % tiles_x
        chosen = rel[None, :] == jnp.arange(tiles_x, dtype=jnp.int32)[:, None]
        wanted = jnp.where(chosen, cells[None, :], 0)
        served = [wanted[0]] + [
            lax.ppermute(wanted[s], "gx", shifted_pairs(tiles_x, s)) for s in range(1, tiles_x)
        ]
        served_ids = jnp.concatenate(served, axis=0)
        back = [None] + [
            lax.ppermute(gather_parts(parent_parts, served[s]), "gx", shifted_pairs(tiles_x, -s))
            for s in range(1, tiles_x)
        ]
        back[0] = gather_parts(parent_parts, served[0])
        forcing_flat = back[0]
        for s in range(1, tiles_x):
            forcing_flat = jnp.where(chosen[s][None, :], back[s], forcing_flat)
    else:
        owner_ids = jnp.arange(tiles_x, dtype=jnp.int32)
        onehot = (owners[:, None] == owner_ids[None, :]).astype(jnp.int32)
        before = jnp.cumsum(onehot, axis=0) - onehot
        order_in = jnp.sum(before * onehot, axis=1)
        places = owners * slots + order_in
        wanted = jnp.zeros((tiles_x * slots,), jnp.int32).at[places].set(cells)
        served_ids = lax.all_to_all(wanted, "gx", split_axis=0, concat_axis=0, tiled=True)
        answers = lax.all_to_all(
            gather_parts(parent_parts, served_ids), "gx", split_axis=1, concat_axis=1, tiled=True
        )
        forcing_flat = jnp.take(answers, places, axis=1)

    block_rows = n_rows // 3
    block_cols = n_cols // 3
    expand = column_expansion(block_cols, n_cols, zero)
    forcing_full = expand_blocks(forcing_flat, block_rows, block_cols, expand)
    row_start = here_x * n_rows
    left_w, right_w = row_weights(nest_segments(nest_of, row_start - 1, n_rows + 2))
    up_w = per_row(left_w, n_rows, n_cols)
    down_w = per_row(right_w, n_rows, n_cols)

    nest_state = nest.reshape(levels, n_rows * n_cols)
    halo = nest_halo
    for turn_no in range(3):
        if turn_no > 0:
            (halo,) = exchange([edges])
        nest_state, edges, extra = stencil_step(
            nest_state, halo, nu_nest, vert_mix, n_rows, n_cols, forcing_full, up_w, down_w, relax,
            gap_of=(expand, forcing_flat) if turn_no == 2 else None,
        )
    (nudge_gap,) = extra
    if by_shift:
        outgoing = jnp.where(chosen[:, None, :], nudge_gap[None, :, :], 0.0).astype(jnp.bfloat16)
        incoming = jnp.concatenate(
            [outgoing[0]]
            + [lax.ppermute(outgoing[s], "gx", shifted_pairs(tiles_x, s)) for s in range(1, tiles_x)],
            axis=1,
        )
    else:
        outgoing = jnp.zeros((levels, tiles_x * slots), jnp.float32).at[:, places].set(nudge_gap)
        incoming = lax.all_to_all(outgoing, "gx", split_axis=1, concat_axis=1, tiled=True)
    summed = scatter_add_columns(incoming, served_ids, flat_parent.shape[1])
    parent_out = (flat_parent + feedback[:, None] * summed).astype(jnp.bfloat16)
    return (
        parent_out.reshape(levels, p_rows, p_cols),
        nest_state.astype(jnp.bfloat16).reshape(levels, n_rows, n_cols),
    )


def solution(mesh):
    placed = (
        P("groups", "gx", Y_AXES),
        P("groups", "gx", Y_AXES),
        P(),
        P(),
        P(),
        P(),
        P(),
        P("gx", Y_AXES, None, None),
        P("gx", Y_AXES, None),
        P(),
    )
    return jax.shard_map(
        body_steps,
        mesh=mesh,
        in_specs=placed,
        out_specs=(P("groups", "gx", Y_AXES), P("groups", "gx", Y_AXES)),
        check_vma=False,
    )
```
